32 devices in a mesh: leaf: 16 (over z, y, x), rows: 2 (over core).
Axes of the slice: x: 2, y: 2, z: 4, core: 2. Of those that a mesh axis runs over, the one named last changes fastest.
Arguments:
- leaf_factor: float32 [16384, 1024], P(('leaf', 'rows')), may hold values from -2 to 2, as said below
- leaf_rhs: float32 [16384, 256], P(('leaf', 'rows')), may hold values from -6 to 6
- update_panel: float32 [16384, 1024], P('leaf', 'rows'), may hold values from -0.1875 to 0.1875
- update_blocks: int32 [16, 8], P('leaf'), may hold values from 0 to 7, each once within a row
- parent_factor: float32 [16384, 1024], P(('leaf', 'rows')), may hold values from -2 to 2, as said below
- parent_rhs: float32 [16384, 128], P(('leaf', 'rows')), may hold values from -6 to 6
Outputs:
- leaf_solution: float32 [16384, 256], P(('leaf', 'rows'))
- parent_solution: float32 [16384, 128], P(('leaf', 'rows'))
The draws below stay inside these ranges and needn't reach their ends.
Inputs may be any that keep to these rules, and one draw needn't show every extreme that they name: `parent_factor`: tiles on the block diagonal are near the identity. Groups 2 q and 2 q + 1 hold equal copies of one parent factor: rows 2 q * 1024 onward equal rows (2 q + 1) * 1024 onward. `leaf_factor`: tiles on the block diagonal are near the identity.
All inputs are finite; a program needn't handle non-finite values.
Results may differ from the reference program's by a relative error of at most 0.0003.
Values sent between devices are 32-bit elements; how exact they have to be, the bound alone decides.
No kernel may reach another device: no remote copies, remote signals or barrier semaphores. Data moves between devices by JAX's collectives and lax.ppermute only.
A program may use at most 64 MiB of HBM per device.

```python
import math
import jax
import jax.numpy as jnp
from jax import lax

S = 1024
P_SIZE = 1024
NRHS = 256
ROW_BLOCK = 128
GROUPS = 16
HALF = 128
LEAF_TILE = 512
PARENT_TILE = 512


def block_factor(key, count, order, tile_rows):
    noise = jax.random.truncated_normal(key, -4.0, 4.0, (count * order, order), jnp.float32)
    row_ids = jnp.arange(count * order) % order
    col_ids = jnp.arange(order)
    same_tile = row_ids[:, None] // tile_rows == col_ids[None, :] // tile_rows
    identity = (row_ids[:, None] == col_ids[None, :]).astype(jnp.float32)
    inside = identity + noise * (0.3 / math.sqrt(tile_rows))
    outside = noise * (1.5 / math.sqrt(order))
    return jnp.where(same_tile, inside, outside)


def draw_leaf_factor(key, part):
    return block_factor(jax.random.fold_in(key, 11), GROUPS, S, LEAF_TILE)


def draw_parent_factor(key, part):
    pairs = block_factor(jax.random.fold_in(key, 12), GROUPS // 2, P_SIZE, PARENT_TILE)
    pairs = pairs.reshape(GROUPS // 2, 1, P_SIZE, P_SIZE)
    return jnp.broadcast_to(pairs, (GROUPS // 2, 2, P_SIZE, P_SIZE)).reshape(GROUPS * P_SIZE, P_SIZE)


def block_scale(own_key, dims, shards, least, high):
    factor_of, own = 1.0, jax.random.fold_in(own_key, 6)
    for dim, shards_of in shards:
        draws = jnp.exp(jax.random.uniform(jax.random.fold_in(own, dim), (shards_of,), jnp.float32, least / len(shards), high / len(shards)))
        factor_of = factor_of * jnp.repeat(draws, dims[dim] // shards_of).reshape([-1 if axis == dim else 1 for axis in range(len(dims))])
    return factor_of


def gaussian(key, extent, width, bound, split=(), kind=jnp.bfloat16):
    factor_of = block_scale(key, extent, split, -0.22, 0.18) if split else 1.0
    result = jax.random.normal(key, extent, jnp.float32) * width * factor_of
    return jnp.minimum(jnp.maximum(result, -bound), bound).astype(kind)


def setup_inputs(seed: int = 0) -> dict:
    keys = jax.random.split(jax.random.key(seed), 7)
    return {
        "leaf_factor": draw_leaf_factor(jax.random.fold_in(keys[6], 71), 0),
        "leaf_rhs": gaussian(keys[1], (GROUPS * S, NRHS), 1.0, 6.0, ((0, 32),), jnp.float32),
        "update_panel": gaussian(keys[2], (GROUPS * P_SIZE, S), S ** -0.5, 0.1875, ((0, 16), (1, 2)), jnp.float32),
        "update_blocks": jax.vmap(lambda own: jax.random.permutation(own, P_SIZE // ROW_BLOCK))(jax.random.split(keys[3], GROUPS)).reshape((GROUPS, P_SIZE // ROW_BLOCK)).astype(jnp.int32),
        "parent_factor": draw_parent_factor(jax.random.fold_in(keys[6], 71), 0),
        "parent_rhs": gaussian(keys[5], (GROUPS * P_SIZE, HALF), 1.0, 6.0, ((0, 32),), jnp.float32),
    }


def matmul(left, right):
    return jnp.dot(left, right, precision=lax.Precision.HIGHEST, preferred_element_type=jnp.float32)


def solve_blocks(factor, right_side, tile_rows):
    order = factor.shape[0]
    solution = jnp.zeros_like(right_side)
    for tile_index in range(order // tile_rows):
        first = tile_index * tile_rows
        factor_rows = factor[first:first + tile_rows]
        target = right_side[first:first + tile_rows]
        if first > 0:
            target = target - matmul(factor_rows[:, :first], solution[:first])
        solved = matmul(factor_rows[:, first:first + tile_rows], target)
        solution = solution.at[first:first + tile_rows].set(solved)
    return solution


def leaf_group(inputs):
    factor, right_side, panel, blocks = inputs
    solution = solve_blocks(factor, right_side, LEAF_TILE)
    product = matmul(panel, solution)
    pieces = product.reshape(P_SIZE // ROW_BLOCK, ROW_BLOCK, NRHS)
    placed = jnp.zeros_like(pieces).at[blocks].set(pieces)
    return solution, placed.reshape(P_SIZE, NRHS)


def parent_group(inputs):
    factor, right_side = inputs
    return solve_blocks(factor, right_side, PARENT_TILE)


def reference(leaf_factor, leaf_rhs, update_panel, update_blocks, parent_factor, parent_rhs):
    solutions, placed = lax.map(leaf_group, (leaf_factor.reshape(GROUPS, S, S), leaf_rhs.reshape(GROUPS, S, NRHS), update_panel.reshape(GROUPS, P_SIZE, S), update_blocks))
    pair_sum = placed.reshape(GROUPS // 2, 2, P_SIZE, NRHS).sum(axis=1)
    halves = pair_sum.reshape(GROUPS // 2, P_SIZE, 2, HALF).transpose(0, 2, 1, 3).reshape(GROUPS, P_SIZE, HALF)
    pending = parent_rhs.reshape(GROUPS, P_SIZE, HALF) - halves
    parent_solution = lax.map(parent_group, (parent_factor.reshape(GROUPS, P_SIZE, P_SIZE), pending))
    return solutions.reshape(GROUPS * S, NRHS), parent_solution.reshape(GROUPS * P_SIZE, HALF)
```

```python
import jax
import jax.numpy as jnp
from jax import lax
from jax.sharding import PartitionSpec as P

ROW_BLOCK = 128


def passed_along(array, axis, by):
    size = lax.axis_size(axis)
    pairs = [(i, i + by) for i in range(size) if 0 <= i + by < size]
    return lax.ppermute(array, axis, pairs)


def swapped(block, axis, apart):
    count = lax.axis_size(axis)
    route = []
    for low in range(count):
        high = low | 1 << apart
        if high != low and high < count:
            route += [(low, high), (high, low)]
    return lax.ppermute(block, axis, route)


def matmul(left, right, precision=lax.Precision.HIGHEST):
    return jnp.dot(left, right, precision=precision, preferred_element_type=jnp.float32)


def leaf_pass(outgoing):
    return passed_along(outgoing, "rows", 1)


def parent_pass(outgoing):
    return passed_along(outgoing, "rows", 1)


def front_forward(factor, right_side, section, sections, pass_tile):
    tile_rows = right_side.shape[0]

    def advance(tick, state):
        pending, solution, incoming = state
        source = tick - section
        useful = jnp.logical_and(source >= 0, source < section)
        safe_source = jnp.clip(source, 0, sections - 1)

        def apply_tile(values):
            factor_tile = lax.dynamic_slice_in_dim(factor, safe_source * tile_rows, tile_rows, 1)
            return values - matmul(factor_tile, incoming)

        pending = lax.cond(useful, apply_tile, lambda values: values, pending)
        own_turn = tick == 2 * section

        def solve_own(values):
            diagonal_tile = lax.dynamic_slice_in_dim(factor, section * tile_rows, tile_rows, 1)
            return matmul(diagonal_tile, values)

        solution = lax.cond(own_turn, solve_own, lambda values: solution, pending)
        outgoing = jnp.where(
            own_turn, solution, jnp.where(useful, incoming, jnp.zeros_like(incoming))
        )
        incoming = pass_tile(outgoing)
        return (pending, solution, incoming)

    initial = (right_side, jnp.zeros_like(right_side), jnp.zeros_like(right_side))
    return lax.fori_loop(0, 2 * sections - 1, advance, initial)[1]


def split_halves(values, sibling, column_half):
    lower_half = values[:, :column_half]
    upper_half = values[:, column_half:]
    kept_half = jnp.where(sibling == 0, lower_half, upper_half)
    sent_half = jnp.where(sibling == 0, upper_half, lower_half)
    return (kept_half, sent_half)


def pair_swap(block, axis):
    return lax.ppermute(block, axis, [(0, 1), (1, 0)])


def two_section_solve(factor, right_side, section, precision):
    tile_rows = right_side.shape[0]
    diagonal = lax.dynamic_slice_in_dim(factor, section * tile_rows, tile_rows, 1)
    below = factor[:, :tile_rows]
    first = matmul(diagonal, right_side, precision)
    arrived = lax.ppermute(first, "rows", [(0, 1)])
    coupling = matmul(diagonal, below, precision)
    return first - matmul(coupling, arrived, precision)


def two_section_shards(leaf_factor, leaf_rhs, update_panel, update_blocks, parent_factor, parent_rhs):
    section = lax.axis_index("rows")
    precision = lax.Precision.HIGHEST
    leaf_solution = two_section_solve(leaf_factor, leaf_rhs, section, precision)
    order = jnp.argsort(update_blocks[0])
    blocks = update_panel.reshape(-1, ROW_BLOCK, update_panel.shape[1])
    panel_placed = jnp.take(blocks, order, axis=0).reshape(update_panel.shape)
    placed = matmul(panel_placed, leaf_solution, precision)
    rows_half = placed.shape[0] // 2
    own_rows = lax.dynamic_slice_in_dim(placed, section * rows_half, rows_half, 0)
    other_rows = lax.dynamic_slice_in_dim(placed, (1 - section) * rows_half, rows_half, 0)
    chip_sum = own_rows + pair_swap(other_rows, "rows")
    column_half = parent_rhs.shape[1]
    sibling = lax.axis_index("leaf") % 2
    kept = lax.dynamic_slice_in_dim(chip_sum, sibling * column_half, column_half, 1)
    sent = lax.dynamic_slice_in_dim(chip_sum, (1 - sibling) * column_half, column_half, 1)
    pending = parent_rhs - (kept + swapped(sent, "leaf", 0))
    parent_solution = two_section_solve(parent_factor, pending, section, precision)
    return (leaf_solution, parent_solution)


def shards(leaf_factor, leaf_rhs, update_panel, update_blocks, parent_factor, parent_rhs):
    sections = lax.axis_size("rows")
    if sections == 2:
        return two_section_shards(leaf_factor, leaf_rhs, update_panel, update_blocks, parent_factor, parent_rhs)
    section = lax.axis_index("rows")
    leaf_solution = front_forward(leaf_factor, leaf_rhs, section, sections, leaf_pass)
    panel_product = matmul(update_panel, leaf_solution)
    columns = panel_product.shape[1]
    pieces = panel_product.reshape(-1, ROW_BLOCK, columns)
    placed = jnp.zeros_like(pieces).at[update_blocks[0]].set(pieces).reshape(panel_product.shape)
    column_half = parent_rhs.shape[1]
    sibling = lax.axis_index("leaf") % 2
    kept_half, sent_half = split_halves(placed, sibling, column_half)
    arrived = swapped(sent_half, "leaf", 0)
    update_sum = lax.psum_scatter(kept_half + arrived, "rows", scatter_dimension=0, tiled=True)
    pending = parent_rhs - update_sum
    parent_solution = front_forward(parent_factor, pending, section, sections, parent_pass)
    return (leaf_solution, parent_solution)


def solution(mesh):
    placed = (
        P(("leaf", "rows"), None),
        P(("leaf", "rows"), None),
        P("leaf", "rows"),
        P("leaf", None),
        P(("leaf", "rows"), None),
        P(("leaf", "rows"), None),
    )
    return jax.shard_map(
        shards,
        mesh=mesh,
        in_specs=placed,
        out_specs=(P(("leaf", "rows"), None), P(("leaf", "rows"), None)),
        check_vma=False,
    )
```

```python
import jax
import jax.numpy as jnp
from jax import lax
from jax.sharding import PartitionSpec as P

ROW_BLOCK = 128


def passed_along(array, axis, by):
    size = lax.axis_size(axis)
    pairs = [(i, i + by) for i in range(size) if 0 <= i + by < size]
    return lax.ppermute(array, axis, pairs)


def swapped(block, axis, apart):
    count = lax.axis_size(axis)
    route = []
    for low in range(count):
        high = low | 1 << apart
        if high != low and high < count:
            route += [(low, high), (high, low)]
    return lax.ppermute(block, axis, route)


def matmul(left, right, precision=lax.Precision.HIGHEST):
    return jnp.dot(left, right, precision=precision, preferred_element_type=jnp.float32)


def leaf_pass(outgoing):
    return passed_along(outgoing, "rows", 1)


def parent_pass(outgoing):
    return passed_along(outgoing, "rows", 1)


def front_forward(factor, right_side, section, sections, pass_tile):
    tile_rows = right_side.shape[0]

    def advance(tick, state):
        pending, solution, incoming = state
        source = tick - section
        useful = jnp.logical_and(source >= 0, source < section)
        safe_source = jnp.clip(source, 0, sections - 1)

        def apply_tile(values):
            factor_tile = lax.dynamic_slice_in_dim(factor, safe_source * tile_rows, tile_rows, 1)
            return values - matmul(factor_tile, incoming)

        pending = lax.cond(useful, apply_tile, lambda values: values, pending)
        own_turn = tick == 2 * section

        def solve_own(values):
            diagonal_tile = lax.dynamic_slice_in_dim(factor, section * tile_rows, tile_rows, 1)
            return matmul(diagonal_tile, values)

        solution = lax.cond(own_turn, solve_own, lambda values: solution, pending)
        outgoing = jnp.where(
            own_turn, solution, jnp.where(useful, incoming, jnp.zeros_like(incoming))
        )
        incoming = pass_tile(outgoing)
        return (pending, solution, incoming)

    initial = (right_side, jnp.zeros_like(right_side), jnp.zeros_like(right_side))
    return lax.fori_loop(0, 2 * sections - 1, advance, initial)[1]


def split_halves(values, sibling, column_half):
    lower_half = values[:, :column_half]
    upper_half = values[:, column_half:]
    kept_half = jnp.where(sibling == 0, lower_half, upper_half)
    sent_half = jnp.where(sibling == 0, upper_half, lower_half)
    return (kept_half, sent_half)


def pair_swap(block, axis):
    return lax.ppermute(block, axis, [(0, 1), (1, 0)])


def two_section_solve(factor, right_side, section, precision):
    tile_rows = right_side.shape[0]
    diagonal = lax.dynamic_slice_in_dim(factor, section * tile_rows, tile_rows, 1)
    below = factor[:, :tile_rows]
    first = matmul(diagonal, right_side, precision)
    arrived = lax.ppermute(first, "rows", [(0, 1)])
    coupling = matmul(diagonal, below, precision)
    return first - matmul(coupling, arrived, precision)


def inverse_order(update_blocks):
    targets = update_blocks[0]
    count = targets.shape[0]
    hits = targets[:, None] == jnp.arange(count)[None, :]
    return jnp.sum(jnp.where(hits, jnp.arange(count)[:, None], 0), axis=0)


def placed_rows(product, order, section):
    pieces = product.reshape(-1, ROW_BLOCK, product.shape[1])
    per_section = pieces.shape[0] // 2
    chosen = lax.dynamic_slice_in_dim(order, section * per_section, per_section)
    taken = jnp.take(pieces, chosen, axis=0, mode="clip")
    return taken.reshape(-1, product.shape[1])


def two_section_shards(leaf_factor, leaf_rhs, update_panel, update_blocks, parent_factor, parent_rhs):
    section = lax.axis_index("rows")
    precision = lax.Precision.HIGH
    leaf_solution = two_section_solve(leaf_factor, leaf_rhs, section, precision)
    order = inverse_order(update_blocks)
    product = matmul(update_panel, leaf_solution, precision)
    other_rows = placed_rows(product, order, 1 - section)
    arrived_rows = pair_swap(other_rows, "rows")
    chip_sum = placed_rows(product, order, section) + arrived_rows
    column_half = parent_rhs.shape[1]
    sibling = lax.axis_index("leaf") % 2
    kept = lax.dynamic_slice_in_dim(chip_sum, sibling * column_half, column_half, 1)
    sent = lax.dynamic_slice_in_dim(chip_sum, (1 - sibling) * column_half, column_half, 1)
    tile_rows = parent_rhs.shape[0]
    diagonal = lax.dynamic_slice_in_dim(parent_factor, section * tile_rows, tile_rows, 1)
    coupling = matmul(diagonal, parent_factor[:, :tile_rows], precision)
    arrived = swapped(sent, "leaf", 0)
    arrived, coupling = lax.optimization_barrier((arrived, coupling))
    pending = parent_rhs - (kept + arrived)
    first = matmul(diagonal, pending, precision)
    arrived = lax.ppermute(first, "rows", [(0, 1)])
    parent_solution = first - matmul(coupling, arrived, precision)
    return (leaf_solution, parent_solution)


def shards(leaf_factor, leaf_rhs, update_panel, update_blocks, parent_factor, parent_rhs):
    sections = lax.axis_size("rows")
    if sections == 2:
        return two_section_shards(leaf_factor, leaf_rhs, update_panel, update_blocks, parent_factor, parent_rhs)
    section = lax.axis_index("rows")
    leaf_solution = front_forward(leaf_factor, leaf_rhs, section, sections, leaf_pass)
    panel_product = matmul(update_panel, leaf_solution)
    columns = panel_product.shape[1]
    pieces = panel_product.reshape(-1, ROW_BLOCK, columns)
    placed = jnp.zeros_like(pieces).at[update_blocks[0]].set(pieces).reshape(panel_product.shape)
    column_half = parent_rhs.shape[1]
    sibling = lax.axis_index("leaf") % 2
    kept_half, sent_half = split_halves(placed, sibling, column_half)
    arrived = swapped(sent_half, "leaf", 0)
    update_sum = lax.psum_scatter(kept_half + arrived, "rows", scatter_dimension=0, tiled=True)
    pending = parent_rhs - update_sum
    parent_solution = front_forward(parent_factor, pending, section, sections, parent_pass)
    return (leaf_solution, parent_solution)


def solution(mesh):
    placed = (
        P(("leaf", "rows"), None),
        P(("leaf", "rows"), None),
        P("leaf", "rows"),
        P("leaf", None),
        P(("leaf", "rows"), None),
        P(("leaf", "rows"), None),
    )
    return jax.shard_map(
        shards,
        mesh=mesh,
        in_specs=placed,
        out_specs=(P(("leaf", "rows"), None), P(("leaf", "rows"), None)),
        check_vma=False,
    )
```

```python
import jax
import jax.numpy as jnp
from jax import lax
from jax.sharding import PartitionSpec as P

ROW_BLOCK = 128


def passed_along(array, axis, by):
    size = lax.axis_size(axis)
    pairs = [(i, i + by) for i in range(size) if 0 <= i + by < size]
    return lax.ppermute(array, axis, pairs)


def swapped(block, axis, apart):
    count = lax.axis_size(axis)
    route = []
    for low in range(count):
        high = low | 1 << apart
        if high != low and high < count:
            route += [(low, high), (high, low)]
    return lax.ppermute(block, axis, route)


def matmul(left, right, precision=lax.Precision.HIGHEST):
    return jnp.dot(left, right, precision=precision, preferred_element_type=jnp.float32)


def leaf_pass(outgoing):
    return passed_along(outgoing, "rows", 1)


def parent_pass(outgoing):
    return passed_along(outgoing, "rows", 1)


def front_forward(factor, right_side, section, sections, pass_tile):
    tile_rows = right_side.shape[0]

    def advance(tick, state):
        pending, solution, incoming = state
        source = tick - section
        useful = jnp.logical_and(source >= 0, source < section)
        safe_source = jnp.clip(source, 0, sections - 1)

        def apply_tile(values):
            factor_tile = lax.dynamic_slice_in_dim(factor, safe_source * tile_rows, tile_rows, 1)
            return values - matmul(factor_tile, incoming)

        pending = lax.cond(useful, apply_tile, lambda values: values, pending)
        own_turn = tick == 2 * section

        def solve_own(values):
            diagonal_tile = lax.dynamic_slice_in_dim(factor, section * tile_rows, tile_rows, 1)
            return matmul(diagonal_tile, values)

        solution = lax.cond(own_turn, solve_own, lambda values: solution, pending)
        outgoing = jnp.where(
            own_turn, solution, jnp.where(useful, incoming, jnp.zeros_like(incoming))
        )
        incoming = pass_tile(outgoing)
        return (pending, solution, incoming)

    initial = (right_side, jnp.zeros_like(right_side), jnp.zeros_like(right_side))
    return lax.fori_loop(0, 2 * sections - 1, advance, initial)[1]


def split_halves(values, sibling, column_half):
    lower_half = values[:, :column_half]
    upper_half = values[:, column_half:]
    kept_half = jnp.where(sibling == 0, lower_half, upper_half)
    sent_half = jnp.where(sibling == 0, upper_half, lower_half)
    return (kept_half, sent_half)


def pair_swap(block, axis):
    return lax.ppermute(block, axis, [(0, 1), (1, 0)])


def two_section_leaf(factor, right_side, section, precision):
    tile_rows = right_side.shape[0]
    diagonal = lax.dynamic_slice_in_dim(factor, section * tile_rows, tile_rows, 1)
    first = matmul(diagonal, right_side, precision)
    arrived = lax.ppermute(first, "rows", [(0, 1)])
    target = right_side - matmul(factor[:, :tile_rows], arrived, precision)
    return matmul(diagonal, target, precision)


def inverse_order(update_blocks):
    targets = update_blocks[0]
    count = targets.shape[0]
    hits = targets[:, None] == jnp.arange(count)[None, :]
    return jnp.sum(jnp.where(hits, jnp.arange(count)[:, None], 0), axis=0)


def placed_rows(product, order, section):
    per_section = product.shape[0] // ROW_BLOCK // 2
    pieces = []
    for k in range(per_section):
        block = lax.dynamic_index_in_dim(order, section * per_section + k, keepdims=False)
        pieces.append(lax.dynamic_slice_in_dim(product, block * ROW_BLOCK, ROW_BLOCK, 0))
    return jnp.concatenate(pieces, 0)


def two_section_shards(leaf_factor, leaf_rhs, update_panel, update_blocks, parent_factor, parent_rhs):
    section = lax.axis_index("rows")
    precision = lax.Precision.HIGH
    leaf_solution = two_section_leaf(leaf_factor, leaf_rhs, section, precision)
    order = inverse_order(update_blocks)
    product = matmul(update_panel, leaf_solution, precision)
    other_rows = placed_rows(product, order, 1 - section)
    arrived_rows = pair_swap(other_rows, "rows")
    chip_sum = placed_rows(product, order, section) + arrived_rows
    column_half = parent_rhs.shape[1]
    sibling = lax.axis_index("leaf") % 2
    kept = lax.dynamic_slice_in_dim(chip_sum, sibling * column_half, column_half, 1)
    sent = lax.dynamic_slice_in_dim(chip_sum, (1 - sibling) * column_half, column_half, 1)
    tile_rows = parent_rhs.shape[0]
    diagonal = lax.dynamic_slice_in_dim(parent_factor, section * tile_rows, tile_rows, 1)
    coupling = matmul(diagonal, parent_factor[:, :tile_rows], precision)
    arrived = swapped(sent, "leaf", 0)
    arrived, coupling = lax.optimization_barrier((arrived, coupling))
    pending = parent_rhs - (kept + arrived)
    first = matmul(diagonal, pending, precision)
    arrived = lax.ppermute(first, "rows", [(0, 1)])
    parent_solution = first - matmul(coupling, arrived, precision)
    return (leaf_solution, parent_solution)


def shards(leaf_factor, leaf_rhs, update_panel, update_blocks, parent_factor, parent_rhs):
    sections = lax.axis_size("rows")
    if sections == 2:
        return two_section_shards(leaf_factor, leaf_rhs, update_panel, update_blocks, parent_factor, parent_rhs)
    section = lax.axis_index("rows")
    leaf_solution = front_forward(leaf_factor, leaf_rhs, section, sections, leaf_pass)
    panel_product = matmul(update_panel, leaf_solution)
    columns = panel_product.shape[1]
    pieces = panel_product.reshape(-1, ROW_BLOCK, columns)
    placed = jnp.zeros_like(pieces).at[update_blocks[0]].set(pieces).reshape(panel_product.shape)
    column_half = parent_rhs.shape[1]
    sibling = lax.axis_index("leaf") % 2
    kept_half, sent_half = split_halves(placed, sibling, column_half)
    arrived = swapped(sent_half, "leaf", 0)
    update_sum = lax.psum_scatter(kept_half + arrived, "rows", scatter_dimension=0, tiled=True)
    pending = parent_rhs - update_sum
    parent_solution = front_forward(parent_factor, pending, section, sections, parent_pass)
    return (leaf_solution, parent_solution)


def solution(mesh):
    placed = (
        P(("leaf", "rows"), None),
        P(("leaf", "rows"), None),
        P("leaf", "rows"),
        P("leaf", None),
        P(("leaf", "rows"), None),
        P(("leaf", "rows"), None),
    )
    return jax.shard_map(
        shards,
        mesh=mesh,
        in_specs=placed,
        out_specs=(P(("leaf", "rows"), None), P(("leaf", "rows"), None)),
        check_vma=False,
    )
```

```python
import jax
import jax.numpy as jnp
from jax import lax
from jax.sharding import PartitionSpec as P

ROW_BLOCK = 128


def passed_along(array, axis, by):
    size = lax.axis_size(axis)
    pairs = [(i, i + by) for i in range(size) if 0 <= i + by < size]
    return lax.ppermute(array, axis, pairs)


def swapped(block, axis, apart):
    count = lax.axis_size(axis)
    route = []
    for low in range(count):
        high = low | 1 << apart
        if high != low and high < count:
            route += [(low, high), (high, low)]
    return lax.ppermute(block, axis, route)


def matmul(left, right, precision=lax.Precision.HIGHEST):
    return jnp.dot(left, right, precision=precision, preferred_element_type=jnp.float32)


def leaf_pass(outgoing):
    return passed_along(outgoing, "rows", 1)


def parent_pass(outgoing):
    return passed_along(outgoing, "rows", 1)


def front_forward(factor, right_side, section, sections, pass_tile):
    tile_rows = right_side.shape[0]

    def advance(tick, state):
        pending, solution, incoming = state
        source = tick - section
        useful = jnp.logical_and(source >= 0, source < section)
        safe_source = jnp.clip(source, 0, sections - 1)

        def apply_tile(values):
            factor_tile = lax.dynamic_slice_in_dim(factor, safe_source * tile_rows, tile_rows, 1)
            return values - matmul(factor_tile, incoming)

        pending = lax.cond(useful, apply_tile, lambda values: values, pending)
        own_turn = tick == 2 * section

        def solve_own(values):
            diagonal_tile = lax.dynamic_slice_in_dim(factor, section * tile_rows, tile_rows, 1)
            return matmul(diagonal_tile, values)

        solution = lax.cond(own_turn, solve_own, lambda values: solution, pending)
        outgoing = jnp.where(
            own_turn, solution, jnp.where(useful, incoming, jnp.zeros_like(incoming))
        )
        incoming = pass_tile(outgoing)
        return (pending, solution, incoming)

    initial = (right_side, jnp.zeros_like(right_side), jnp.zeros_like(right_side))
    return lax.fori_loop(0, 2 * sections - 1, advance, initial)[1]


def split_halves(values, sibling, column_half):
    lower_half = values[:, :column_half]
    upper_half = values[:, column_half:]
    kept_half = jnp.where(sibling == 0, lower_half, upper_half)
    sent_half = jnp.where(sibling == 0, upper_half, lower_half)
    return (kept_half, sent_half)


def pair_swap(block, axis):
    return lax.ppermute(block, axis, [(0, 1), (1, 0)])


def two_section_solve(factor, right_side, section, precision):
    tile_rows = right_side.shape[0]
    diagonal = lax.dynamic_slice_in_dim(factor, section * tile_rows, tile_rows, 1)
    first = matmul(diagonal, right_side, precision)
    arrived = lax.ppermute(first, "rows", [(0, 1)])
    coupling = matmul(diagonal, factor[:, :tile_rows], precision)
    return first - matmul(coupling, arrived, precision)


def inverse_order(update_blocks):
    targets = update_blocks[0]
    count = targets.shape[0]
    hits = targets[:, None] == jnp.arange(count)[None, :]
    return jnp.sum(jnp.where(hits, jnp.arange(count)[:, None], 0), axis=0)


def placed_rows(product, order, section):
    per_section = product.shape[0] // ROW_BLOCK // 2
    pieces = []
    for k in range(per_section):
        block = lax.dynamic_index_in_dim(order, section * per_section + k, keepdims=False)
        pieces.append(lax.dynamic_slice_in_dim(product, block * ROW_BLOCK, ROW_BLOCK, 0))
    return jnp.concatenate(pieces, 0)


def two_section_shards(leaf_factor, leaf_rhs, update_panel, update_blocks, parent_factor, parent_rhs):
    section = lax.axis_index("rows")
    precision = lax.Precision.HIGH
    leaf_solution = two_section_solve(leaf_factor, leaf_rhs, section, precision)
    order = inverse_order(update_blocks)
    product = matmul(update_panel, leaf_solution, precision)
    other_rows = placed_rows(product, order, 1 - section)
    arrived_rows = pair_swap(other_rows, "rows")
    chip_sum = placed_rows(product, order, section) + arrived_rows
    column_half = parent_rhs.shape[1]
    sibling = lax.axis_index("leaf") % 2
    kept = lax.dynamic_slice_in_dim(chip_sum, sibling * column_half, column_half, 1)
    sent = lax.dynamic_slice_in_dim(chip_sum, (1 - sibling) * column_half, column_half, 1)
    tile_rows = parent_rhs.shape[0]
    diagonal = lax.dynamic_slice_in_dim(parent_factor, section * tile_rows, tile_rows, 1)
    coupling = matmul(diagonal, parent_factor[:, :tile_rows], precision)
    arrived = swapped(sent, "leaf", 0)
    arrived, coupling = lax.optimization_barrier((arrived, coupling))
    pending = parent_rhs - (kept + arrived)
    first = matmul(diagonal, pending, precision)
    arrived = lax.ppermute(first, "rows", [(0, 1)])
    parent_solution = first - matmul(coupling, arrived, precision)
    return (leaf_solution, parent_solution)


def shards(leaf_factor, leaf_rhs, update_panel, update_blocks, parent_factor, parent_rhs):
    sections = lax.axis_size("rows")
    if sections == 2:
        return two_section_shards(leaf_factor, leaf_rhs, update_panel, update_blocks, parent_factor, parent_rhs)
    section = lax.axis_index("rows")
    leaf_solution = front_forward(leaf_factor, leaf_rhs, section, sections, leaf_pass)
    panel_product = matmul(update_panel, leaf_solution)
    columns = panel_product.shape[1]
    pieces = panel_product.reshape(-1, ROW_BLOCK, columns)
    placed = jnp.zeros_like(pieces).at[update_blocks[0]].set(pieces).reshape(panel_product.shape)
    column_half = parent_rhs.shape[1]
    sibling = lax.axis_index("leaf") % 2
    kept_half, sent_half = split_halves(placed, sibling, column_half)
    arrived = swapped(sent_half, "leaf", 0)
    update_sum = lax.psum_scatter(kept_half + arrived, "rows", scatter_dimension=0, tiled=True)
    pending = parent_rhs - update_sum
    parent_solution = front_forward(parent_factor, pending, section, sections, parent_pass)
    return (leaf_solution, parent_solution)


def solution(mesh):
    placed = (
        P(("leaf", "rows"), None),
        P(("leaf", "rows"), None),
        P("leaf", "rows"),
        P("leaf", None),
        P(("leaf", "rows"), None),
        P(("leaf", "rows"), None),
    )
    return jax.shard_map(
        shards,
        mesh=mesh,
        in_specs=placed,
        out_specs=(P(("leaf", "rows"), None), P(("leaf", "rows"), None)),
        check_vma=False,
    )
```

```python
import jax
import jax.numpy as jnp
from jax import lax
from jax.sharding import PartitionSpec as P

ROW_BLOCK = 128


def passed_along(array, axis, by):
    size = lax.axis_size(axis)
    pairs = [(i, i + by) for i in range(size) if 0 <= i + by < size]
    return lax.ppermute(array, axis, pairs)


def swapped(block, axis, apart):
    count = lax.axis_size(axis)
    route = []
    for low in range(count):
        high = low | 1 << apart
        if high != low and high < count:
            route += [(low, high), (high, low)]
    return lax.ppermute(block, axis, route)


def matmul(left, right, precision=lax.Precision.HIGHEST):
    return jnp.dot(left, right, precision=precision, preferred_element_type=jnp.float32)


def leaf_pass(outgoing):
    return passed_along(outgoing, "rows", 1)


def parent_pass(outgoing):
    return passed_along(outgoing, "rows", 1)


def front_forward(factor, right_side, section, sections, pass_tile):
    tile_rows = right_side.shape[0]

    def advance(tick, state):
        pending, solution, incoming = state
        source = tick - section
        useful = jnp.logical_and(source >= 0, source < section)
        safe_source = jnp.clip(source, 0, sections - 1)

        def apply_tile(values):
            factor_tile = lax.dynamic_slice_in_dim(factor, safe_source * tile_rows, tile_rows, 1)
            return values - matmul(factor_tile, incoming)

        pending = lax.cond(useful, apply_tile, lambda values: values, pending)
        own_turn = tick == 2 * section

        def solve_own(values):
            diagonal_tile = lax.dynamic_slice_in_dim(factor, section * tile_rows, tile_rows, 1)
            return matmul(diagonal_tile, values)

        solution = lax.cond(own_turn, solve_own, lambda values: solution, pending)
        outgoing = jnp.where(
            own_turn, solution, jnp.where(useful, incoming, jnp.zeros_like(incoming))
        )
        incoming = pass_tile(outgoing)
        return (pending, solution, incoming)

    initial = (right_side, jnp.zeros_like(right_side), jnp.zeros_like(right_side))
    return lax.fori_loop(0, 2 * sections - 1, advance, initial)[1]


def split_halves(values, sibling, column_half):
    lower_half = values[:, :column_half]
    upper_half = values[:, column_half:]
    kept_half = jnp.where(sibling == 0, lower_half, upper_half)
    sent_half = jnp.where(sibling == 0, upper_half, lower_half)
    return (kept_half, sent_half)


def pair_swap(block, axis):
    return lax.ppermute(block, axis, [(0, 1), (1, 0)])


def two_section_solve(factor, right_side, section, precision):
    tile_rows = right_side.shape[0]
    diagonal = lax.dynamic_slice_in_dim(factor, section * tile_rows, tile_rows, 1)
    first = matmul(diagonal, right_side, precision)
    arrived = lax.ppermute(first, "rows", [(0, 1)])
    coupling = matmul(diagonal, factor[:, :tile_rows], precision)
    return first - matmul(coupling, arrived, precision)


def inverse_order(update_blocks):
    targets = update_blocks[0]
    count = targets.shape[0]
    hits = targets[:, None] == jnp.arange(count)[None, :]
    return jnp.sum(jnp.where(hits, jnp.arange(count)[:, None], 0), axis=0)


def two_section_shards(leaf_factor, leaf_rhs, update_panel, update_blocks, parent_factor, parent_rhs):
    section = lax.axis_index("rows")
    precision = lax.Precision.HIGH
    leaf_solution = two_section_solve(leaf_factor, leaf_rhs, section, precision)
    blocks = update_panel.reshape(-1, ROW_BLOCK, update_panel.shape[1])
    panel_placed = jnp.take(blocks, inverse_order(update_blocks), axis=0, mode="clip")
    placed = matmul(panel_placed.reshape(update_panel.shape), leaf_solution, precision)
    rows_half = placed.shape[0] // 2
    own_rows = lax.dynamic_slice_in_dim(placed, section * rows_half, rows_half, 0)
    other_rows = lax.dynamic_slice_in_dim(placed, (1 - section) * rows_half, rows_half, 0)
    chip_sum = own_rows + pair_swap(other_rows, "rows")
    column_half = parent_rhs.shape[1]
    sibling = lax.axis_index("leaf") % 2
    kept = lax.dynamic_slice_in_dim(chip_sum, sibling * column_half, column_half, 1)
    sent = lax.dynamic_slice_in_dim(chip_sum, (1 - sibling) * column_half, column_half, 1)
    tile_rows = parent_rhs.shape[0]
    diagonal = lax.dynamic_slice_in_dim(parent_factor, section * tile_rows, tile_rows, 1)
    coupling = matmul(diagonal, parent_factor[:, :tile_rows], precision)
    arrived = swapped(sent, "leaf", 0)
    arrived, coupling = lax.optimization_barrier((arrived, coupling))
    pending = parent_rhs - (kept + arrived)
    first = matmul(diagonal, pending, precision)
    arrived = lax.ppermute(first, "rows", [(0, 1)])
    parent_solution = first - matmul(coupling, arrived, precision)
    return (leaf_solution, parent_solution)


def shards(leaf_factor, leaf_rhs, update_panel, update_blocks, parent_factor, parent_rhs):
    sections = lax.axis_size("rows")
    if sections == 2:
        return two_section_shards(leaf_factor, leaf_rhs, update_panel, update_blocks, parent_factor, parent_rhs)
    section = lax.axis_index("rows")
    leaf_solution = front_forward(leaf_factor, leaf_rhs, section, sections, leaf_pass)
    panel_product = matmul(update_panel, leaf_solution)
    columns = panel_product.shape[1]
    pieces = panel_product.reshape(-1, ROW_BLOCK, columns)
    placed = jnp.zeros_like(pieces).at[update_blocks[0]].set(pieces).reshape(panel_product.shape)
    column_half = parent_rhs.shape[1]
    sibling = lax.axis_index("leaf") % 2
    kept_half, sent_half = split_halves(placed, sibling, column_half)
    arrived = swapped(sent_half, "leaf", 0)
    update_sum = lax.psum_scatter(kept_half + arrived, "rows", scatter_dimension=0, tiled=True)
    pending = parent_rhs - update_sum
    parent_solution = front_forward(parent_factor, pending, section, sections, parent_pass)
    return (leaf_solution, parent_solution)


def solution(mesh):
    placed = (
        P(("leaf", "rows"), None),
        P(("leaf", "rows"), None),
        P("leaf", "rows"),
        P("leaf", None),
        P(("leaf", "rows"), None),
        P(("leaf", "rows"), None),
    )
    return jax.shard_map(
        shards,
        mesh=mesh,
        in_specs=placed,
        out_specs=(P(("leaf", "rows"), None), P(("leaf", "rows"), None)),
        check_vma=False,
    )
```

```python
import jax
import jax.numpy as jnp
from jax import lax
from jax.sharding import PartitionSpec as P

ROW_BLOCK = 128


def passed_along(array, axis, by):
    size = lax.axis_size(axis)
    pairs = [(i, i + by) for i in range(size) if 0 <= i + by < size]
    return lax.ppermute(array, axis, pairs)


def swapped(block, axis, apart):
    count = lax.axis_size(axis)
    route = []
    for low in range(count):
        high = low | 1 << apart
        if high != low and high < count:
            route += [(low, high), (high, low)]
    return lax.ppermute(block, axis, route)


def matmul(left, right, precision=lax.Precision.HIGHEST):
    return jnp.dot(left, right, precision=precision, preferred_element_type=jnp.float32)


def leaf_pass(outgoing):
    return passed_along(outgoing, "rows", 1)


def parent_pass(outgoing):
    return passed_along(outgoing, "rows", 1)


def front_forward(factor, right_side, section, sections, pass_tile):
    tile_rows = right_side.shape[0]

    def advance(tick, state):
        pending, solution, incoming = state
        source = tick - section
        useful = jnp.logical_and(source >= 0, source < section)
        safe_source = jnp.clip(source, 0, sections - 1)

        def apply_tile(values):
            factor_tile = lax.dynamic_slice_in_dim(factor, safe_source * tile_rows, tile_rows, 1)
            return values - matmul(factor_tile, incoming)

        pending = lax.cond(useful, apply_tile, lambda values: values, pending)
        own_turn = tick == 2 * section

        def solve_own(values):
            diagonal_tile = lax.dynamic_slice_in_dim(factor, section * tile_rows, tile_rows, 1)
            return matmul(diagonal_tile, values)

        solution = lax.cond(own_turn, solve_own, lambda values: solution, pending)
        outgoing = jnp.where(
            own_turn, solution, jnp.where(useful, incoming, jnp.zeros_like(incoming))
        )
        incoming = pass_tile(outgoing)
        return (pending, solution, incoming)

    initial = (right_side, jnp.zeros_like(right_side), jnp.zeros_like(right_side))
    return lax.fori_loop(0, 2 * sections - 1, advance, initial)[1]


def split_halves(values, sibling, column_half):
    lower_half = values[:, :column_half]
    upper_half = values[:, column_half:]
    kept_half = jnp.where(sibling == 0, lower_half, upper_half)
    sent_half = jnp.where(sibling == 0, upper_half, lower_half)
    return (kept_half, sent_half)


def pair_swap(block, axis):
    return lax.ppermute(block, axis, [(0, 1), (1, 0)])


def lower_coupling(factor, diagonal, section, precision):
    tile_rows = diagonal.shape[0]
    below = jnp.where(section > 0, factor[:, :tile_rows], jnp.zeros_like(diagonal))
    return matmul(diagonal, below, precision)


def two_section_solve(factor, right_side, section, precision):
    tile_rows = right_side.shape[0]
    diagonal = lax.dynamic_slice_in_dim(factor, section * tile_rows, tile_rows, 1)
    first = matmul(diagonal, right_side, precision)
    arrived = pair_swap(first, "rows")
    coupling = lower_coupling(factor, diagonal, section, precision)
    return first - matmul(coupling, arrived, precision)


def inverse_order(update_blocks):
    targets = update_blocks[0]
    count = targets.shape[0]
    hits = targets[:, None] == jnp.arange(count)[None, :]
    return jnp.sum(jnp.where(hits, jnp.arange(count)[:, None], 0), axis=0)


def two_section_shards(leaf_factor, leaf_rhs, update_panel, update_blocks, parent_factor, parent_rhs):
    section = lax.axis_index("rows")
    precision = lax.Precision.HIGH
    leaf_solution = two_section_solve(leaf_factor, leaf_rhs, section, precision)
    blocks = update_panel.reshape(-1, ROW_BLOCK, update_panel.shape[1])
    panel_placed = jnp.take(blocks, inverse_order(update_blocks), axis=0, mode="clip")
    placed = matmul(panel_placed.reshape(update_panel.shape), leaf_solution, precision)
    rows_half = placed.shape[0] // 2
    own_rows = lax.dynamic_slice_in_dim(placed, section * rows_half, rows_half, 0)
    other_rows = lax.dynamic_slice_in_dim(placed, (1 - section) * rows_half, rows_half, 0)
    chip_sum = own_rows + pair_swap(other_rows, "rows")
    column_half = parent_rhs.shape[1]
    sibling = lax.axis_index("leaf") % 2
    kept = lax.dynamic_slice_in_dim(chip_sum, sibling * column_half, column_half, 1)
    sent = lax.dynamic_slice_in_dim(chip_sum, (1 - sibling) * column_half, column_half, 1)
    tile_rows = parent_rhs.shape[0]
    diagonal = lax.dynamic_slice_in_dim(parent_factor, section * tile_rows, tile_rows, 1)
    coupling = lower_coupling(parent_factor, diagonal, section, precision)
    arrived = swapped(sent, "leaf", 0)
    arrived, coupling = lax.optimization_barrier((arrived, coupling))
    pending = parent_rhs - (kept + arrived)
    first = matmul(diagonal, pending, precision)
    arrived = pair_swap(first, "rows")
    parent_solution = first - matmul(coupling, arrived, precision)
    return (leaf_solution, parent_solution)


def shards(leaf_factor, leaf_rhs, update_panel, update_blocks, parent_factor, parent_rhs):
    sections = lax.axis_size("rows")
    if sections == 2:
        return two_section_shards(leaf_factor, leaf_rhs, update_panel, update_blocks, parent_factor, parent_rhs)
    section = lax.axis_index("rows")
    leaf_solution = front_forward(leaf_factor, leaf_rhs, section, sections, leaf_pass)
    panel_product = matmul(update_panel, leaf_solution)
    columns = panel_product.shape[1]
    pieces = panel_product.reshape(-1, ROW_BLOCK, columns)
    placed = jnp.zeros_like(pieces).at[update_blocks[0]].set(pieces).reshape(panel_product.shape)
    column_half = parent_rhs.shape[1]
    sibling = lax.axis_index("leaf") % 2
    kept_half, sent_half = split_halves(placed, sibling, column_half)
    arrived = swapped(sent_half, "leaf", 0)
    update_sum = lax.psum_scatter(kept_half + arrived, "rows", scatter_dimension=0, tiled=True)
    pending = parent_rhs - update_sum
    parent_solution = front_forward(parent_factor, pending, section, sections, parent_pass)
    return (leaf_solution, parent_solution)


def solution(mesh):
    placed = (
        P(("leaf", "rows"), None),
        P(("leaf", "rows"), None),
        P("leaf", "rows"),
        P("leaf", None),
        P(("leaf", "rows"), None),
        P(("leaf", "rows"), None),
    )
    return jax.shard_map(
        shards,
        mesh=mesh,
        in_specs=placed,
        out_specs=(P(("leaf", "rows"), None), P(("leaf", "rows"), None)),
        check_vma=False,
    )
```

```python
import jax
import jax.numpy as jnp
from jax import lax
from jax.sharding import PartitionSpec as P

ROW_BLOCK = 128


def passed_along(array, axis, by):
    size = lax.axis_size(axis)
    pairs = [(i, i + by) for i in range(size) if 0 <= i + by < size]
    return lax.ppermute(array, axis, pairs)


def swapped(block, axis, apart):
    count = lax.axis_size(axis)
    route = []
    for low in range(count):
        high = low | 1 << apart
        if high != low and high < count:
            route += [(low, high), (high, low)]
    return lax.ppermute(block, axis, route)


def matmul(left, right, precision=lax.Precision.HIGHEST):
    return jnp.dot(left, right, precision=precision, preferred_element_type=jnp.float32)


def leaf_pass(outgoing):
    return passed_along(outgoing, "rows", 1)


def parent_pass(outgoing):
    return passed_along(outgoing, "rows", 1)


def front_forward(factor, right_side, section, sections, pass_tile):
    tile_rows = right_side.shape[0]

    def advance(tick, state):
        pending, solution, incoming = state
        source = tick - section
        useful = jnp.logical_and(source >= 0, source < section)
        safe_source = jnp.clip(source, 0, sections - 1)

        def apply_tile(values):
            factor_tile = lax.dynamic_slice_in_dim(factor, safe_source * tile_rows, tile_rows, 1)
            return values - matmul(factor_tile, incoming)

        pending = lax.cond(useful, apply_tile, lambda values: values, pending)
        own_turn = tick == 2 * section

        def solve_own(values):
            diagonal_tile = lax.dynamic_slice_in_dim(factor, section * tile_rows, tile_rows, 1)
            return matmul(diagonal_tile, values)

        solution = lax.cond(own_turn, solve_own, lambda values: solution, pending)
        outgoing = jnp.where(
            own_turn, solution, jnp.where(useful, incoming, jnp.zeros_like(incoming))
        )
        incoming = pass_tile(outgoing)
        return (pending, solution, incoming)

    initial = (right_side, jnp.zeros_like(right_side), jnp.zeros_like(right_side))
    return lax.fori_loop(0, 2 * sections - 1, advance, initial)[1]


def split_halves(values, sibling, column_half):
    lower_half = values[:, :column_half]
    upper_half = values[:, column_half:]
    kept_half = jnp.where(sibling == 0, lower_half, upper_half)
    sent_half = jnp.where(sibling == 0, upper_half, lower_half)
    return (kept_half, sent_half)


def pair_swap(block, axis):
    return lax.ppermute(block, axis, [(0, 1), (1, 0)])


def lower_coupling(factor, diagonal, section, precision):
    tile_rows = diagonal.shape[0]
    below = jnp.where(section > 0, factor[:, :tile_rows], jnp.zeros_like(diagonal))
    return matmul(diagonal, below, precision)


def two_section_leaf(factor, right_side, section, precision):
    tile_rows = right_side.shape[0]
    diagonal = lax.dynamic_slice_in_dim(factor, section * tile_rows, tile_rows, 1)
    first = matmul(diagonal, right_side, precision)
    arrived = pair_swap(first, "rows")
    below = jnp.where(section > 0, factor[:, :tile_rows], jnp.zeros_like(diagonal))
    return matmul(diagonal, right_side - matmul(below, arrived, precision), precision)


def inverse_order(update_blocks):
    targets = update_blocks[0]
    count = targets.shape[0]
    hits = targets[:, None] == jnp.arange(count)[None, :]
    return jnp.sum(jnp.where(hits, jnp.arange(count)[:, None], 0), axis=0)


def two_section_shards(leaf_factor, leaf_rhs, update_panel, update_blocks, parent_factor, parent_rhs):
    section = lax.axis_index("rows")
    precision = lax.Precision.HIGH
    leaf_solution = two_section_leaf(leaf_factor, leaf_rhs, section, precision)
    blocks = update_panel.reshape(-1, ROW_BLOCK, update_panel.shape[1])
    order = inverse_order(update_blocks)
    per_section = blocks.shape[0] // 2

    def section_panel(rows_of):
        chosen = lax.dynamic_slice_in_dim(order, rows_of * per_section, per_section)
        taken = jnp.take(blocks, chosen, axis=0, mode="clip")
        return taken.reshape(-1, update_panel.shape[1])

    other_rows = matmul(section_panel(1 - section), leaf_solution, precision)
    arrived_rows = pair_swap(other_rows, "rows")
    chip_sum = matmul(section_panel(section), leaf_solution, precision) + arrived_rows
    column_half = parent_rhs.shape[1]
    sibling = lax.axis_index("leaf") % 2
    kept = lax.dynamic_slice_in_dim(chip_sum, sibling * column_half, column_half, 1)
    sent = lax.dynamic_slice_in_dim(chip_sum, (1 - sibling) * column_half, column_half, 1)
    tile_rows = parent_rhs.shape[0]
    diagonal = lax.dynamic_slice_in_dim(parent_factor, section * tile_rows, tile_rows, 1)
    coupling = lower_coupling(parent_factor, diagonal, section, precision)
    arrived = swapped(sent, "leaf", 0)
    arrived, coupling = lax.optimization_barrier((arrived, coupling))
    pending = parent_rhs - (kept + arrived)
    first = matmul(diagonal, pending, precision)
    arrived = pair_swap(first, "rows")
    parent_solution = first - matmul(coupling, arrived, precision)
    return (leaf_solution, parent_solution)


def shards(leaf_factor, leaf_rhs, update_panel, update_blocks, parent_factor, parent_rhs):
    sections = lax.axis_size("rows")
    if sections == 2:
        return two_section_shards(leaf_factor, leaf_rhs, update_panel, update_blocks, parent_factor, parent_rhs)
    section = lax.axis_index("rows")
    leaf_solution = front_forward(leaf_factor, leaf_rhs, section, sections, leaf_pass)
    panel_product = matmul(update_panel, leaf_solution)
    columns = panel_product.shape[1]
    pieces = panel_product.reshape(-1, ROW_BLOCK, columns)
    placed = jnp.zeros_like(pieces).at[update_blocks[0]].set(pieces).reshape(panel_product.shape)
    column_half = parent_rhs.shape[1]
    sibling = lax.axis_index("leaf") % 2
    kept_half, sent_half = split_halves(placed, sibling, column_half)
    arrived = swapped(sent_half, "leaf", 0)
    update_sum = lax.psum_scatter(kept_half + arrived, "rows", scatter_dimension=0, tiled=True)
    pending = parent_rhs - update_sum
    parent_solution = front_forward(parent_factor, pending, section, sections, parent_pass)
    return (leaf_solution, parent_solution)


def solution(mesh):
    placed = (
        P(("leaf", "rows"), None),
        P(("leaf", "rows"), None),
        P("leaf", "rows"),
        P("leaf", None),
        P(("leaf", "rows"), None),
        P(("leaf", "rows"), None),
    )
    return jax.shard_map(
        shards,
        mesh=mesh,
        in_specs=placed,
        out_specs=(P(("leaf", "rows"), None), P(("leaf", "rows"), None)),
        check_vma=False,
    )
```

```python
import jax
import jax.numpy as jnp
from jax import lax
from jax.sharding import PartitionSpec as P
from jax.experimental import pallas as pl
from jax.experimental.pallas import tpu as pltpu

ROW_BLOCK = 128


def passed_along(array, axis, by):
    size = lax.axis_size(axis)
    pairs = [(i, i + by) for i in range(size) if 0 <= i + by < size]
    return lax.ppermute(array, axis, pairs)


def swapped(block, axis, apart):
    count = lax.axis_size(axis)
    route = []
    for low in range(count):
        high = low | 1 << apart
        if high != low and high < count:
            route += [(low, high), (high, low)]
    return lax.ppermute(block, axis, route)


def matmul(left, right, precision=lax.Precision.HIGHEST):
    return jnp.dot(left, right, precision=precision, preferred_element_type=jnp.float32)


def leaf_pass(outgoing):
    return passed_along(outgoing, "rows", 1)


def parent_pass(outgoing):
    return passed_along(outgoing, "rows", 1)


def front_forward(factor, right_side, section, sections, pass_tile):
    tile_rows = right_side.shape[0]

    def advance(tick, state):
        pending, solution, incoming = state
        source = tick - section
        useful = jnp.logical_and(source >= 0, source < section)
        safe_source = jnp.clip(source, 0, sections - 1)

        def apply_tile(values):
            factor_tile = lax.dynamic_slice_in_dim(factor, safe_source * tile_rows, tile_rows, 1)
            return values - matmul(factor_tile, incoming)

        pending = lax.cond(useful, apply_tile, lambda values: values, pending)
        own_turn = tick == 2 * section

        def solve_own(values):
            diagonal_tile = lax.dynamic_slice_in_dim(factor, section * tile_rows, tile_rows, 1)
            return matmul(diagonal_tile, values)

        solution = lax.cond(own_turn, solve_own, lambda values: solution, pending)
        outgoing = jnp.where(
            own_turn, solution, jnp.where(useful, incoming, jnp.zeros_like(incoming))
        )
        incoming = pass_tile(outgoing)
        return (pending, solution, incoming)

    initial = (right_side, jnp.zeros_like(right_side), jnp.zeros_like(right_side))
    return lax.fori_loop(0, 2 * sections - 1, advance, initial)[1]


def split_halves(values, sibling, column_half):
    lower_half = values[:, :column_half]
    upper_half = values[:, column_half:]
    kept_half = jnp.where(sibling == 0, lower_half, upper_half)
    sent_half = jnp.where(sibling == 0, upper_half, lower_half)
    return (kept_half, sent_half)


def split_bf16(values):
    high = values.astype(jnp.bfloat16)
    low = (values - high.astype(jnp.float32)).astype(jnp.bfloat16)
    return high, low


def dot_bf16x3(left, right):
    left_high, left_low = split_bf16(left)
    right_high, right_low = split_bf16(right)

    def part(a, b):
        return jnp.dot(a, b, preferred_element_type=jnp.float32)

    return part(left_high, right_high) + (part(left_low, right_high) + part(left_high, right_low))


def block_matmul_kernel(rows_ref, column_ref, keep_ref, left_ref, right_ref, *rest):
    product = dot_bf16x3(left_ref[...], right_ref[...])
    if len(rest) == 1:
        rest[0][...] = product
        return
    extra_ref, out_ref = rest
    out_ref[...] = extra_ref[...] - jnp.where(keep_ref[0] > 0, product, 0.0)


def block_matmul(left, right, rows, column, block_rows, extra=None, keep=None):
    inner, width = right.shape
    steps = rows.shape[0]
    if keep is None:
        keep = jnp.ones((1,), jnp.int32)
    in_specs = [
        pl.BlockSpec((block_rows, inner), lambda i, r, c, k: (r[i], c[0])),
        pl.BlockSpec((inner, width), lambda i, r, c, k: (0, 0)),
    ]
    operands = [left, right]
    if extra is not None:
        in_specs.append(pl.BlockSpec((block_rows, width), lambda i, r, c, k: (i, 0)))
        operands.append(extra)
    grid_spec = pltpu.PrefetchScalarGridSpec(
        num_scalar_prefetch=3,
        grid=(steps,),
        in_specs=in_specs,
        out_specs=pl.BlockSpec((block_rows, width), lambda i, r, c, k: (i, 0)),
    )
    return pl.pallas_call(
        block_matmul_kernel,
        grid_spec=grid_spec,
        out_shape=jax.ShapeDtypeStruct((steps * block_rows, width), jnp.float32),
    )(rows.astype(jnp.int32), jnp.reshape(column, (1,)).astype(jnp.int32), jnp.reshape(keep, (1,)).astype(jnp.int32), *operands)


def pair_swap(block, axis):
    return lax.ppermute(block, axis, [(0, 1), (1, 0)])


def lower_coupling(factor, diagonal, section, precision):
    tile_rows = diagonal.shape[0]
    below = jnp.where(section > 0, factor[:, :tile_rows], jnp.zeros_like(diagonal))
    return matmul(diagonal, below, precision)


def two_section_leaf(factor, right_side, section):
    tile_rows = right_side.shape[0]
    steps = jnp.arange(tile_rows // ROW_BLOCK)
    first = block_matmul(factor, right_side, steps, section, ROW_BLOCK)
    arrived = pair_swap(first, "rows")
    target = block_matmul(factor, arrived, steps, 0, ROW_BLOCK, extra=right_side, keep=section)
    return block_matmul(factor, target, steps, section, ROW_BLOCK)


def inverse_order(update_blocks):
    targets = update_blocks[0]
    count = targets.shape[0]
    hits = targets[:, None] == jnp.arange(count)[None, :]
    return jnp.sum(jnp.where(hits, jnp.arange(count)[:, None], 0), axis=0)


def two_section_shards(leaf_factor, leaf_rhs, update_panel, update_blocks, parent_factor, parent_rhs):
    section = lax.axis_index("rows")
    precision = lax.Precision.HIGH
    leaf_solution = two_section_leaf(leaf_factor, leaf_rhs, section)
    order = inverse_order(update_blocks)
    per_section = order.shape[0] // 2
    other_blocks = lax.dynamic_slice_in_dim(order, (1 - section) * per_section, per_section)
    own_blocks = lax.dynamic_slice_in_dim(order, section * per_section, per_section)
    other_rows = block_matmul(update_panel, leaf_solution, other_blocks, 0, ROW_BLOCK)
    arrived_rows = pair_swap(other_rows, "rows")
    chip_sum = block_matmul(update_panel, leaf_solution, own_blocks, 0, ROW_BLOCK) + arrived_rows
    column_half = parent_rhs.shape[1]
    sibling = lax.axis_index("leaf") % 2
    kept = lax.dynamic_slice_in_dim(chip_sum, sibling * column_half, column_half, 1)
    sent = lax.dynamic_slice_in_dim(chip_sum, (1 - sibling) * column_half, column_half, 1)
    tile_rows = parent_rhs.shape[0]
    diagonal = lax.dynamic_slice_in_dim(parent_factor, section * tile_rows, tile_rows, 1)
    coupling = lower_coupling(parent_factor, diagonal, section, precision)
    arrived = swapped(sent, "leaf", 0)
    arrived, coupling = lax.optimization_barrier((arrived, coupling))
    pending = parent_rhs - (kept + arrived)
    first = matmul(diagonal, pending, precision)
    arrived = pair_swap(first, "rows")
    steps = jnp.arange(tile_rows // ROW_BLOCK)
    parent_solution = block_matmul(coupling, arrived, steps, 0, ROW_BLOCK, extra=first)
    return (leaf_solution, parent_solution)


def shards(leaf_factor, leaf_rhs, update_panel, update_blocks, parent_factor, parent_rhs):
    sections = lax.axis_size("rows")
    if sections == 2:
        return two_section_shards(leaf_factor, leaf_rhs, update_panel, update_blocks, parent_factor, parent_rhs)
    section = lax.axis_index("rows")
    leaf_solution = front_forward(leaf_factor, leaf_rhs, section, sections, leaf_pass)
    panel_product = matmul(update_panel, leaf_solution)
    columns = panel_product.shape[1]
    pieces = panel_product.reshape(-1, ROW_BLOCK, columns)
    placed = jnp.zeros_like(pieces).at[update_blocks[0]].set(pieces).reshape(panel_product.shape)
    column_half = parent_rhs.shape[1]
    sibling = lax.axis_index("leaf") % 2
    kept_half, sent_half = split_halves(placed, sibling, column_half)
    arrived = swapped(sent_half, "leaf", 0)
    update_sum = lax.psum_scatter(kept_half + arrived, "rows", scatter_dimension=0, tiled=True)
    pending = parent_rhs - update_sum
    parent_solution = front_forward(parent_factor, pending, section, sections, parent_pass)
    return (leaf_solution, parent_solution)


def solution(mesh):
    placed = (
        P(("leaf", "rows"), None),
        P(("leaf", "rows"), None),
        P("leaf", "rows"),
        P("leaf", None),
        P(("leaf", "rows"), None),
        P(("leaf", "rows"), None),
    )
    return jax.shard_map(
        shards,
        mesh=mesh,
        in_specs=placed,
        out_specs=(P(("leaf", "rows"), None), P(("leaf", "rows"), None)),
        check_vma=False,
    )
```

```python
import jax
import jax.numpy as jnp
from jax import lax
from jax.sharding import PartitionSpec as P

ROW_BLOCK = 128


def passed_along(array, axis, by):
    size = lax.axis_size(axis)
    pairs = [(i, i + by) for i in range(size) if 0 <= i + by < size]
    return lax.ppermute(array, axis, pairs)


def swapped(block, axis, apart):
    count = lax.axis_size(axis)
    route = []
    for low in range(count):
        high = low | 1 << apart
        if high != low and high < count:
            route += [(low, high), (high, low)]
    return lax.ppermute(block, axis, route)


def matmul(left, right, precision=lax.Precision.HIGHEST):
    return jnp.dot(left, right, precision=precision, preferred_element_type=jnp.float32)


def leaf_pass(outgoing):
    return passed_along(outgoing, "rows", 1)


def parent_pass(outgoing):
    return passed_along(outgoing, "rows", 1)


def front_forward(factor, right_side, section, sections, pass_tile):
    tile_rows = right_side.shape[0]

    def advance(tick, state):
        pending, solution, incoming = state
        source = tick - section
        useful = jnp.logical_and(source >= 0, source < section)
        safe_source = jnp.clip(source, 0, sections - 1)

        def apply_tile(values):
            factor_tile = lax.dynamic_slice_in_dim(factor, safe_source * tile_rows, tile_rows, 1)
            return values - matmul(factor_tile, incoming)

        pending = lax.cond(useful, apply_tile, lambda values: values, pending)
        own_turn = tick == 2 * section

        def solve_own(values):
            diagonal_tile = lax.dynamic_slice_in_dim(factor, section * tile_rows, tile_rows, 1)
            return matmul(diagonal_tile, values)

        solution = lax.cond(own_turn, solve_own, lambda values: solution, pending)
        outgoing = jnp.where(
            own_turn, solution, jnp.where(useful, incoming, jnp.zeros_like(incoming))
        )
        incoming = pass_tile(outgoing)
        return (pending, solution, incoming)

    initial = (right_side, jnp.zeros_like(right_side), jnp.zeros_like(right_side))
    return lax.fori_loop(0, 2 * sections - 1, advance, initial)[1]


def split_halves(values, sibling, column_half):
    lower_half = values[:, :column_half]
    upper_half = values[:, column_half:]
    kept_half = jnp.where(sibling == 0, lower_half, upper_half)
    sent_half = jnp.where(sibling == 0, upper_half, lower_half)
    return (kept_half, sent_half)


def pair_swap(block, axis):
    return lax.ppermute(block, axis, [(0, 1), (1, 0)])


def lower_coupling(factor, diagonal, section, precision):
    tile_rows = diagonal.shape[0]
    below = jnp.where(section > 0, factor[:, :tile_rows], jnp.zeros_like(diagonal))
    return matmul(diagonal, below, precision)


def two_section_leaf(factor, right_side, section, precision):
    tile_rows = right_side.shape[0]
    diagonal = lax.dynamic_slice_in_dim(factor, section * tile_rows, tile_rows, 1)
    diagonal = lax.optimization_barrier(diagonal)
    first = matmul(diagonal, right_side, precision)
    arrived = pair_swap(first, "rows")
    below = jnp.where(section > 0, factor[:, :tile_rows], jnp.zeros_like(diagonal))
    below, first = lax.optimization_barrier((below, first))
    return matmul(diagonal, right_side - matmul(below, arrived, precision), precision)


def inverse_order(update_blocks):
    targets = update_blocks[0]
    count = targets.shape[0]
    hits = targets[:, None] == jnp.arange(count)[None, :]
    return jnp.sum(jnp.where(hits, jnp.arange(count)[:, None], 0), axis=0)


def two_section_shards(leaf_factor, leaf_rhs, update_panel, update_blocks, parent_factor, parent_rhs):
    section = lax.axis_index("rows")
    precision = lax.Precision.HIGH
    leaf_solution = two_section_leaf(leaf_factor, leaf_rhs, section, precision)
    blocks = update_panel.reshape(-1, ROW_BLOCK, update_panel.shape[1])
    order = inverse_order(update_blocks)
    per_section = blocks.shape[0] // 2

    def section_panel(rows_of):
        chosen = lax.dynamic_slice_in_dim(order, rows_of * per_section, per_section)
        taken = jnp.take(blocks, chosen, axis=0, mode="clip")
        return taken.reshape(-1, update_panel.shape[1])

    other_rows = matmul(section_panel(1 - section), leaf_solution, precision)
    arrived_rows = pair_swap(other_rows, "rows")
    chip_sum = matmul(section_panel(section), leaf_solution, precision) + arrived_rows
    column_half = parent_rhs.shape[1]
    sibling = lax.axis_index("leaf") % 2
    kept = lax.dynamic_slice_in_dim(chip_sum, sibling * column_half, column_half, 1)
    sent = lax.dynamic_slice_in_dim(chip_sum, (1 - sibling) * column_half, column_half, 1)
    tile_rows = parent_rhs.shape[0]
    diagonal = lax.dynamic_slice_in_dim(parent_factor, section * tile_rows, tile_rows, 1)
    coupling = lower_coupling(parent_factor, diagonal, section, precision)
    arrived = swapped(sent, "leaf", 0)
    arrived, coupling = lax.optimization_barrier((arrived, coupling))
    pending = parent_rhs - (kept + arrived)
    first = matmul(diagonal, pending, precision)
    arrived = pair_swap(first, "rows")
    parent_solution = first - matmul(coupling, arrived, precision)
    return (leaf_solution, parent_solution)


def shards(leaf_factor, leaf_rhs, update_panel, update_blocks, parent_factor, parent_rhs):
    sections = lax.axis_size("rows")
    if sections == 2:
        return two_section_shards(leaf_factor, leaf_rhs, update_panel, update_blocks, parent_factor, parent_rhs)
    section = lax.axis_index("rows")
    leaf_solution = front_forward(leaf_factor, leaf_rhs, section, sections, leaf_pass)
    panel_product = matmul(update_panel, leaf_solution)
    columns = panel_product.shape[1]
    pieces = panel_product.reshape(-1, ROW_BLOCK, columns)
    placed = jnp.zeros_like(pieces).at[update_blocks[0]].set(pieces).reshape(panel_product.shape)
    column_half = parent_rhs.shape[1]
    sibling = lax.axis_index("leaf") % 2
    kept_half, sent_half = split_halves(placed, sibling, column_half)
    arrived = swapped(sent_half, "leaf", 0)
    update_sum = lax.psum_scatter(kept_half + arrived, "rows", scatter_dimension=0, tiled=True)
    pending = parent_rhs - update_sum
    parent_solution = front_forward(parent_factor, pending, section, sections, parent_pass)
    return (leaf_solution, parent_solution)


def solution(mesh):
    placed = (
        P(("leaf", "rows"), None),
        P(("leaf", "rows"), None),
        P("leaf", "rows"),
        P("leaf", None),
        P(("leaf", "rows"), None),
        P(("leaf", "rows"), None),
    )
    return jax.shard_map(
        shards,
        mesh=mesh,
        in_specs=placed,
        out_specs=(P(("leaf", "rows"), None), P(("leaf", "rows"), None)),
        check_vma=False,
    )
```

```python
import jax
import jax.numpy as jnp
from jax import lax
from jax.sharding import PartitionSpec as P

ROW_BLOCK = 128


def passed_along(array, axis, by):
    size = lax.axis_size(axis)
    pairs = [(i, i + by) for i in range(size) if 0 <= i + by < size]
    return lax.ppermute(array, axis, pairs)


def swapped(block, axis, apart):
    count = lax.axis_size(axis)
    route = []
    for low in range(count):
        high = low | 1 << apart
        if high != low and high < count:
            route += [(low, high), (high, low)]
    return lax.ppermute(block, axis, route)


def matmul(left, right, precision=lax.Precision.HIGHEST):
    return jnp.dot(left, right, precision=precision, preferred_element_type=jnp.float32)


def leaf_pass(outgoing):
    return passed_along(outgoing, "rows", 1)


def parent_pass(outgoing):
    return passed_along(outgoing, "rows", 1)


def front_forward(factor, right_side, section, sections, pass_tile):
    tile_rows = right_side.shape[0]

    def advance(tick, state):
        pending, solution, incoming = state
        source = tick - section
        useful = jnp.logical_and(source >= 0, source < section)
        safe_source = jnp.clip(source, 0, sections - 1)

        def apply_tile(values):
            factor_tile = lax.dynamic_slice_in_dim(factor, safe_source * tile_rows, tile_rows, 1)
            return values - matmul(factor_tile, incoming)

        pending = lax.cond(useful, apply_tile, lambda values: values, pending)
        own_turn = tick == 2 * section

        def solve_own(values):
            diagonal_tile = lax.dynamic_slice_in_dim(factor, section * tile_rows, tile_rows, 1)
            return matmul(diagonal_tile, values)

        solution = lax.cond(own_turn, solve_own, lambda values: solution, pending)
        outgoing = jnp.where(
            own_turn, solution, jnp.where(useful, incoming, jnp.zeros_like(incoming))
        )
        incoming = pass_tile(outgoing)
        return (pending, solution, incoming)

    initial = (right_side, jnp.zeros_like(right_side), jnp.zeros_like(right_side))
    return lax.fori_loop(0, 2 * sections - 1, advance, initial)[1]


def split_halves(values, sibling, column_half):
    lower_half = values[:, :column_half]
    upper_half = values[:, column_half:]
    kept_half = jnp.where(sibling == 0, lower_half, upper_half)
    sent_half = jnp.where(sibling == 0, upper_half, lower_half)
    return (kept_half, sent_half)


def pair_swap(block, axis):
    return lax.ppermute(block, axis, [(0, 1), (1, 0)])


def lower_coupling(factor, diagonal, section, precision):
    tile_rows = diagonal.shape[0]
    below = jnp.where(section > 0, factor[:, :tile_rows], jnp.zeros_like(diagonal))
    return matmul(diagonal, below, precision)


def two_section_leaf(factor, right_side, section, precision):
    tile_rows = right_side.shape[0]
    diagonal = lax.dynamic_slice_in_dim(factor, section * tile_rows, tile_rows, 1)
    first = matmul(diagonal, right_side, precision)
    arrived = pair_swap(first, "rows")
    below = jnp.where(section > 0, factor[:, :tile_rows], jnp.zeros_like(diagonal))
    return matmul(diagonal, right_side - matmul(below, arrived, precision), precision)


def inverse_order(update_blocks):
    targets = update_blocks[0]
    count = targets.shape[0]
    hits = targets[:, None] == jnp.arange(count)[None, :]
    return jnp.sum(jnp.where(hits, jnp.arange(count)[:, None], 0), axis=0)


def two_section_shards(leaf_factor, leaf_rhs, update_panel, update_blocks, parent_factor, parent_rhs):
    section = lax.axis_index("rows")
    precision = lax.Precision.HIGH
    leaf_solution = two_section_leaf(leaf_factor, leaf_rhs, section, precision)
    blocks = update_panel.reshape(-1, ROW_BLOCK, update_panel.shape[1])
    order = inverse_order(update_blocks)
    per_section = blocks.shape[0] // 2

    def section_panel(rows_of):
        chosen = lax.dynamic_slice_in_dim(order, rows_of * per_section, per_section)
        taken = jnp.take(blocks, chosen, axis=0, mode="clip")
        return taken.reshape(-1, update_panel.shape[1])

    other_rows = matmul(section_panel(1 - section), leaf_solution, precision)
    arrived_rows = pair_swap(other_rows, "rows")
    own_rows = matmul(section_panel(section), leaf_solution, precision)
    own_rows, arrived_rows = lax.optimization_barrier((own_rows, arrived_rows))
    chip_sum = own_rows + arrived_rows
    column_half = parent_rhs.shape[1]
    sibling = lax.axis_index("leaf") % 2
    kept = lax.dynamic_slice_in_dim(chip_sum, sibling * column_half, column_half, 1)
    sent = lax.dynamic_slice_in_dim(chip_sum, (1 - sibling) * column_half, column_half, 1)
    tile_rows = parent_rhs.shape[0]
    diagonal = lax.dynamic_slice_in_dim(parent_factor, section * tile_rows, tile_rows, 1)
    coupling = lower_coupling(parent_factor, diagonal, section, precision)
    arrived = swapped(sent, "leaf", 0)
    arrived, coupling = lax.optimization_barrier((arrived, coupling))
    pending = parent_rhs - (kept + arrived)
    first = matmul(diagonal, pending, precision)
    arrived = pair_swap(first, "rows")
    parent_solution = first - matmul(coupling, arrived, precision)
    return (leaf_solution, parent_solution)


def shards(leaf_factor, leaf_rhs, update_panel, update_blocks, parent_factor, parent_rhs):
    sections = lax.axis_size("rows")
    if sections == 2:
        return two_section_shards(leaf_factor, leaf_rhs, update_panel, update_blocks, parent_factor, parent_rhs)
    section = lax.axis_index("rows")
    leaf_solution = front_forward(leaf_factor, leaf_rhs, section, sections, leaf_pass)
    panel_product = matmul(update_panel, leaf_solution)
    columns = panel_product.shape[1]
    pieces = panel_product.reshape(-1, ROW_BLOCK, columns)
    placed = jnp.zeros_like(pieces).at[update_blocks[0]].set(pieces).reshape(panel_product.shape)
    column_half = parent_rhs.shape[1]
    sibling = lax.axis_index("leaf") % 2
    kept_half, sent_half = split_halves(placed, sibling, column_half)
    arrived = swapped(sent_half, "leaf", 0)
    update_sum = lax.psum_scatter(kept_half + arrived, "rows", scatter_dimension=0, tiled=True)
    pending = parent_rhs - update_sum
    parent_solution = front_forward(parent_factor, pending, section, sections, parent_pass)
    return (leaf_solution, parent_solution)


def solution(mesh):
    placed = (
        P(("leaf", "rows"), None),
        P(("leaf", "rows"), None),
        P("leaf", "rows"),
        P("leaf", None),
        P(("leaf", "rows"), None),
        P(("leaf", "rows"), None),
    )
    return jax.shard_map(
        shards,
        mesh=mesh,
        in_specs=placed,
        out_specs=(P(("leaf", "rows"), None), P(("leaf", "rows"), None)),
        check_vma=False,
    )
```

```python
import jax
import jax.numpy as jnp
from jax import lax
from jax.sharding import PartitionSpec as P

ROW_BLOCK = 128


def passed_along(array, axis, by):
    size = lax.axis_size(axis)
    pairs = [(i, i + by) for i in range(size) if 0 <= i + by < size]
    return lax.ppermute(array, axis, pairs)


def swapped(block, axis, apart):
    count = lax.axis_size(axis)
    route = []
    for low in range(count):
        high = low | 1 << apart
        if high != low and high < count:
            route += [(low, high), (high, low)]
    return lax.ppermute(block, axis, route)


def matmul(left, right, precision=lax.Precision.HIGHEST):
    return jnp.dot(left, right, precision=precision, preferred_element_type=jnp.float32)


def leaf_pass(outgoing):
    return passed_along(outgoing, "rows", 1)


def parent_pass(outgoing):
    return passed_along(outgoing, "rows", 1)


def front_forward(factor, right_side, section, sections, pass_tile):
    tile_rows = right_side.shape[0]

    def advance(tick, state):
        pending, solution, incoming = state
        source = tick - section
        useful = jnp.logical_and(source >= 0, source < section)
        safe_source = jnp.clip(source, 0, sections - 1)

        def apply_tile(values):
            factor_tile = lax.dynamic_slice_in_dim(factor, safe_source * tile_rows, tile_rows, 1)
            return values - matmul(factor_tile, incoming)

        pending = lax.cond(useful, apply_tile, lambda values: values, pending)
        own_turn = tick == 2 * section

        def solve_own(values):
            diagonal_tile = lax.dynamic_slice_in_dim(factor, section * tile_rows, tile_rows, 1)
            return matmul(diagonal_tile, values)

        solution = lax.cond(own_turn, solve_own, lambda values: solution, pending)
        outgoing = jnp.where(
            own_turn, solution, jnp.where(useful, incoming, jnp.zeros_like(incoming))
        )
        incoming = pass_tile(outgoing)
        return (pending, solution, incoming)

    initial = (right_side, jnp.zeros_like(right_side), jnp.zeros_like(right_side))
    return lax.fori_loop(0, 2 * sections - 1, advance, initial)[1]


def split_halves(values, sibling, column_half):
    lower_half = values[:, :column_half]
    upper_half = values[:, column_half:]
    kept_half = jnp.where(sibling == 0, lower_half, upper_half)
    sent_half = jnp.where(sibling == 0, upper_half, lower_half)
    return (kept_half, sent_half)


def pair_swap(block, axis):
    return lax.ppermute(block, axis, [(0, 1), (1, 0)])


def lower_coupling(factor, diagonal, section, precision):
    tile_rows = diagonal.shape[0]
    below = jnp.where(section > 0, factor[:, :tile_rows], jnp.zeros_like(diagonal))
    return matmul(diagonal, below, precision)


def two_section_leaf(factor, right_side, section, precision):
    tile_rows = right_side.shape[0]
    diagonal = lax.dynamic_slice_in_dim(factor, section * tile_rows, tile_rows, 1)
    first = matmul(diagonal, right_side, precision)
    arrived = pair_swap(first, "rows")
    below = jnp.where(section > 0, factor[:, :tile_rows], jnp.zeros_like(diagonal))
    return matmul(diagonal, right_side - matmul(below, arrived, precision), precision)


def inverse_order(update_blocks):
    targets = update_blocks[0]
    count = targets.shape[0]
    hits = targets[:, None] == jnp.arange(count)[None, :]
    return jnp.sum(jnp.where(hits, jnp.arange(count)[:, None], 0), axis=0)


def two_section_shards(leaf_factor, leaf_rhs, update_panel, update_blocks, parent_factor, parent_rhs):
    section = lax.axis_index("rows")
    precision = lax.Precision.HIGH
    leaf_solution = two_section_leaf(leaf_factor, leaf_rhs, section, precision)
    blocks = update_panel.reshape(-1, ROW_BLOCK, update_panel.shape[1])
    order = inverse_order(update_blocks)
    per_section = blocks.shape[0] // 2

    def section_panel(rows_of):
        chosen = lax.dynamic_slice_in_dim(order, rows_of * per_section, per_section)
        taken = jnp.zeros((per_section,) + blocks.shape[1:], blocks.dtype)
        for candidate in range(blocks.shape[0]):
            hit = (chosen == candidate)[:, None, None]
            taken = jnp.where(hit, blocks[candidate][None], taken)
        return taken.reshape(-1, update_panel.shape[1])

    other_rows = matmul(section_panel(1 - section), leaf_solution, precision)
    arrived_rows = pair_swap(other_rows, "rows")
    own_rows = matmul(section_panel(section), leaf_solution, precision)
    own_rows, arrived_rows = lax.optimization_barrier((own_rows, arrived_rows))
    chip_sum = own_rows + arrived_rows
    column_half = parent_rhs.shape[1]
    sibling = lax.axis_index("leaf") % 2
    kept = lax.dynamic_slice_in_dim(chip_sum, sibling * column_half, column_half, 1)
    sent = lax.dynamic_slice_in_dim(chip_sum, (1 - sibling) * column_half, column_half, 1)
    tile_rows = parent_rhs.shape[0]
    diagonal = lax.dynamic_slice_in_dim(parent_factor, section * tile_rows, tile_rows, 1)
    coupling = lower_coupling(parent_factor, diagonal, section, precision)
    arrived = swapped(sent, "leaf", 0)
    arrived, coupling = lax.optimization_barrier((arrived, coupling))
    pending = parent_rhs - (kept + arrived)
    first = matmul(diagonal, pending, precision)
    arrived = pair_swap(first, "rows")
    parent_solution = first - matmul(coupling, arrived, precision)
    return (leaf_solution, parent_solution)


def shards(leaf_factor, leaf_rhs, update_panel, update_blocks, parent_factor, parent_rhs):
    sections = lax.axis_size("rows")
    if sections == 2:
        return two_section_shards(leaf_factor, leaf_rhs, update_panel, update_blocks, parent_factor, parent_rhs)
    section = lax.axis_index("rows")
    leaf_solution = front_forward(leaf_factor, leaf_rhs, section, sections, leaf_pass)
    panel_product = matmul(update_panel, leaf_solution)
    columns = panel_product.shape[1]
    pieces = panel_product.reshape(-1, ROW_BLOCK, columns)
    placed = jnp.zeros_like(pieces).at[update_blocks[0]].set(pieces).reshape(panel_product.shape)
    column_half = parent_rhs.shape[1]
    sibling = lax.axis_index("leaf") % 2
    kept_half, sent_half = split_halves(placed, sibling, column_half)
    arrived = swapped(sent_half, "leaf", 0)
    update_sum = lax.psum_scatter(kept_half + arrived, "rows", scatter_dimension=0, tiled=True)
    pending = parent_rhs - update_sum
    parent_solution = front_forward(parent_factor, pending, section, sections, parent_pass)
    return (leaf_solution, parent_solution)


def solution(mesh):
    placed = (
        P(("leaf", "rows"), None),
        P(("leaf", "rows"), None),
        P("leaf", "rows"),
        P("leaf", None),
        P(("leaf", "rows"), None),
        P(("leaf", "rows"), None),
    )
    return jax.shard_map(
        shards,
        mesh=mesh,
        in_specs=placed,
        out_specs=(P(("leaf", "rows"), None), P(("leaf", "rows"), None)),
        check_vma=False,
    )
```

```python
import jax
import jax.numpy as jnp
from jax import lax
from jax.sharding import PartitionSpec as P

ROW_BLOCK = 128


def passed_along(array, axis, by):
    size = lax.axis_size(axis)
    pairs = [(i, i + by) for i in range(size) if 0 <= i + by < size]
    return lax.ppermute(array, axis, pairs)


def swapped(block, axis, apart):
    count = lax.axis_size(axis)
    route = []
    for low in range(count):
        high = low | 1 << apart
        if high != low and high < count:
            route += [(low, high), (high, low)]
    return lax.ppermute(block, axis, route)


def matmul(left, right, precision=lax.Precision.HIGHEST):
    return jnp.dot(left, right, precision=precision, preferred_element_type=jnp.float32)


def leaf_pass(outgoing):
    return passed_along(outgoing, "rows", 1)


def parent_pass(outgoing):
    return passed_along(outgoing, "rows", 1)


def front_forward(factor, right_side, section, sections, pass_tile):
    tile_rows = right_side.shape[0]

    def advance(tick, state):
        pending, solution, incoming = state
        source = tick - section
        useful = jnp.logical_and(source >= 0, source < section)
        safe_source = jnp.clip(source, 0, sections - 1)

        def apply_tile(values):
            factor_tile = lax.dynamic_slice_in_dim(factor, safe_source * tile_rows, tile_rows, 1)
            return values - matmul(factor_tile, incoming)

        pending = lax.cond(useful, apply_tile, lambda values: values, pending)
        own_turn = tick == 2 * section

        def solve_own(values):
            diagonal_tile = lax.dynamic_slice_in_dim(factor, section * tile_rows, tile_rows, 1)
            return matmul(diagonal_tile, values)

        solution = lax.cond(own_turn, solve_own, lambda values: solution, pending)
        outgoing = jnp.where(
            own_turn, solution, jnp.where(useful, incoming, jnp.zeros_like(incoming))
        )
        incoming = pass_tile(outgoing)
        return (pending, solution, incoming)

    initial = (right_side, jnp.zeros_like(right_side), jnp.zeros_like(right_side))
    return lax.fori_loop(0, 2 * sections - 1, advance, initial)[1]


def split_halves(values, sibling, column_half):
    lower_half = values[:, :column_half]
    upper_half = values[:, column_half:]
    kept_half = jnp.where(sibling == 0, lower_half, upper_half)
    sent_half = jnp.where(sibling == 0, upper_half, lower_half)
    return (kept_half, sent_half)


def pair_swap(block, axis):
    return lax.ppermute(block, axis, [(0, 1), (1, 0)])


def lower_coupling(factor, diagonal, section, precision):
    tile_rows = diagonal.shape[0]
    below = jnp.where(section > 0, factor[:, :tile_rows], jnp.zeros_like(diagonal))
    return matmul(diagonal, below, precision)


def two_section_leaf(factor, right_side, section, precision):
    tile_rows = right_side.shape[0]
    diagonal = lax.dynamic_slice_in_dim(factor, section * tile_rows, tile_rows, 1)
    first = matmul(diagonal, right_side, precision)
    arrived = pair_swap(first, "rows")
    below = jnp.where(section > 0, factor[:, :tile_rows], jnp.zeros_like(diagonal))
    return matmul(diagonal, right_side - matmul(below, arrived, precision), precision)


def inverse_order(update_blocks):
    targets = update_blocks[0]
    count = targets.shape[0]
    hits = targets[:, None] == jnp.arange(count)[None, :]
    return jnp.sum(jnp.where(hits, jnp.arange(count)[:, None], 0), axis=0)


def two_section_shards(leaf_factor, leaf_rhs, update_panel, update_blocks, parent_factor, parent_rhs):
    section = lax.axis_index("rows")
    precision = lax.Precision.HIGH
    leaf_solution = two_section_leaf(leaf_factor, leaf_rhs, section, precision)
    blocks = update_panel.reshape(-1, ROW_BLOCK, update_panel.shape[1])
    order = inverse_order(update_blocks)
    per_section = blocks.shape[0] // 2

    def section_panel(rows_of):
        chosen = lax.dynamic_slice_in_dim(order, rows_of * per_section, per_section)
        taken = jnp.take(blocks, chosen, axis=0, mode="clip")
        return taken.reshape(-1, update_panel.shape[1])

    column_half = parent_rhs.shape[1]
    sibling = lax.axis_index("leaf") % 2
    solution_kept = lax.dynamic_slice_in_dim(leaf_solution, sibling * column_half, column_half, 1)
    solution_sent = lax.dynamic_slice_in_dim(leaf_solution, (1 - sibling) * column_half, column_half, 1)
    panel_other = section_panel(1 - section)
    panel_own = section_panel(section)
    other_sent = matmul(panel_other, solution_sent, precision)
    arrived_sent = pair_swap(other_sent, "rows")
    own_sent = matmul(panel_own, solution_sent, precision)
    own_sent, arrived_sent = lax.optimization_barrier((own_sent, arrived_sent))
    sent = own_sent + arrived_sent
    sent, solution_kept = lax.optimization_barrier((sent, solution_kept))
    other_kept = matmul(panel_other, solution_kept, precision)
    arrived_kept = pair_swap(other_kept, "rows")
    kept = matmul(panel_own, solution_kept, precision) + arrived_kept
    tile_rows = parent_rhs.shape[0]
    diagonal = lax.dynamic_slice_in_dim(parent_factor, section * tile_rows, tile_rows, 1)
    coupling = lower_coupling(parent_factor, diagonal, section, precision)
    arrived = swapped(sent, "leaf", 0)
    arrived, coupling, kept = lax.optimization_barrier((arrived, coupling, kept))
    pending = parent_rhs - (kept + arrived)
    first = matmul(diagonal, pending, precision)
    arrived = pair_swap(first, "rows")
    parent_solution = first - matmul(coupling, arrived, precision)
    return (leaf_solution, parent_solution)


def shards(leaf_factor, leaf_rhs, update_panel, update_blocks, parent_factor, parent_rhs):
    sections = lax.axis_size("rows")
    if sections == 2:
        return two_section_shards(leaf_factor, leaf_rhs, update_panel, update_blocks, parent_factor, parent_rhs)
    section = lax.axis_index("rows")
    leaf_solution = front_forward(leaf_factor, leaf_rhs, section, sections, leaf_pass)
    panel_product = matmul(update_panel, leaf_solution)
    columns = panel_product.shape[1]
    pieces = panel_product.reshape(-1, ROW_BLOCK, columns)
    placed = jnp.zeros_like(pieces).at[update_blocks[0]].set(pieces).reshape(panel_product.shape)
    column_half = parent_rhs.shape[1]
    sibling = lax.axis_index("leaf") % 2
    kept_half, sent_half = split_halves(placed, sibling, column_half)
    arrived = swapped(sent_half, "leaf", 0)
    update_sum = lax.psum_scatter(kept_half + arrived, "rows", scatter_dimension=0, tiled=True)
    pending = parent_rhs - update_sum
    parent_solution = front_forward(parent_factor, pending, section, sections, parent_pass)
    return (leaf_solution, parent_solution)


def solution(mesh):
    placed = (
        P(("leaf", "rows"), None),
        P(("leaf", "rows"), None),
        P("leaf", "rows"),
        P("leaf", None),
        P(("leaf", "rows"), None),
        P(("leaf", "rows"), None),
    )
    return jax.shard_map(
        shards,
        mesh=mesh,
        in_specs=placed,
        out_specs=(P(("leaf", "rows"), None), P(("leaf", "rows"), None)),
        check_vma=False,
    )
```

```python
import jax
import jax.numpy as jnp
from jax import lax
from jax.sharding import PartitionSpec as P

ROW_BLOCK = 128


def passed_along(array, axis, by):
    size = lax.axis_size(axis)
    pairs = [(i, i + by) for i in range(size) if 0 <= i + by < size]
    return lax.ppermute(array, axis, pairs)


def swapped(block, axis, apart):
    count = lax.axis_size(axis)
    route = []
    for low in range(count):
        high = low | 1 << apart
        if high != low and high < count:
            route += [(low, high), (high, low)]
    return lax.ppermute(block, axis, route)


def matmul(left, right, precision=lax.Precision.HIGHEST):
    return jnp.dot(left, right, precision=precision, preferred_element_type=jnp.float32)


def leaf_pass(outgoing):
    return passed_along(outgoing, "rows", 1)


def parent_pass(outgoing):
    return passed_along(outgoing, "rows", 1)


def front_forward(factor, right_side, section, sections, pass_tile):
    tile_rows = right_side.shape[0]

    def advance(tick, state):
        pending, solution, incoming = state
        source = tick - section
        useful = jnp.logical_and(source >= 0, source < section)
        safe_source = jnp.clip(source, 0, sections - 1)

        def apply_tile(values):
            factor_tile = lax.dynamic_slice_in_dim(factor, safe_source * tile_rows, tile_rows, 1)
            return values - matmul(factor_tile, incoming)

        pending = lax.cond(useful, apply_tile, lambda values: values, pending)
        own_turn = tick == 2 * section

        def solve_own(values):
            diagonal_tile = lax.dynamic_slice_in_dim(factor, section * tile_rows, tile_rows, 1)
            return matmul(diagonal_tile, values)

        solution = lax.cond(own_turn, solve_own, lambda values: solution, pending)
        outgoing = jnp.where(
            own_turn, solution, jnp.where(useful, incoming, jnp.zeros_like(incoming))
        )
        incoming = pass_tile(outgoing)
        return (pending, solution, incoming)

    initial = (right_side, jnp.zeros_like(right_side), jnp.zeros_like(right_side))
    return lax.fori_loop(0, 2 * sections - 1, advance, initial)[1]


def split_halves(values, sibling, column_half):
    lower_half = values[:, :column_half]
    upper_half = values[:, column_half:]
    kept_half = jnp.where(sibling == 0, lower_half, upper_half)
    sent_half = jnp.where(sibling == 0, upper_half, lower_half)
    return (kept_half, sent_half)


def pair_swap(block, axis):
    return lax.ppermute(block, axis, [(0, 1), (1, 0)])


def lower_coupling(factor, diagonal, section, precision):
    tile_rows = diagonal.shape[0]
    below = jnp.where(section > 0, factor[:, :tile_rows], jnp.zeros_like(diagonal))
    return matmul(diagonal, below, precision)


def two_section_leaf(factor, right_side, section, precision, early=()):
    tile_rows = right_side.shape[0]
    diagonal = lax.dynamic_slice_in_dim(factor, section * tile_rows, tile_rows, 1)
    first = matmul(diagonal, right_side, precision)
    arrived = pair_swap(first, "rows")
    arrived, early = lax.optimization_barrier((arrived, early))
    below = jnp.where(section > 0, factor[:, :tile_rows], jnp.zeros_like(diagonal))
    return matmul(diagonal, right_side - matmul(below, arrived, precision), precision), early


def inverse_order(update_blocks):
    targets = update_blocks[0]
    count = targets.shape[0]
    hits = targets[:, None] == jnp.arange(count)[None, :]
    return jnp.sum(jnp.where(hits, jnp.arange(count)[:, None], 0), axis=0)


def two_section_shards(leaf_factor, leaf_rhs, update_panel, update_blocks, parent_factor, parent_rhs):
    section = lax.axis_index("rows")
    precision = lax.Precision.HIGH
    blocks = update_panel.reshape(-1, ROW_BLOCK, update_panel.shape[1])
    order = inverse_order(update_blocks)
    per_section = blocks.shape[0] // 2

    def section_panel(rows_of):
        chosen = lax.dynamic_slice_in_dim(order, rows_of * per_section, per_section)
        taken = jnp.take(blocks, chosen, axis=0, mode="clip")
        return taken.reshape(-1, update_panel.shape[1])

    panels = (section_panel(1 - section), section_panel(section))
    leaf_solution, (panel_other, panel_own) = two_section_leaf(leaf_factor, leaf_rhs, section, precision, panels)
    other_rows = matmul(panel_other, leaf_solution, precision)
    arrived_rows = pair_swap(other_rows, "rows")
    own_rows = matmul(panel_own, leaf_solution, precision)
    own_rows, arrived_rows = lax.optimization_barrier((own_rows, arrived_rows))
    chip_sum = own_rows + arrived_rows
    column_half = parent_rhs.shape[1]
    sibling = lax.axis_index("leaf") % 2
    kept = lax.dynamic_slice_in_dim(chip_sum, sibling * column_half, column_half, 1)
    sent = lax.dynamic_slice_in_dim(chip_sum, (1 - sibling) * column_half, column_half, 1)
    tile_rows = parent_rhs.shape[0]
    diagonal = lax.dynamic_slice_in_dim(parent_factor, section * tile_rows, tile_rows, 1)
    coupling = lower_coupling(parent_factor, diagonal, section, precision)
    arrived = swapped(sent, "leaf", 0)
    arrived, coupling = lax.optimization_barrier((arrived, coupling))
    pending = parent_rhs - (kept + arrived)
    first = matmul(diagonal, pending, precision)
    arrived = pair_swap(first, "rows")
    parent_solution = first - matmul(coupling, arrived, precision)
    return (leaf_solution, parent_solution)


def shards(leaf_factor, leaf_rhs, update_panel, update_blocks, parent_factor, parent_rhs):
    sections = lax.axis_size("rows")
    if sections == 2:
        return two_section_shards(leaf_factor, leaf_rhs, update_panel, update_blocks, parent_factor, parent_rhs)
    section = lax.axis_index("rows")
    leaf_solution = front_forward(leaf_factor, leaf_rhs, section, sections, leaf_pass)
    panel_product = matmul(update_panel, leaf_solution)
    columns = panel_product.shape[1]
    pieces = panel_product.reshape(-1, ROW_BLOCK, columns)
    placed = jnp.zeros_like(pieces).at[update_blocks[0]].set(pieces).reshape(panel_product.shape)
    column_half = parent_rhs.shape[1]
    sibling = lax.axis_index("leaf") % 2
    kept_half, sent_half = split_halves(placed, sibling, column_half)
    arrived = swapped(sent_half, "leaf", 0)
    update_sum = lax.psum_scatter(kept_half + arrived, "rows", scatter_dimension=0, tiled=True)
    pending = parent_rhs - update_sum
    parent_solution = front_forward(parent_factor, pending, section, sections, parent_pass)
    return (leaf_solution, parent_solution)


def solution(mesh):
    placed = (
        P(("leaf", "rows"), None),
        P(("leaf", "rows"), None),
        P("leaf", "rows"),
        P("leaf", None),
        P(("leaf", "rows"), None),
        P(("leaf", "rows"), None),
    )
    return jax.shard_map(
        shards,
        mesh=mesh,
        in_specs=placed,
        out_specs=(P(("leaf", "rows"), None), P(("leaf", "rows"), None)),
        check_vma=False,
    )
```

```python
import jax
import jax.numpy as jnp
from jax import lax
from jax.sharding import PartitionSpec as P

ROW_BLOCK = 128


def passed_along(array, axis, by):
    size = lax.axis_size(axis)
    pairs = [(i, i + by) for i in range(size) if 0 <= i + by < size]
    return lax.ppermute(array, axis, pairs)


def swapped(block, axis, apart):
    count = lax.axis_size(axis)
    route = []
    for low in range(count):
        high = low | 1 << apart
        if high != low and high < count:
            route += [(low, high), (high, low)]
    return lax.ppermute(block, axis, route)


def matmul(left, right, precision=lax.Precision.HIGHEST):
    return jnp.dot(left, right, precision=precision, preferred_element_type=jnp.float32)


def leaf_pass(outgoing):
    return passed_along(outgoing, "rows", 1)


def parent_pass(outgoing):
    return passed_along(outgoing, "rows", 1)


def front_forward(factor, right_side, section, sections, pass_tile):
    tile_rows = right_side.shape[0]

    def advance(tick, state):
        pending, solution, incoming = state
        source = tick - section
        useful = jnp.logical_and(source >= 0, source < section)
        safe_source = jnp.clip(source, 0, sections - 1)

        def apply_tile(values):
            factor_tile = lax.dynamic_slice_in_dim(factor, safe_source * tile_rows, tile_rows, 1)
            return values - matmul(factor_tile, incoming)

        pending = lax.cond(useful, apply_tile, lambda values: values, pending)
        own_turn = tick == 2 * section

        def solve_own(values):
            diagonal_tile = lax.dynamic_slice_in_dim(factor, section * tile_rows, tile_rows, 1)
            return matmul(diagonal_tile, values)

        solution = lax.cond(own_turn, solve_own, lambda values: solution, pending)
        outgoing = jnp.where(
            own_turn, solution, jnp.where(useful, incoming, jnp.zeros_like(incoming))
        )
        incoming = pass_tile(outgoing)
        return (pending, solution, incoming)

    initial = (right_side, jnp.zeros_like(right_side), jnp.zeros_like(right_side))
    return lax.fori_loop(0, 2 * sections - 1, advance, initial)[1]


def split_halves(values, sibling, column_half):
    lower_half = values[:, :column_half]
    upper_half = values[:, column_half:]
    kept_half = jnp.where(sibling == 0, lower_half, upper_half)
    sent_half = jnp.where(sibling == 0, upper_half, lower_half)
    return (kept_half, sent_half)


def pair_swap(block, axis):
    return lax.ppermute(block, axis, [(0, 1), (1, 0)])


def lower_coupling(factor, diagonal, section, precision):
    tile_rows = diagonal.shape[0]
    below = jnp.where(section > 0, factor[:, :tile_rows], jnp.zeros_like(diagonal))
    return matmul(diagonal, below, precision)


def two_section_leaf(factor, right_side, section, precision, early=()):
    tile_rows = right_side.shape[0]
    diagonal = lax.dynamic_slice_in_dim(factor, section * tile_rows, tile_rows, 1)
    first = matmul(diagonal, right_side, precision)
    arrived = pair_swap(first, "rows")
    arrived, early = lax.optimization_barrier((arrived, early))
    below = jnp.where(section > 0, factor[:, :tile_rows], jnp.zeros_like(diagonal))
    return matmul(diagonal, right_side - matmul(below, arrived, precision), precision), early


def inverse_order(update_blocks):
    targets = update_blocks[0]
    count = targets.shape[0]
    hits = targets[:, None] == jnp.arange(count)[None, :]
    return jnp.sum(jnp.where(hits, jnp.arange(count)[:, None], 0), axis=0)


def two_section_shards(leaf_factor, leaf_rhs, update_panel, update_blocks, parent_factor, parent_rhs):
    section = lax.axis_index("rows")
    precision = lax.Precision.HIGH
    blocks = update_panel.reshape(-1, ROW_BLOCK, update_panel.shape[1])
    order = inverse_order(update_blocks)

    placed_panel = jnp.take(blocks, order, axis=0, mode="clip").reshape(update_panel.shape)
    placed_panel = two_section_leaf(leaf_factor, leaf_rhs, section, precision, placed_panel)
    leaf_solution, placed_panel = placed_panel
    rows_half = placed_panel.shape[0] // 2
    panel_other = lax.dynamic_slice_in_dim(placed_panel, (1 - section) * rows_half, rows_half, 0)
    panel_own = lax.dynamic_slice_in_dim(placed_panel, section * rows_half, rows_half, 0)
    other_rows = matmul(panel_other, leaf_solution, precision)
    arrived_rows = pair_swap(other_rows, "rows")
    own_rows = matmul(panel_own, leaf_solution, precision)
    own_rows, arrived_rows = lax.optimization_barrier((own_rows, arrived_rows))
    chip_sum = own_rows + arrived_rows
    column_half = parent_rhs.shape[1]
    sibling = lax.axis_index("leaf") % 2
    kept = lax.dynamic_slice_in_dim(chip_sum, sibling * column_half, column_half, 1)
    sent = lax.dynamic_slice_in_dim(chip_sum, (1 - sibling) * column_half, column_half, 1)
    tile_rows = parent_rhs.shape[0]
    diagonal = lax.dynamic_slice_in_dim(parent_factor, section * tile_rows, tile_rows, 1)
    coupling = lower_coupling(parent_factor, diagonal, section, precision)
    arrived = swapped(sent, "leaf", 0)
    arrived, coupling = lax.optimization_barrier((arrived, coupling))
    pending = parent_rhs - (kept + arrived)
    first = matmul(diagonal, pending, precision)
    arrived = pair_swap(first, "rows")
    parent_solution = first - matmul(coupling, arrived, precision)
    return (leaf_solution, parent_solution)


def shards(leaf_factor, leaf_rhs, update_panel, update_blocks, parent_factor, parent_rhs):
    sections = lax.axis_size("rows")
    if sections == 2:
        return two_section_shards(leaf_factor, leaf_rhs, update_panel, update_blocks, parent_factor, parent_rhs)
    section = lax.axis_index("rows")
    leaf_solution = front_forward(leaf_factor, leaf_rhs, section, sections, leaf_pass)
    panel_product = matmul(update_panel, leaf_solution)
    columns = panel_product.shape[1]
    pieces = panel_product.reshape(-1, ROW_BLOCK, columns)
    placed = jnp.zeros_like(pieces).at[update_blocks[0]].set(pieces).reshape(panel_product.shape)
    column_half = parent_rhs.shape[1]
    sibling = lax.axis_index("leaf") % 2
    kept_half, sent_half = split_halves(placed, sibling, column_half)
    arrived = swapped(sent_half, "leaf", 0)
    update_sum = lax.psum_scatter(kept_half + arrived, "rows", scatter_dimension=0, tiled=True)
    pending = parent_rhs - update_sum
    parent_solution = front_forward(parent_factor, pending, section, sections, parent_pass)
    return (leaf_solution, parent_solution)


def solution(mesh):
    placed = (
        P(("leaf", "rows"), None),
        P(("leaf", "rows"), None),
        P("leaf", "rows"),
        P("leaf", None),
        P(("leaf", "rows"), None),
        P(("leaf", "rows"), None),
    )
    return jax.shard_map(
        shards,
        mesh=mesh,
        in_specs=placed,
        out_specs=(P(("leaf", "rows"), None), P(("leaf", "rows"), None)),
        check_vma=False,
    )
```

```python
import jax
import jax.numpy as jnp
from jax import lax
from jax.sharding import PartitionSpec as P

ROW_BLOCK = 128


def passed_along(array, axis, by):
    size = lax.axis_size(axis)
    pairs = [(i, i + by) for i in range(size) if 0 <= i + by < size]
    return lax.ppermute(array, axis, pairs)


def swapped(block, axis, apart):
    count = lax.axis_size(axis)
    route = []
    for low in range(count):
        high = low | 1 << apart
        if high != low and high < count:
            route += [(low, high), (high, low)]
    return lax.ppermute(block, axis, route)


def matmul(left, right, precision=lax.Precision.HIGHEST):
    return jnp.dot(left, right, precision=precision, preferred_element_type=jnp.float32)


def leaf_pass(outgoing):
    return passed_along(outgoing, "rows", 1)


def parent_pass(outgoing):
    return passed_along(outgoing, "rows", 1)


def front_forward(factor, right_side, section, sections, pass_tile):
    tile_rows = right_side.shape[0]

    def advance(tick, state):
        pending, solution, incoming = state
        source = tick - section
        useful = jnp.logical_and(source >= 0, source < section)
        safe_source = jnp.clip(source, 0, sections - 1)

        def apply_tile(values):
            factor_tile = lax.dynamic_slice_in_dim(factor, safe_source * tile_rows, tile_rows, 1)
            return values - matmul(factor_tile, incoming)

        pending = lax.cond(useful, apply_tile, lambda values: values, pending)
        own_turn = tick == 2 * section

        def solve_own(values):
            diagonal_tile = lax.dynamic_slice_in_dim(factor, section * tile_rows, tile_rows, 1)
            return matmul(diagonal_tile, values)

        solution = lax.cond(own_turn, solve_own, lambda values: solution, pending)
        outgoing = jnp.where(
            own_turn, solution, jnp.where(useful, incoming, jnp.zeros_like(incoming))
        )
        incoming = pass_tile(outgoing)
        return (pending, solution, incoming)

    initial = (right_side, jnp.zeros_like(right_side), jnp.zeros_like(right_side))
    return lax.fori_loop(0, 2 * sections - 1, advance, initial)[1]


def split_halves(values, sibling, column_half):
    lower_half = values[:, :column_half]
    upper_half = values[:, column_half:]
    kept_half = jnp.where(sibling == 0, lower_half, upper_half)
    sent_half = jnp.where(sibling == 0, upper_half, lower_half)
    return (kept_half, sent_half)


def pair_swap(block, axis):
    return lax.ppermute(block, axis, [(0, 1), (1, 0)])


def lower_coupling(factor, diagonal, section, precision):
    tile_rows = diagonal.shape[0]
    below = jnp.where(section > 0, factor[:, :tile_rows], jnp.zeros_like(diagonal))
    return matmul(diagonal, below, precision)


def two_section_leaf(factor, right_side, section, precision, early=()):
    tile_rows = right_side.shape[0]
    diagonal = lax.dynamic_slice_in_dim(factor, section * tile_rows, tile_rows, 1)
    first = matmul(diagonal, right_side, precision)
    arrived = pair_swap(first, "rows")
    arrived, early = lax.optimization_barrier((arrived, early))
    below = jnp.where(section > 0, factor[:, :tile_rows], jnp.zeros_like(diagonal))
    return matmul(diagonal, right_side - matmul(below, arrived, precision), precision), early


def inverse_order(update_blocks):
    targets = update_blocks[0]
    count = targets.shape[0]
    hits = targets[:, None] == jnp.arange(count)[None, :]
    return jnp.sum(jnp.where(hits, jnp.arange(count)[:, None], 0), axis=0)


def two_section_shards(leaf_factor, leaf_rhs, update_panel, update_blocks, parent_factor, parent_rhs):
    section = lax.axis_index("rows")
    precision = lax.Precision.HIGH
    blocks = update_panel.reshape(-1, ROW_BLOCK, update_panel.shape[1])
    order = inverse_order(update_blocks)

    placed_panel = jnp.take(blocks, order, axis=0, mode="clip").reshape(update_panel.shape)
    placed_panel = two_section_leaf(leaf_factor, leaf_rhs, section, precision, placed_panel)
    leaf_solution, placed_panel = placed_panel
    rows_half = placed_panel.shape[0] // 2
    panel_other = lax.dynamic_slice_in_dim(placed_panel, (1 - section) * rows_half, rows_half, 0)
    panel_own = lax.dynamic_slice_in_dim(placed_panel, section * rows_half, rows_half, 0)
    other_rows = matmul(panel_other, leaf_solution, precision)
    arrived_rows = pair_swap(other_rows, "rows")
    own_rows = matmul(panel_own, leaf_solution, precision)
    own_rows, arrived_rows = lax.optimization_barrier((own_rows, arrived_rows))
    column_half = parent_rhs.shape[1]
    sibling = lax.axis_index("leaf") % 2

    def column_sum(half):
        own_part = lax.dynamic_slice_in_dim(own_rows, half * column_half, column_half, 1)
        arrived_part = lax.dynamic_slice_in_dim(arrived_rows, half * column_half, column_half, 1)
        return own_part + arrived_part

    sent = column_sum(1 - sibling)
    sent, own_rows, arrived_rows = lax.optimization_barrier((sent, own_rows, arrived_rows))
    kept = column_sum(sibling)
    tile_rows = parent_rhs.shape[0]
    diagonal = lax.dynamic_slice_in_dim(parent_factor, section * tile_rows, tile_rows, 1)
    coupling = lower_coupling(parent_factor, diagonal, section, precision)
    arrived = swapped(sent, "leaf", 0)
    arrived, coupling, kept = lax.optimization_barrier((arrived, coupling, kept))
    pending = parent_rhs - (kept + arrived)
    first = matmul(diagonal, pending, precision)
    arrived = pair_swap(first, "rows")
    parent_solution = first - matmul(coupling, arrived, precision)
    return (leaf_solution, parent_solution)


def shards(leaf_factor, leaf_rhs, update_panel, update_blocks, parent_factor, parent_rhs):
    sections = lax.axis_size("rows")
    if sections == 2:
        return two_section_shards(leaf_factor, leaf_rhs, update_panel, update_blocks, parent_factor, parent_rhs)
    section = lax.axis_index("rows")
    leaf_solution = front_forward(leaf_factor, leaf_rhs, section, sections, leaf_pass)
    panel_product = matmul(update_panel, leaf_solution)
    columns = panel_product.shape[1]
    pieces = panel_product.reshape(-1, ROW_BLOCK, columns)
    placed = jnp.zeros_like(pieces).at[update_blocks[0]].set(pieces).reshape(panel_product.shape)
    column_half = parent_rhs.shape[1]
    sibling = lax.axis_index("leaf") % 2
    kept_half, sent_half = split_halves(placed, sibling, column_half)
    arrived = swapped(sent_half, "leaf", 0)
    update_sum = lax.psum_scatter(kept_half + arrived, "rows", scatter_dimension=0, tiled=True)
    pending = parent_rhs - update_sum
    parent_solution = front_forward(parent_factor, pending, section, sections, parent_pass)
    return (leaf_solution, parent_solution)


def solution(mesh):
    placed = (
        P(("leaf", "rows"), None),
        P(("leaf", "rows"), None),
        P("leaf", "rows"),
        P("leaf", None),
        P(("leaf", "rows"), None),
        P(("leaf", "rows"), None),
    )
    return jax.shard_map(
        shards,
        mesh=mesh,
        in_specs=placed,
        out_specs=(P(("leaf", "rows"), None), P(("leaf", "rows"), None)),
        check_vma=False,
    )
```

```python
import jax
import jax.numpy as jnp
from jax import lax
from jax.sharding import PartitionSpec as P

ROW_BLOCK = 128


def passed_along(array, axis, by):
    size = lax.axis_size(axis)
    pairs = [(i, i + by) for i in range(size) if 0 <= i + by < size]
    return lax.ppermute(array, axis, pairs)


def swapped(block, axis, apart):
    count = lax.axis_size(axis)
    route = []
    for low in range(count):
        high = low | 1 << apart
        if high != low and high < count:
            route += [(low, high), (high, low)]
    return lax.ppermute(block, axis, route)


def matmul(left, right, precision=lax.Precision.HIGHEST):
    return jnp.dot(left, right, precision=precision, preferred_element_type=jnp.float32)


def leaf_pass(outgoing):
    return passed_along(outgoing, "rows", 1)


def parent_pass(outgoing):
    return passed_along(outgoing, "rows", 1)


def front_forward(factor, right_side, section, sections, pass_tile):
    tile_rows = right_side.shape[0]

    def advance(tick, state):
        pending, solution, incoming = state
        source = tick - section
        useful = jnp.logical_and(source >= 0, source < section)
        safe_source = jnp.clip(source, 0, sections - 1)

        def apply_tile(values):
            factor_tile = lax.dynamic_slice_in_dim(factor, safe_source * tile_rows, tile_rows, 1)
            return values - matmul(factor_tile, incoming)

        pending = lax.cond(useful, apply_tile, lambda values: values, pending)
        own_turn = tick == 2 * section

        def solve_own(values):
            diagonal_tile = lax.dynamic_slice_in_dim(factor, section * tile_rows, tile_rows, 1)
            return matmul(diagonal_tile, values)

        solution = lax.cond(own_turn, solve_own, lambda values: solution, pending)
        outgoing = jnp.where(
            own_turn, solution, jnp.where(useful, incoming, jnp.zeros_like(incoming))
        )
        incoming = pass_tile(outgoing)
        return (pending, solution, incoming)

    initial = (right_side, jnp.zeros_like(right_side), jnp.zeros_like(right_side))
    return lax.fori_loop(0, 2 * sections - 1, advance, initial)[1]


def split_halves(values, sibling, column_half):
    lower_half = values[:, :column_half]
    upper_half = values[:, column_half:]
    kept_half = jnp.where(sibling == 0, lower_half, upper_half)
    sent_half = jnp.where(sibling == 0, upper_half, lower_half)
    return (kept_half, sent_half)


def pair_swap(block, axis):
    return lax.ppermute(block, axis, [(0, 1), (1, 0)])


def lower_coupling(factor, diagonal, section, precision):
    tile_rows = diagonal.shape[0]
    below = jnp.where(section > 0, factor[:, :tile_rows], jnp.zeros_like(diagonal))
    return matmul(diagonal, below, precision)


def two_section_leaf(factor, right_side, section, precision, early=()):
    tile_rows = right_side.shape[0]
    diagonal = lax.dynamic_slice_in_dim(factor, section * tile_rows, tile_rows, 1)
    first = matmul(diagonal, right_side, precision)
    arrived = pair_swap(first, "rows")
    arrived, early = lax.optimization_barrier((arrived, early))
    below = jnp.where(section > 0, factor[:, :tile_rows], jnp.zeros_like(diagonal))
    return matmul(diagonal, right_side - matmul(below, arrived, precision), precision), early


def inverse_order(update_blocks):
    targets = update_blocks[0]
    count = targets.shape[0]
    hits = targets[:, None] == jnp.arange(count)[None, :]
    return jnp.sum(jnp.where(hits, jnp.arange(count)[:, None], 0), axis=0)


def two_section_shards(leaf_factor, leaf_rhs, update_panel, update_blocks, parent_factor, parent_rhs):
    section = lax.axis_index("rows")
    precision = lax.Precision.HIGH
    blocks = update_panel.reshape(-1, ROW_BLOCK, update_panel.shape[1])
    order = inverse_order(update_blocks)

    placed_panel = jnp.take(blocks, order, axis=0, mode="clip").reshape(update_panel.shape)
    placed_panel = two_section_leaf(leaf_factor, leaf_rhs, section, precision, placed_panel)
    leaf_solution, placed_panel = placed_panel
    rows_half = placed_panel.shape[0] // 2
    panel_other = lax.dynamic_slice_in_dim(placed_panel, (1 - section) * rows_half, rows_half, 0)
    panel_own = lax.dynamic_slice_in_dim(placed_panel, section * rows_half, rows_half, 0)
    other_rows = matmul(panel_other, leaf_solution, precision)
    arrived_rows = pair_swap(other_rows, "rows")
    own_rows = matmul(panel_own, leaf_solution, precision)
    own_rows, arrived_rows = lax.optimization_barrier((own_rows, arrived_rows))
    column_half = parent_rhs.shape[1]
    sibling = lax.axis_index("leaf") % 2

    def column_sum(half):
        own_part = lax.dynamic_slice_in_dim(own_rows, half * column_half, column_half, 1)
        arrived_part = lax.dynamic_slice_in_dim(arrived_rows, half * column_half, column_half, 1)
        return own_part + arrived_part

    sent = column_sum(1 - sibling)
    sent, own_rows, arrived_rows = lax.optimization_barrier((sent, own_rows, arrived_rows))
    kept = column_sum(sibling)
    tile_rows = parent_rhs.shape[0]
    diagonal = lax.dynamic_slice_in_dim(parent_factor, section * tile_rows, tile_rows, 1)
    coupling = lower_coupling(parent_factor, diagonal, section, precision)
    arrived = swapped(sent, "leaf", 0)
    arrived, coupling, kept = lax.optimization_barrier((arrived, coupling, kept))
    pending = parent_rhs - (kept + arrived)
    first = matmul(diagonal, pending, precision)
    arrived = pair_swap(first, "rows")
    correction = lax.optimization_barrier(matmul(coupling, arrived, precision))
    parent_solution = first - correction
    return (leaf_solution, parent_solution)


def shards(leaf_factor, leaf_rhs, update_panel, update_blocks, parent_factor, parent_rhs):
    sections = lax.axis_size("rows")
    if sections == 2:
        return two_section_shards(leaf_factor, leaf_rhs, update_panel, update_blocks, parent_factor, parent_rhs)
    section = lax.axis_index("rows")
    leaf_solution = front_forward(leaf_factor, leaf_rhs, section, sections, leaf_pass)
    panel_product = matmul(update_panel, leaf_solution)
    columns = panel_product.shape[1]
    pieces = panel_product.reshape(-1, ROW_BLOCK, columns)
    placed = jnp.zeros_like(pieces).at[update_blocks[0]].set(pieces).reshape(panel_product.shape)
    column_half = parent_rhs.shape[1]
    sibling = lax.axis_index("leaf") % 2
    kept_half, sent_half = split_halves(placed, sibling, column_half)
    arrived = swapped(sent_half, "leaf", 0)
    update_sum = lax.psum_scatter(kept_half + arrived, "rows", scatter_dimension=0, tiled=True)
    pending = parent_rhs - update_sum
    parent_solution = front_forward(parent_factor, pending, section, sections, parent_pass)
    return (leaf_solution, parent_solution)


def solution(mesh):
    placed = (
        P(("leaf", "rows"), None),
        P(("leaf", "rows"), None),
        P("leaf", "rows"),
        P("leaf", None),
        P(("leaf", "rows"), None),
        P(("leaf", "rows"), None),
    )
    return jax.shard_map(
        shards,
        mesh=mesh,
        in_specs=placed,
        out_specs=(P(("leaf", "rows"), None), P(("leaf", "rows"), None)),
        check_vma=False,
    )
```

```python
import jax
import jax.numpy as jnp
from jax import lax
from jax.sharding import PartitionSpec as P

ROW_BLOCK = 128


def passed_along(array, axis, by):
    size = lax.axis_size(axis)
    pairs = [(i, i + by) for i in range(size) if 0 <= i + by < size]
    return lax.ppermute(array, axis, pairs)


def swapped(block, axis, apart):
    count = lax.axis_size(axis)
    route = []
    for low in range(count):
        high = low | 1 << apart
        if high != low and high < count:
            route += [(low, high), (high, low)]
    return lax.ppermute(block, axis, route)


def matmul(left, right, precision=lax.Precision.HIGHEST):
    return jnp.dot(left, right, precision=precision, preferred_element_type=jnp.float32)


def leaf_pass(outgoing):
    return passed_along(outgoing, "rows", 1)


def parent_pass(outgoing):
    return passed_along(outgoing, "rows", 1)


def front_forward(factor, right_side, section, sections, pass_tile):
    tile_rows = right_side.shape[0]

    def advance(tick, state):
        pending, solution, incoming = state
        source = tick - section
        useful = jnp.logical_and(source >= 0, source < section)
        safe_source = jnp.clip(source, 0, sections - 1)

        def apply_tile(values):
            factor_tile = lax.dynamic_slice_in_dim(factor, safe_source * tile_rows, tile_rows, 1)
            return values - matmul(factor_tile, incoming)

        pending = lax.cond(useful, apply_tile, lambda values: values, pending)
        own_turn = tick == 2 * section

        def solve_own(values):
            diagonal_tile = lax.dynamic_slice_in_dim(factor, section * tile_rows, tile_rows, 1)
            return matmul(diagonal_tile, values)

        solution = lax.cond(own_turn, solve_own, lambda values: solution, pending)
        outgoing = jnp.where(
            own_turn, solution, jnp.where(useful, incoming, jnp.zeros_like(incoming))
        )
        incoming = pass_tile(outgoing)
        return (pending, solution, incoming)

    initial = (right_side, jnp.zeros_like(right_side), jnp.zeros_like(right_side))
    return lax.fori_loop(0, 2 * sections - 1, advance, initial)[1]


def split_halves(values, sibling, column_half):
    lower_half = values[:, :column_half]
    upper_half = values[:, column_half:]
    kept_half = jnp.where(sibling == 0, lower_half, upper_half)
    sent_half = jnp.where(sibling == 0, upper_half, lower_half)
    return (kept_half, sent_half)


def pair_swap(block, axis):
    return lax.ppermute(block, axis, [(0, 1), (1, 0)])


def lower_coupling(factor, diagonal, section, precision):
    tile_rows = diagonal.shape[0]
    below = jnp.where(section > 0, factor[:, :tile_rows], jnp.zeros_like(diagonal))
    return matmul(diagonal, below, precision)


def two_section_leaf(factor, right_side, section, precision, early=()):
    tile_rows = right_side.shape[0]
    diagonal = lax.dynamic_slice_in_dim(factor, section * tile_rows, tile_rows, 1)
    first = matmul(diagonal, right_side, precision)
    arrived = pair_swap(first, "rows")
    below = jnp.where(section > 0, factor[:, :tile_rows], jnp.zeros_like(diagonal))
    arrived, below, early = lax.optimization_barrier((arrived, below, early))
    return matmul(diagonal, right_side - matmul(below, arrived, precision), precision), early


def inverse_order(update_blocks):
    targets = update_blocks[0]
    count = targets.shape[0]
    hits = targets[:, None] == jnp.arange(count)[None, :]
    return jnp.sum(jnp.where(hits, jnp.arange(count)[:, None], 0), axis=0)


def two_section_shards(leaf_factor, leaf_rhs, update_panel, update_blocks, parent_factor, parent_rhs):
    section = lax.axis_index("rows")
    precision = lax.Precision.HIGH
    blocks = update_panel.reshape(-1, ROW_BLOCK, update_panel.shape[1])
    order = inverse_order(update_blocks)

    placed_panel = jnp.take(blocks, order, axis=0, mode="clip").reshape(update_panel.shape)
    placed_panel = two_section_leaf(leaf_factor, leaf_rhs, section, precision, placed_panel)
    leaf_solution, placed_panel = placed_panel
    rows_half = placed_panel.shape[0] // 2
    panel_other = lax.dynamic_slice_in_dim(placed_panel, (1 - section) * rows_half, rows_half, 0)
    panel_own = lax.dynamic_slice_in_dim(placed_panel, section * rows_half, rows_half, 0)
    other_rows = matmul(panel_other, leaf_solution, precision)
    arrived_rows = pair_swap(other_rows, "rows")
    own_rows = matmul(panel_own, leaf_solution, precision)
    own_rows, arrived_rows = lax.optimization_barrier((own_rows, arrived_rows))
    column_half = parent_rhs.shape[1]
    sibling = lax.axis_index("leaf") % 2

    def column_sum(half):
        own_part = lax.dynamic_slice_in_dim(own_rows, half * column_half, column_half, 1)
        arrived_part = lax.dynamic_slice_in_dim(arrived_rows, half * column_half, column_half, 1)
        return own_part + arrived_part

    sent = column_sum(1 - sibling)
    sent, own_rows, arrived_rows = lax.optimization_barrier((sent, own_rows, arrived_rows))
    kept = column_sum(sibling)
    tile_rows = parent_rhs.shape[0]
    diagonal = lax.dynamic_slice_in_dim(parent_factor, section * tile_rows, tile_rows, 1)
    coupling = lower_coupling(parent_factor, diagonal, section, precision)
    arrived = swapped(sent, "leaf", 0)
    arrived, coupling, kept = lax.optimization_barrier((arrived, coupling, kept))
    pending = parent_rhs - (kept + arrived)
    first = matmul(diagonal, pending, precision)
    arrived = pair_swap(first, "rows")
    parent_solution = first - matmul(coupling, arrived, precision)
    return (leaf_solution, parent_solution)


def shards(leaf_factor, leaf_rhs, update_panel, update_blocks, parent_factor, parent_rhs):
    sections = lax.axis_size("rows")
    if sections == 2:
        return two_section_shards(leaf_factor, leaf_rhs, update_panel, update_blocks, parent_factor, parent_rhs)
    section = lax.axis_index("rows")
    leaf_solution = front_forward(leaf_factor, leaf_rhs, section, sections, leaf_pass)
    panel_product = matmul(update_panel, leaf_solution)
    columns = panel_product.shape[1]
    pieces = panel_product.reshape(-1, ROW_BLOCK, columns)
    placed = jnp.zeros_like(pieces).at[update_blocks[0]].set(pieces).reshape(panel_product.shape)
    column_half = parent_rhs.shape[1]
    sibling = lax.axis_index("leaf") % 2
    kept_half, sent_half = split_halves(placed, sibling, column_half)
    arrived = swapped(sent_half, "leaf", 0)
    update_sum = lax.psum_scatter(kept_half + arrived, "rows", scatter_dimension=0, tiled=True)
    pending = parent_rhs - update_sum
    parent_solution = front_forward(parent_factor, pending, section, sections, parent_pass)
    return (leaf_solution, parent_solution)


def solution(mesh):
    placed = (
        P(("leaf", "rows"), None),
        P(("leaf", "rows"), None),
        P("leaf", "rows"),
        P("leaf", None),
        P(("leaf", "rows"), None),
        P(("leaf", "rows"), None),
    )
    return jax.shard_map(
        shards,
        mesh=mesh,
        in_specs=placed,
        out_specs=(P(("leaf", "rows"), None), P(("leaf", "rows"), None)),
        check_vma=False,
    )
```

```python
import jax
import jax.numpy as jnp
from jax import lax
from jax.sharding import PartitionSpec as P

ROW_BLOCK = 128


def passed_along(array, axis, by):
    size = lax.axis_size(axis)
    pairs = [(i, i + by) for i in range(size) if 0 <= i + by < size]
    return lax.ppermute(array, axis, pairs)


def swapped(block, axis, apart):
    count = lax.axis_size(axis)
    route = []
    for low in range(count):
        high = low | 1 << apart
        if high != low and high < count:
            route += [(low, high), (high, low)]
    return lax.ppermute(block, axis, route)


def matmul(left, right, precision=lax.Precision.HIGHEST):
    return jnp.dot(left, right, precision=precision, preferred_element_type=jnp.float32)


def leaf_pass(outgoing):
    return passed_along(outgoing, "rows", 1)


def parent_pass(outgoing):
    return passed_along(outgoing, "rows", 1)


def front_forward(factor, right_side, section, sections, pass_tile):
    tile_rows = right_side.shape[0]

    def advance(tick, state):
        pending, solution, incoming = state
        source = tick - section
        useful = jnp.logical_and(source >= 0, source < section)
        safe_source = jnp.clip(source, 0, sections - 1)

        def apply_tile(values):
            factor_tile = lax.dynamic_slice_in_dim(factor, safe_source * tile_rows, tile_rows, 1)
            return values - matmul(factor_tile, incoming)

        pending = lax.cond(useful, apply_tile, lambda values: values, pending)
        own_turn = tick == 2 * section

        def solve_own(values):
            diagonal_tile = lax.dynamic_slice_in_dim(factor, section * tile_rows, tile_rows, 1)
            return matmul(diagonal_tile, values)

        solution = lax.cond(own_turn, solve_own, lambda values: solution, pending)
        outgoing = jnp.where(
            own_turn, solution, jnp.where(useful, incoming, jnp.zeros_like(incoming))
        )
        incoming = pass_tile(outgoing)
        return (pending, solution, incoming)

    initial = (right_side, jnp.zeros_like(right_side), jnp.zeros_like(right_side))
    return lax.fori_loop(0, 2 * sections - 1, advance, initial)[1]


def split_halves(values, sibling, column_half):
    lower_half = values[:, :column_half]
    upper_half = values[:, column_half:]
    kept_half = jnp.where(sibling == 0, lower_half, upper_half)
    sent_half = jnp.where(sibling == 0, upper_half, lower_half)
    return (kept_half, sent_half)


def pair_swap(block, axis):
    return lax.ppermute(block, axis, [(0, 1), (1, 0)])


def lower_coupling(factor, diagonal, section, precision):
    tile_rows = diagonal.shape[0]
    below = jnp.where(section > 0, factor[:, :tile_rows], jnp.zeros_like(diagonal))
    return matmul(diagonal, below, precision)


def two_section_leaf(factor, right_side, section, precision, early=()):
    tile_rows = right_side.shape[0]
    diagonal = lax.dynamic_slice_in_dim(factor, section * tile_rows, tile_rows, 1)
    first = matmul(diagonal, right_side, precision)
    arrived = pair_swap(first, "rows")
    arrived, early = lax.optimization_barrier((arrived, early))
    below = jnp.where(section > 0, factor[:, :tile_rows], jnp.zeros_like(diagonal))
    return matmul(diagonal, right_side - matmul(below, arrived, precision), precision), early


def inverse_order(update_blocks):
    targets = update_blocks[0]
    count = targets.shape[0]
    hits = targets[:, None] == jnp.arange(count)[None, :]
    return jnp.sum(jnp.where(hits, jnp.arange(count)[:, None], 0), axis=0)


def two_section_shards(leaf_factor, leaf_rhs, update_panel, update_blocks, parent_factor, parent_rhs):
    section = lax.axis_index("rows")
    precision = lax.Precision.HIGH
    blocks = update_panel.reshape(-1, ROW_BLOCK, update_panel.shape[1])
    order = inverse_order(update_blocks)

    placed_panel = jnp.take(blocks, order, axis=0, mode="clip").reshape(update_panel.shape)
    placed_panel = two_section_leaf(leaf_factor, leaf_rhs, section, precision, placed_panel)
    leaf_solution, placed_panel = placed_panel
    rows_half = placed_panel.shape[0] // 2
    panel_other = lax.dynamic_slice_in_dim(placed_panel, (1 - section) * rows_half, rows_half, 0)
    panel_own = lax.dynamic_slice_in_dim(placed_panel, section * rows_half, rows_half, 0)
    column_half = parent_rhs.shape[1]
    sibling = lax.axis_index("leaf") % 2
    solution_kept = lax.dynamic_slice_in_dim(leaf_solution, sibling * column_half, column_half, 1)
    solution_sent = lax.dynamic_slice_in_dim(leaf_solution, (1 - sibling) * column_half, column_half, 1)
    other_sent = matmul(panel_other, solution_sent, precision)
    arrived_sent = pair_swap(other_sent, "rows")
    own_sent = matmul(panel_own, solution_sent, precision)
    own_sent, arrived_sent = lax.optimization_barrier((own_sent, arrived_sent))
    sent = own_sent + arrived_sent
    sent, solution_kept = lax.optimization_barrier((sent, solution_kept))
    other_kept = matmul(panel_other, solution_kept, precision)
    arrived_kept = pair_swap(other_kept, "rows")
    kept = matmul(panel_own, solution_kept, precision) + arrived_kept
    tile_rows = parent_rhs.shape[0]
    diagonal = lax.dynamic_slice_in_dim(parent_factor, section * tile_rows, tile_rows, 1)
    coupling = lower_coupling(parent_factor, diagonal, section, precision)
    arrived = swapped(sent, "leaf", 0)
    arrived, kept = lax.optimization_barrier((arrived, kept))
    pending = parent_rhs - (kept + arrived)
    first = matmul(diagonal, pending, precision)
    arrived = pair_swap(first, "rows")
    arrived, coupling = lax.optimization_barrier((arrived, coupling))
    parent_solution = first - matmul(coupling, arrived, precision)
    return (leaf_solution, parent_solution)


def shards(leaf_factor, leaf_rhs, update_panel, update_blocks, parent_factor, parent_rhs):
    sections = lax.axis_size("rows")
    if sections == 2:
        return two_section_shards(leaf_factor, leaf_rhs, update_panel, update_blocks, parent_factor, parent_rhs)
    section = lax.axis_index("rows")
    leaf_solution = front_forward(leaf_factor, leaf_rhs, section, sections, leaf_pass)
    panel_product = matmul(update_panel, leaf_solution)
    columns = panel_product.shape[1]
    pieces = panel_product.reshape(-1, ROW_BLOCK, columns)
    placed = jnp.zeros_like(pieces).at[update_blocks[0]].set(pieces).reshape(panel_product.shape)
    column_half = parent_rhs.shape[1]
    sibling = lax.axis_index("leaf") % 2
    kept_half, sent_half = split_halves(placed, sibling, column_half)
    arrived = swapped(sent_half, "leaf", 0)
    update_sum = lax.psum_scatter(kept_half + arrived, "rows", scatter_dimension=0, tiled=True)
    pending = parent_rhs - update_sum
    parent_solution = front_forward(parent_factor, pending, section, sections, parent_pass)
    return (leaf_solution, parent_solution)


def solution(mesh):
    placed = (
        P(("leaf", "rows"), None),
        P(("leaf", "rows"), None),
        P("leaf", "rows"),
        P("leaf", None),
        P(("leaf", "rows"), None),
        P(("leaf", "rows"), None),
    )
    return jax.shard_map(
        shards,
        mesh=mesh,
        in_specs=placed,
        out_specs=(P(("leaf", "rows"), None), P(("leaf", "rows"), None)),
        check_vma=False,
    )
```

```python
import jax
import jax.numpy as jnp
from jax import lax
from jax.sharding import PartitionSpec as P

ROW_BLOCK = 128


def passed_along(array, axis, by):
    size = lax.axis_size(axis)
    pairs = [(i, i + by) for i in range(size) if 0 <= i + by < size]
    return lax.ppermute(array, axis, pairs)


def swapped(block, axis, apart):
    count = lax.axis_size(axis)
    route = []
    for low in range(count):
        high = low | 1 << apart
        if high != low and high < count:
            route += [(low, high), (high, low)]
    return lax.ppermute(block, axis, route)


def matmul(left, right, precision=lax.Precision.HIGHEST):
    return jnp.dot(left, right, precision=precision, preferred_element_type=jnp.float32)


def leaf_pass(outgoing):
    return passed_along(outgoing, "rows", 1)


def parent_pass(outgoing):
    return passed_along(outgoing, "rows", 1)


def front_forward(factor, right_side, section, sections, pass_tile):
    tile_rows = right_side.shape[0]

    def advance(tick, state):
        pending, solution, incoming = state
        source = tick - section
        useful = jnp.logical_and(source >= 0, source < section)
        safe_source = jnp.clip(source, 0, sections - 1)

        def apply_tile(values):
            factor_tile = lax.dynamic_slice_in_dim(factor, safe_source * tile_rows, tile_rows, 1)
            return values - matmul(factor_tile, incoming)

        pending = lax.cond(useful, apply_tile, lambda values: values, pending)
        own_turn = tick == 2 * section

        def solve_own(values):
            diagonal_tile = lax.dynamic_slice_in_dim(factor, section * tile_rows, tile_rows, 1)
            return matmul(diagonal_tile, values)

        solution = lax.cond(own_turn, solve_own, lambda values: solution, pending)
        outgoing = jnp.where(
            own_turn, solution, jnp.where(useful, incoming, jnp.zeros_like(incoming))
        )
        incoming = pass_tile(outgoing)
        return (pending, solution, incoming)

    initial = (right_side, jnp.zeros_like(right_side), jnp.zeros_like(right_side))
    return lax.fori_loop(0, 2 * sections - 1, advance, initial)[1]


def split_halves(values, sibling, column_half):
    lower_half = values[:, :column_half]
    upper_half = values[:, column_half:]
    kept_half = jnp.where(sibling == 0, lower_half, upper_half)
    sent_half = jnp.where(sibling == 0, upper_half, lower_half)
    return (kept_half, sent_half)


def pair_swap(block, axis):
    return lax.ppermute(block, axis, [(0, 1), (1, 0)])


def lower_coupling(factor, diagonal, section, precision):
    tile_rows = diagonal.shape[0]
    below = jnp.where(section > 0, factor[:, :tile_rows], jnp.zeros_like(diagonal))
    return matmul(diagonal, below, precision)


def two_section_leaf(factor, right_side, section, precision, early=()):
    tile_rows = right_side.shape[0]
    diagonal = lax.dynamic_slice_in_dim(factor, section * tile_rows, tile_rows, 1)
    first = matmul(diagonal, right_side, precision)
    arrived = pair_swap(first, "rows")
    arrived, early = lax.optimization_barrier((arrived, early))
    below = jnp.where(section > 0, factor[:, :tile_rows], jnp.zeros_like(diagonal))
    return matmul(diagonal, right_side - matmul(below, arrived, precision), precision), early


def inverse_order(update_blocks):
    targets = update_blocks[0]
    count = targets.shape[0]
    hits = targets[:, None] == jnp.arange(count)[None, :]
    return jnp.sum(jnp.where(hits, jnp.arange(count)[:, None], 0), axis=0)


def two_section_shards(leaf_factor, leaf_rhs, update_panel, update_blocks, parent_factor, parent_rhs):
    section = lax.axis_index("rows")
    precision = lax.Precision.HIGH
    blocks = update_panel.reshape(-1, ROW_BLOCK, update_panel.shape[1])
    order = inverse_order(update_blocks)

    placed_panel = jnp.take(blocks, order, axis=0, mode="clip").reshape(update_panel.shape)
    placed_panel = two_section_leaf(leaf_factor, leaf_rhs, section, precision, placed_panel)
    leaf_solution, placed_panel = placed_panel
    rows_half = placed_panel.shape[0] // 2
    panel_other = lax.dynamic_slice_in_dim(placed_panel, (1 - section) * rows_half, rows_half, 0)
    panel_own = lax.dynamic_slice_in_dim(placed_panel, section * rows_half, rows_half, 0)
    other_rows = matmul(panel_other, leaf_solution, precision)
    arrived_rows = pair_swap(other_rows, "rows")
    own_rows = matmul(panel_own, leaf_solution, precision)
    own_rows, arrived_rows = lax.optimization_barrier((own_rows, arrived_rows))
    column_half = parent_rhs.shape[1]
    sibling = lax.axis_index("leaf") % 2

    def column_sum(half):
        own_part = lax.dynamic_slice_in_dim(own_rows, half * column_half, column_half, 1)
        arrived_part = lax.dynamic_slice_in_dim(arrived_rows, half * column_half, column_half, 1)
        return own_part + arrived_part

    sent = column_sum(1 - sibling)
    sent, own_rows, arrived_rows = lax.optimization_barrier((sent, own_rows, arrived_rows))
    kept = column_sum(sibling)
    tile_rows = parent_rhs.shape[0]
    diagonal = lax.dynamic_slice_in_dim(parent_factor, section * tile_rows, tile_rows, 1)
    coupling = lower_coupling(parent_factor, diagonal, section, precision)
    arrived = swapped(sent, "leaf", 0)
    arrived, kept = lax.optimization_barrier((arrived, kept))
    pending = parent_rhs - (kept + arrived)
    first = matmul(diagonal, pending, precision)
    arrived = pair_swap(first, "rows")
    arrived, coupling = lax.optimization_barrier((arrived, coupling))
    parent_solution = first - matmul(coupling, arrived, precision)
    return (leaf_solution, parent_solution)


def shards(leaf_factor, leaf_rhs, update_panel, update_blocks, parent_factor, parent_rhs):
    sections = lax.axis_size("rows")
    if sections == 2:
        return two_section_shards(leaf_factor, leaf_rhs, update_panel, update_blocks, parent_factor, parent_rhs)
    section = lax.axis_index("rows")
    leaf_solution = front_forward(leaf_factor, leaf_rhs, section, sections, leaf_pass)
    panel_product = matmul(update_panel, leaf_solution)
    columns = panel_product.shape[1]
    pieces = panel_product.reshape(-1, ROW_BLOCK, columns)
    placed = jnp.zeros_like(pieces).at[update_blocks[0]].set(pieces).reshape(panel_product.shape)
    column_half = parent_rhs.shape[1]
    sibling = lax.axis_index("leaf") % 2
    kept_half, sent_half = split_halves(placed, sibling, column_half)
    arrived = swapped(sent_half, "leaf", 0)
    update_sum = lax.psum_scatter(kept_half + arrived, "rows", scatter_dimension=0, tiled=True)
    pending = parent_rhs - update_sum
    parent_solution = front_forward(parent_factor, pending, section, sections, parent_pass)
    return (leaf_solution, parent_solution)


def solution(mesh):
    placed = (
        P(("leaf", "rows"), None),
        P(("leaf", "rows"), None),
        P("leaf", "rows"),
        P("leaf", None),
        P(("leaf", "rows"), None),
        P(("leaf", "rows"), None),
    )
    return jax.shard_map(
        shards,
        mesh=mesh,
        in_specs=placed,
        out_specs=(P(("leaf", "rows"), None), P(("leaf", "rows"), None)),
        check_vma=False,
    )
```

```python
import jax
import jax.numpy as jnp
from jax import lax
from jax.sharding import PartitionSpec as P

ROW_BLOCK = 128


def passed_along(array, axis, by):
    size = lax.axis_size(axis)
    pairs = [(i, i + by) for i in range(size) if 0 <= i + by < size]
    return lax.ppermute(array, axis, pairs)


def swapped(block, axis, apart):
    count = lax.axis_size(axis)
    route = []
    for low in range(count):
        high = low | 1 << apart
        if high != low and high < count:
            route += [(low, high), (high, low)]
    return lax.ppermute(block, axis, route)


def matmul(left, right, precision=lax.Precision.HIGHEST):
    return jnp.dot(left, right, precision=precision, preferred_element_type=jnp.float32)


def leaf_pass(outgoing):
    return passed_along(outgoing, "rows", 1)


def parent_pass(outgoing):
    return passed_along(outgoing, "rows", 1)


def front_forward(factor, right_side, section, sections, pass_tile):
    tile_rows = right_side.shape[0]

    def advance(tick, state):
        pending, solution, incoming = state
        source = tick - section
        useful = jnp.logical_and(source >= 0, source < section)
        safe_source = jnp.clip(source, 0, sections - 1)

        def apply_tile(values):
            factor_tile = lax.dynamic_slice_in_dim(factor, safe_source * tile_rows, tile_rows, 1)
            return values - matmul(factor_tile, incoming)

        pending = lax.cond(useful, apply_tile, lambda values: values, pending)
        own_turn = tick == 2 * section

        def solve_own(values):
            diagonal_tile = lax.dynamic_slice_in_dim(factor, section * tile_rows, tile_rows, 1)
            return matmul(diagonal_tile, values)

        solution = lax.cond(own_turn, solve_own, lambda values: solution, pending)
        outgoing = jnp.where(
            own_turn, solution, jnp.where(useful, incoming, jnp.zeros_like(incoming))
        )
        incoming = pass_tile(outgoing)
        return (pending, solution, incoming)

    initial = (right_side, jnp.zeros_like(right_side), jnp.zeros_like(right_side))
    return lax.fori_loop(0, 2 * sections - 1, advance, initial)[1]


def split_halves(values, sibling, column_half):
    lower_half = values[:, :column_half]
    upper_half = values[:, column_half:]
    kept_half = jnp.where(sibling == 0, lower_half, upper_half)
    sent_half = jnp.where(sibling == 0, upper_half, lower_half)
    return (kept_half, sent_half)


def pair_swap(block, axis):
    return lax.ppermute(block, axis, [(0, 1), (1, 0)])


def lower_coupling(factor, diagonal, section, precision):
    tile_rows = diagonal.shape[0]
    below = jnp.where(section > 0, factor[:, :tile_rows], jnp.zeros_like(diagonal))
    return matmul(diagonal, below, precision)


def two_section_leaf(factor, right_side, section, precision, early=()):
    tile_rows = right_side.shape[0]
    diagonal = lax.dynamic_slice_in_dim(factor, section * tile_rows, tile_rows, 1)
    first = matmul(diagonal, right_side, precision)
    arrived = pair_swap(first, "rows")
    arrived, early = lax.optimization_barrier((arrived, early))
    below = jnp.where(section > 0, factor[:, :tile_rows], jnp.zeros_like(diagonal))
    return matmul(diagonal, right_side - matmul(below, arrived, precision), precision), early


def inverse_order(update_blocks):
    targets = update_blocks[0]
    count = targets.shape[0]
    hits = targets[:, None] == jnp.arange(count)[None, :]
    return jnp.sum(jnp.where(hits, jnp.arange(count)[:, None], 0), axis=0)


def two_section_shards(leaf_factor, leaf_rhs, update_panel, update_blocks, parent_factor, parent_rhs):
    section = lax.axis_index("rows")
    precision = lax.Precision.HIGH
    blocks = update_panel.reshape(-1, ROW_BLOCK, update_panel.shape[1])
    order = inverse_order(update_blocks)

    placed_panel = jnp.take(blocks, order, axis=0, mode="clip").reshape(update_panel.shape)
    placed_panel = two_section_leaf(leaf_factor, leaf_rhs, section, precision, placed_panel)
    leaf_solution, placed_panel = placed_panel
    rows_half = placed_panel.shape[0] // 2
    panel_other = lax.dynamic_slice_in_dim(placed_panel, (1 - section) * rows_half, rows_half, 0)
    panel_own = lax.dynamic_slice_in_dim(placed_panel, section * rows_half, rows_half, 0)
    column_half = parent_rhs.shape[1]
    sibling = lax.axis_index("leaf") % 2
    solution_kept = lax.dynamic_slice_in_dim(leaf_solution, sibling * column_half, column_half, 1)
    solution_sent = lax.dynamic_slice_in_dim(leaf_solution, (1 - sibling) * column_half, column_half, 1)
    other_sent = matmul(panel_other, solution_sent, precision)
    arrived_sent = pair_swap(other_sent, "rows")
    other_kept = matmul(panel_other, solution_kept, precision)
    solution_sent, other_kept = lax.optimization_barrier((solution_sent, other_kept))
    arrived_kept = pair_swap(other_kept, "rows")
    own_sent = matmul(panel_own, solution_sent, precision)
    own_sent, arrived_sent = lax.optimization_barrier((own_sent, arrived_sent))
    sent = own_sent + arrived_sent
    sent, solution_kept = lax.optimization_barrier((sent, solution_kept))
    kept = matmul(panel_own, solution_kept, precision) + arrived_kept
    tile_rows = parent_rhs.shape[0]
    diagonal = lax.dynamic_slice_in_dim(parent_factor, section * tile_rows, tile_rows, 1)
    coupling = lower_coupling(parent_factor, diagonal, section, precision)
    arrived = swapped(sent, "leaf", 0)
    arrived, kept = lax.optimization_barrier((arrived, kept))
    pending = parent_rhs - (kept + arrived)
    first = matmul(diagonal, pending, precision)
    arrived = pair_swap(first, "rows")
    arrived, coupling = lax.optimization_barrier((arrived, coupling))
    parent_solution = first - matmul(coupling, arrived, precision)
    return (leaf_solution, parent_solution)


def shards(leaf_factor, leaf_rhs, update_panel, update_blocks, parent_factor, parent_rhs):
    sections = lax.axis_size("rows")
    if sections == 2:
        return two_section_shards(leaf_factor, leaf_rhs, update_panel, update_blocks, parent_factor, parent_rhs)
    section = lax.axis_index("rows")
    leaf_solution = front_forward(leaf_factor, leaf_rhs, section, sections, leaf_pass)
    panel_product = matmul(update_panel, leaf_solution)
    columns = panel_product.shape[1]
    pieces = panel_product.reshape(-1, ROW_BLOCK, columns)
    placed = jnp.zeros_like(pieces).at[update_blocks[0]].set(pieces).reshape(panel_product.shape)
    column_half = parent_rhs.shape[1]
    sibling = lax.axis_index("leaf") % 2
    kept_half, sent_half = split_halves(placed, sibling, column_half)
    arrived = swapped(sent_half, "leaf", 0)
    update_sum = lax.psum_scatter(kept_half + arrived, "rows", scatter_dimension=0, tiled=True)
    pending = parent_rhs - update_sum
    parent_solution = front_forward(parent_factor, pending, section, sections, parent_pass)
    return (leaf_solution, parent_solution)


def solution(mesh):
    placed = (
        P(("leaf", "rows"), None),
        P(("leaf", "rows"), None),
        P("leaf", "rows"),
        P("leaf", None),
        P(("leaf", "rows"), None),
        P(("leaf", "rows"), None),
    )
    return jax.shard_map(
        shards,
        mesh=mesh,
        in_specs=placed,
        out_specs=(P(("leaf", "rows"), None), P(("leaf", "rows"), None)),
        check_vma=False,
    )
```

```python
import jax
import jax.numpy as jnp
from jax import lax
from jax.sharding import PartitionSpec as P

ROW_BLOCK = 128


def passed_along(array, axis, by):
    size = lax.axis_size(axis)
    pairs = [(i, i + by) for i in range(size) if 0 <= i + by < size]
    return lax.ppermute(array, axis, pairs)


def swapped(block, axis, apart):
    count = lax.axis_size(axis)
    route = []
    for low in range(count):
        high = low | 1 << apart
        if high != low and high < count:
            route += [(low, high), (high, low)]
    return lax.ppermute(block, axis, route)


def matmul(left, right, precision=lax.Precision.HIGHEST):
    return jnp.dot(left, right, precision=precision, preferred_element_type=jnp.float32)


def leaf_pass(outgoing):
    return passed_along(outgoing, "rows", 1)


def parent_pass(outgoing):
    return passed_along(outgoing, "rows", 1)


def front_forward(factor, right_side, section, sections, pass_tile):
    tile_rows = right_side.shape[0]

    def advance(tick, state):
        pending, solution, incoming = state
        source = tick - section
        useful = jnp.logical_and(source >= 0, source < section)
        safe_source = jnp.clip(source, 0, sections - 1)

        def apply_tile(values):
            factor_tile = lax.dynamic_slice_in_dim(factor, safe_source * tile_rows, tile_rows, 1)
            return values - matmul(factor_tile, incoming)

        pending = lax.cond(useful, apply_tile, lambda values: values, pending)
        own_turn = tick == 2 * section

        def solve_own(values):
            diagonal_tile = lax.dynamic_slice_in_dim(factor, section * tile_rows, tile_rows, 1)
            return matmul(diagonal_tile, values)

        solution = lax.cond(own_turn, solve_own, lambda values: solution, pending)
        outgoing = jnp.where(
            own_turn, solution, jnp.where(useful, incoming, jnp.zeros_like(incoming))
        )
        incoming = pass_tile(outgoing)
        return (pending, solution, incoming)

    initial = (right_side, jnp.zeros_like(right_side), jnp.zeros_like(right_side))
    return lax.fori_loop(0, 2 * sections - 1, advance, initial)[1]


def split_halves(values, sibling, column_half):
    lower_half = values[:, :column_half]
    upper_half = values[:, column_half:]
    kept_half = jnp.where(sibling == 0, lower_half, upper_half)
    sent_half = jnp.where(sibling == 0, upper_half, lower_half)
    return (kept_half, sent_half)


def pair_swap(block, axis):
    return lax.ppermute(block, axis, [(0, 1), (1, 0)])


def lower_coupling(factor, diagonal, section, precision):
    tile_rows = diagonal.shape[0]
    below = jnp.where(section > 0, factor[:, :tile_rows], jnp.zeros_like(diagonal))
    return matmul(diagonal, below, precision)


def two_section_leaf(factor, right_side, section, precision, early=()):
    tile_rows = right_side.shape[0]
    diagonal = lax.dynamic_slice_in_dim(factor, section * tile_rows, tile_rows, 1)
    first = matmul(diagonal, right_side, precision)
    arrived = pair_swap(first, "rows")
    arrived, early = lax.optimization_barrier((arrived, early))
    below = jnp.where(section > 0, factor[:, :tile_rows], jnp.zeros_like(diagonal))
    return matmul(diagonal, right_side - matmul(below, arrived, precision), precision), early


def inverse_order(update_blocks):
    targets = update_blocks[0]
    count = targets.shape[0]
    hits = targets[:, None] == jnp.arange(count)[None, :]
    return jnp.sum(jnp.where(hits, jnp.arange(count)[:, None], 0), axis=0)


def two_section_shards(leaf_factor, leaf_rhs, update_panel, update_blocks, parent_factor, parent_rhs):
    section = lax.axis_index("rows")
    precision = lax.Precision.HIGH
    blocks = update_panel.reshape(-1, ROW_BLOCK, update_panel.shape[1])
    order = inverse_order(update_blocks)

    placed_panel = jnp.take(blocks, order, axis=0, mode="clip").reshape(update_panel.shape)
    placed_panel = two_section_leaf(leaf_factor, leaf_rhs, section, precision, placed_panel)
    leaf_solution, placed_panel = placed_panel
    rows_half = placed_panel.shape[0] // 2
    panel_other = lax.dynamic_slice_in_dim(placed_panel, (1 - section) * rows_half, rows_half, 0)
    panel_own = lax.dynamic_slice_in_dim(placed_panel, section * rows_half, rows_half, 0)
    column_half = parent_rhs.shape[1]
    sibling = lax.axis_index("leaf") % 2
    solution_kept = lax.dynamic_slice_in_dim(leaf_solution, sibling * column_half, column_half, 1)
    solution_sent = lax.dynamic_slice_in_dim(leaf_solution, (1 - sibling) * column_half, column_half, 1)
    other_sent = matmul(panel_other, solution_sent, precision)
    arrived_sent = pair_swap(other_sent, "rows")
    other_kept = matmul(panel_other, solution_kept, precision)
    solution_sent, other_kept = lax.optimization_barrier((solution_sent, other_kept))
    arrived_kept = pair_swap(other_kept, "rows")
    own_sent = matmul(panel_own, solution_sent, precision)
    own_sent, arrived_sent = lax.optimization_barrier((own_sent, arrived_sent))
    sent = own_sent + arrived_sent
    sent, solution_kept, arrived_kept = lax.optimization_barrier((sent, solution_kept, arrived_kept))
    kept = matmul(panel_own, solution_kept, precision) + arrived_kept
    tile_rows = parent_rhs.shape[0]
    diagonal = lax.dynamic_slice_in_dim(parent_factor, section * tile_rows, tile_rows, 1)
    coupling = lower_coupling(parent_factor, diagonal, section, precision)
    arrived = swapped(sent, "leaf", 0)
    arrived, kept = lax.optimization_barrier((arrived, kept))
    pending = parent_rhs - (kept + arrived)
    first = matmul(diagonal, pending, precision)
    arrived = pair_swap(first, "rows")
    arrived, coupling = lax.optimization_barrier((arrived, coupling))
    parent_solution = first - matmul(coupling, arrived, precision)
    return (leaf_solution, parent_solution)


def shards(leaf_factor, leaf_rhs, update_panel, update_blocks, parent_factor, parent_rhs):
    sections = lax.axis_size("rows")
    if sections == 2:
        return two_section_shards(leaf_factor, leaf_rhs, update_panel, update_blocks, parent_factor, parent_rhs)
    section = lax.axis_index("rows")
    leaf_solution = front_forward(leaf_factor, leaf_rhs, section, sections, leaf_pass)
    panel_product = matmul(update_panel, leaf_solution)
    columns = panel_product.shape[1]
    pieces = panel_product.reshape(-1, ROW_BLOCK, columns)
    placed = jnp.zeros_like(pieces).at[update_blocks[0]].set(pieces).reshape(panel_product.shape)
    column_half = parent_rhs.shape[1]
    sibling = lax.axis_index("leaf") % 2
    kept_half, sent_half = split_halves(placed, sibling, column_half)
    arrived = swapped(sent_half, "leaf", 0)
    update_sum = lax.psum_scatter(kept_half + arrived, "rows", scatter_dimension=0, tiled=True)
    pending = parent_rhs - update_sum
    parent_solution = front_forward(parent_factor, pending, section, sections, parent_pass)
    return (leaf_solution, parent_solution)


def solution(mesh):
    placed = (
        P(("leaf", "rows"), None),
        P(("leaf", "rows"), None),
        P("leaf", "rows"),
        P("leaf", None),
        P(("leaf", "rows"), None),
        P(("leaf", "rows"), None),
    )
    return jax.shard_map(
        shards,
        mesh=mesh,
        in_specs=placed,
        out_specs=(P(("leaf", "rows"), None), P(("leaf", "rows"), None)),
        check_vma=False,
    )
```

```python
import jax
import jax.numpy as jnp
from jax import lax
from jax.sharding import PartitionSpec as P

ROW_BLOCK = 128


def passed_along(array, axis, by):
    size = lax.axis_size(axis)
    pairs = [(i, i + by) for i in range(size) if 0 <= i + by < size]
    return lax.ppermute(array, axis, pairs)


def swapped(block, axis, apart):
    count = lax.axis_size(axis)
    route = []
    for low in range(count):
        high = low | 1 << apart
        if high != low and high < count:
            route += [(low, high), (high, low)]
    return lax.ppermute(block, axis, route)


def matmul(left, right, precision=lax.Precision.HIGHEST):
    return jnp.dot(left, right, precision=precision, preferred_element_type=jnp.float32)


def leaf_pass(outgoing):
    return passed_along(outgoing, "rows", 1)


def parent_pass(outgoing):
    return passed_along(outgoing, "rows", 1)


def front_forward(factor, right_side, section, sections, pass_tile):
    tile_rows = right_side.shape[0]

    def advance(tick, state):
        pending, solution, incoming = state
        source = tick - section
        useful = jnp.logical_and(source >= 0, source < section)
        safe_source = jnp.clip(source, 0, sections - 1)

        def apply_tile(values):
            factor_tile = lax.dynamic_slice_in_dim(factor, safe_source * tile_rows, tile_rows, 1)
            return values - matmul(factor_tile, incoming)

        pending = lax.cond(useful, apply_tile, lambda values: values, pending)
        own_turn = tick == 2 * section

        def solve_own(values):
            diagonal_tile = lax.dynamic_slice_in_dim(factor, section * tile_rows, tile_rows, 1)
            return matmul(diagonal_tile, values)

        solution = lax.cond(own_turn, solve_own, lambda values: solution, pending)
        outgoing = jnp.where(
            own_turn, solution, jnp.where(useful, incoming, jnp.zeros_like(incoming))
        )
        incoming = pass_tile(outgoing)
        return (pending, solution, incoming)

    initial = (right_side, jnp.zeros_like(right_side), jnp.zeros_like(right_side))
    return lax.fori_loop(0, 2 * sections - 1, advance, initial)[1]


def split_halves(values, sibling, column_half):
    lower_half = values[:, :column_half]
    upper_half = values[:, column_half:]
    kept_half = jnp.where(sibling == 0, lower_half, upper_half)
    sent_half = jnp.where(sibling == 0, upper_half, lower_half)
    return (kept_half, sent_half)


def pair_swap(block, axis):
    return lax.ppermute(block, axis, [(0, 1), (1, 0)])


def lower_coupling(factor, diagonal, section, precision):
    tile_rows = diagonal.shape[0]
    below = jnp.where(section > 0, factor[:, :tile_rows], jnp.zeros_like(diagonal))
    return matmul(diagonal, below, precision)


def two_section_leaf(factor, right_side, section, precision, early=()):
    tile_rows = right_side.shape[0]
    diagonal = lax.dynamic_slice_in_dim(factor, section * tile_rows, tile_rows, 1)
    first = matmul(diagonal, right_side, precision)
    arrived = pair_swap(first, "rows")
    arrived, early = lax.optimization_barrier((arrived, early))
    below = jnp.where(section > 0, factor[:, :tile_rows], jnp.zeros_like(diagonal))
    return matmul(diagonal, right_side - matmul(below, arrived, precision), precision), early


def inverse_order(update_blocks):
    targets = update_blocks[0]
    count = targets.shape[0]
    hits = targets[:, None] == jnp.arange(count)[None, :]
    return jnp.sum(jnp.where(hits, jnp.arange(count)[:, None], 0), axis=0)


def two_section_shards(leaf_factor, leaf_rhs, update_panel, update_blocks, parent_factor, parent_rhs):
    section = lax.axis_index("rows")
    precision = lax.Precision.HIGH
    blocks = update_panel.reshape(-1, ROW_BLOCK, update_panel.shape[1])
    placed_panel = jnp.take(blocks, inverse_order(update_blocks), axis=0, mode="clip").reshape(update_panel.shape)
    tile_rows = leaf_rhs.shape[0]
    leaf_diagonal = lax.dynamic_slice_in_dim(leaf_factor, section * tile_rows, tile_rows, 1)
    leaf_first = matmul(leaf_diagonal, leaf_rhs, precision)
    leaf_arrived = pair_swap(leaf_first, "rows")
    leaf_arrived, placed_panel = lax.optimization_barrier((leaf_arrived, placed_panel))
    below = jnp.where(section > 0, leaf_factor[:, :tile_rows], jnp.zeros_like(leaf_diagonal))
    column_half = parent_rhs.shape[1]
    sibling = lax.axis_index("leaf") % 2

    def leaf_columns(half, arrived_all):
        rhs_part = lax.dynamic_slice_in_dim(leaf_rhs, half * column_half, column_half, 1)
        arrived_part = lax.dynamic_slice_in_dim(arrived_all, half * column_half, column_half, 1)
        target = rhs_part - matmul(below, arrived_part, precision)
        return matmul(leaf_diagonal, target, precision)

    rows_half = placed_panel.shape[0] // 2
    panel_other = lax.dynamic_slice_in_dim(placed_panel, (1 - section) * rows_half, rows_half, 0)
    panel_own = lax.dynamic_slice_in_dim(placed_panel, section * rows_half, rows_half, 0)
    solution_sent = leaf_columns(1 - sibling, leaf_arrived)
    other_sent = matmul(panel_other, solution_sent, precision)
    arrived_sent = pair_swap(other_sent, "rows")
    own_sent = matmul(panel_own, solution_sent, precision)
    own_sent, arrived_sent = lax.optimization_barrier((own_sent, arrived_sent))
    sent = own_sent + arrived_sent
    sent, leaf_arrived = lax.optimization_barrier((sent, leaf_arrived))
    solution_kept = leaf_columns(sibling, leaf_arrived)
    other_kept = matmul(panel_other, solution_kept, precision)
    arrived_kept = pair_swap(other_kept, "rows")
    kept = matmul(panel_own, solution_kept, precision) + arrived_kept
    leaf_solution = jnp.zeros_like(leaf_rhs)
    leaf_solution = lax.dynamic_update_slice_in_dim(leaf_solution, solution_kept, sibling * column_half, 1)
    leaf_solution = lax.dynamic_update_slice_in_dim(leaf_solution, solution_sent, (1 - sibling) * column_half, 1)
    tile_rows = parent_rhs.shape[0]
    diagonal = lax.dynamic_slice_in_dim(parent_factor, section * tile_rows, tile_rows, 1)
    coupling = lower_coupling(parent_factor, diagonal, section, precision)
    arrived = swapped(sent, "leaf", 0)
    arrived, kept = lax.optimization_barrier((arrived, kept))
    pending = parent_rhs - (kept + arrived)
    first = matmul(diagonal, pending, precision)
    arrived = pair_swap(first, "rows")
    arrived, coupling = lax.optimization_barrier((arrived, coupling))
    parent_solution = first - matmul(coupling, arrived, precision)
    return (leaf_solution, parent_solution)


def shards(leaf_factor, leaf_rhs, update_panel, update_blocks, parent_factor, parent_rhs):
    sections = lax.axis_size("rows")
    if sections == 2 and leaf_rhs.shape[1] == 2 * parent_rhs.shape[1]:
        return two_section_shards(leaf_factor, leaf_rhs, update_panel, update_blocks, parent_factor, parent_rhs)
    section = lax.axis_index("rows")
    leaf_solution = front_forward(leaf_factor, leaf_rhs, section, sections, leaf_pass)
    panel_product = matmul(update_panel, leaf_solution)
    columns = panel_product.shape[1]
    pieces = panel_product.reshape(-1, ROW_BLOCK, columns)
    placed = jnp.zeros_like(pieces).at[update_blocks[0]].set(pieces).reshape(panel_product.shape)
    column_half = parent_rhs.shape[1]
    sibling = lax.axis_index("leaf") % 2
    kept_half, sent_half = split_halves(placed, sibling, column_half)
    arrived = swapped(sent_half, "leaf", 0)
    update_sum = lax.psum_scatter(kept_half + arrived, "rows", scatter_dimension=0, tiled=True)
    pending = parent_rhs - update_sum
    parent_solution = front_forward(parent_factor, pending, section, sections, parent_pass)
    return (leaf_solution, parent_solution)


def solution(mesh):
    placed = (
        P(("leaf", "rows"), None),
        P(("leaf", "rows"), None),
        P("leaf", "rows"),
        P("leaf", None),
        P(("leaf", "rows"), None),
        P(("leaf", "rows"), None),
    )
    return jax.shard_map(
        shards,
        mesh=mesh,
        in_specs=placed,
        out_specs=(P(("leaf", "rows"), None), P(("leaf", "rows"), None)),
        check_vma=False,
    )
```

```python
import jax
import jax.numpy as jnp
from jax import lax
from jax.sharding import PartitionSpec as P

ROW_BLOCK = 128


def passed_along(array, axis, by):
    size = lax.axis_size(axis)
    pairs = [(i, i + by) for i in range(size) if 0 <= i + by < size]
    return lax.ppermute(array, axis, pairs)


def swapped(block, axis, apart):
    count = lax.axis_size(axis)
    route = []
    for low in range(count):
        high = low | 1 << apart
        if high != low and high < count:
            route += [(low, high), (high, low)]
    return lax.ppermute(block, axis, route)


def matmul(left, right, precision=lax.Precision.HIGHEST):
    return jnp.dot(left, right, precision=precision, preferred_element_type=jnp.float32)


def leaf_pass(outgoing):
    return passed_along(outgoing, "rows", 1)


def parent_pass(outgoing):
    return passed_along(outgoing, "rows", 1)


def front_forward(factor, right_side, section, sections, pass_tile):
    tile_rows = right_side.shape[0]

    def advance(tick, state):
        pending, solution, incoming = state
        source = tick - section
        useful = jnp.logical_and(source >= 0, source < section)
        safe_source = jnp.clip(source, 0, sections - 1)

        def apply_tile(values):
            factor_tile = lax.dynamic_slice_in_dim(factor, safe_source * tile_rows, tile_rows, 1)
            return values - matmul(factor_tile, incoming)

        pending = lax.cond(useful, apply_tile, lambda values: values, pending)
        own_turn = tick == 2 * section

        def solve_own(values):
            diagonal_tile = lax.dynamic_slice_in_dim(factor, section * tile_rows, tile_rows, 1)
            return matmul(diagonal_tile, values)

        solution = lax.cond(own_turn, solve_own, lambda values: solution, pending)
        outgoing = jnp.where(
            own_turn, solution, jnp.where(useful, incoming, jnp.zeros_like(incoming))
        )
        incoming = pass_tile(outgoing)
        return (pending, solution, incoming)

    initial = (right_side, jnp.zeros_like(right_side), jnp.zeros_like(right_side))
    return lax.fori_loop(0, 2 * sections - 1, advance, initial)[1]


def split_halves(values, sibling, column_half):
    lower_half = values[:, :column_half]
    upper_half = values[:, column_half:]
    kept_half = jnp.where(sibling == 0, lower_half, upper_half)
    sent_half = jnp.where(sibling == 0, upper_half, lower_half)
    return (kept_half, sent_half)


def pair_swap(block, axis):
    return lax.ppermute(block, axis, [(0, 1), (1, 0)])


def lower_coupling(factor, diagonal, section, precision):
    tile_rows = diagonal.shape[0]
    below = jnp.where(section > 0, factor[:, :tile_rows], jnp.zeros_like(diagonal))
    return matmul(diagonal, below, precision)


def two_section_leaf(factor, right_side, section, precision, early=()):
    tile_rows = right_side.shape[0]
    diagonal = lax.dynamic_slice_in_dim(factor, section * tile_rows, tile_rows, 1)
    first = matmul(diagonal, right_side, precision)
    arrived = pair_swap(first, "rows")
    arrived, early = lax.optimization_barrier((arrived, early))
    below = jnp.where(section > 0, factor[:, :tile_rows], jnp.zeros_like(diagonal))
    return matmul(diagonal, right_side - matmul(below, arrived, precision), precision), early


def inverse_order(update_blocks):
    targets = update_blocks[0]
    count = targets.shape[0]
    hits = targets[:, None] == jnp.arange(count)[None, :]
    return jnp.sum(jnp.where(hits, jnp.arange(count)[:, None], 0), axis=0)


def two_section_shards(leaf_factor, leaf_rhs, update_panel, update_blocks, parent_factor, parent_rhs):
    section = lax.axis_index("rows")
    precision = lax.Precision.HIGH
    blocks = update_panel.reshape(-1, ROW_BLOCK, update_panel.shape[1])
    order = inverse_order(update_blocks)

    placed_panel = jnp.take(blocks, order, axis=0, mode="clip").reshape(update_panel.shape)
    placed_panel = two_section_leaf(leaf_factor, leaf_rhs, section, precision, placed_panel)
    leaf_solution, placed_panel = placed_panel
    rows_half = placed_panel.shape[0] // 2
    panel_other = lax.dynamic_slice_in_dim(placed_panel, (1 - section) * rows_half, rows_half, 0)
    panel_own = lax.dynamic_slice_in_dim(placed_panel, section * rows_half, rows_half, 0)
    column_half = parent_rhs.shape[1]
    sibling = lax.axis_index("leaf") % 2
    solution_kept = lax.dynamic_slice_in_dim(leaf_solution, sibling * column_half, column_half, 1)
    solution_sent = lax.dynamic_slice_in_dim(leaf_solution, (1 - sibling) * column_half, column_half, 1)
    other_sent = matmul(panel_other, solution_sent, precision)
    arrived_sent = pair_swap(other_sent, "rows")
    other_kept = matmul(panel_other, solution_kept, precision)
    solution_sent, other_kept = lax.optimization_barrier((solution_sent, other_kept))
    arrived_kept = pair_swap(other_kept, "rows")
    own_sent = matmul(panel_own, solution_sent, precision)
    own_sent, arrived_sent = lax.optimization_barrier((own_sent, arrived_sent))
    sent = own_sent + arrived_sent
    sent, solution_kept = lax.optimization_barrier((sent, solution_kept))
    kept = matmul(panel_own, solution_kept, precision) + arrived_kept
    tile_rows = parent_rhs.shape[0]
    diagonal = lax.dynamic_slice_in_dim(parent_factor, section * tile_rows, tile_rows, 1)
    coupling = lower_coupling(parent_factor, diagonal, section, precision)
    arrived = swapped(sent, "leaf", 0)
    arrived, kept, coupling = lax.optimization_barrier((arrived, kept, coupling))
    pending = parent_rhs - (kept + arrived)
    half_rows = tile_rows // 2
    first_top = matmul(diagonal[:half_rows], pending, precision)
    arrived_top = pair_swap(first_top, "rows")
    first_bottom = matmul(diagonal[half_rows:], pending, precision)
    arrived_bottom = pair_swap(first_bottom, "rows")
    correction = matmul(coupling[:, :half_rows], arrived_top, precision)
    correction = correction + matmul(coupling[:, half_rows:], arrived_bottom, precision)
    parent_solution = jnp.concatenate([first_top, first_bottom], axis=0) - correction
    return (leaf_solution, parent_solution)


def shards(leaf_factor, leaf_rhs, update_panel, update_blocks, parent_factor, parent_rhs):
    sections = lax.axis_size("rows")
    if sections == 2:
        return two_section_shards(leaf_factor, leaf_rhs, update_panel, update_blocks, parent_factor, parent_rhs)
    section = lax.axis_index("rows")
    leaf_solution = front_forward(leaf_factor, leaf_rhs, section, sections, leaf_pass)
    panel_product = matmul(update_panel, leaf_solution)
    columns = panel_product.shape[1]
    pieces = panel_product.reshape(-1, ROW_BLOCK, columns)
    placed = jnp.zeros_like(pieces).at[update_blocks[0]].set(pieces).reshape(panel_product.shape)
    column_half = parent_rhs.shape[1]
    sibling = lax.axis_index("leaf") % 2
    kept_half, sent_half = split_halves(placed, sibling, column_half)
    arrived = swapped(sent_half, "leaf", 0)
    update_sum = lax.psum_scatter(kept_half + arrived, "rows", scatter_dimension=0, tiled=True)
    pending = parent_rhs - update_sum
    parent_solution = front_forward(parent_factor, pending, section, sections, parent_pass)
    return (leaf_solution, parent_solution)


def solution(mesh):
    placed = (
        P(("leaf", "rows"), None),
        P(("leaf", "rows"), None),
        P("leaf", "rows"),
        P("leaf", None),
        P(("leaf", "rows"), None),
        P(("leaf", "rows"), None),
    )
    return jax.shard_map(
        shards,
        mesh=mesh,
        in_specs=placed,
        out_specs=(P(("leaf", "rows"), None), P(("leaf", "rows"), None)),
        check_vma=False,
    )
```

```python
import jax
import jax.numpy as jnp
from jax import lax
from jax.sharding import PartitionSpec as P

ROW_BLOCK = 128


def passed_along(array, axis, by):
    size = lax.axis_size(axis)
    pairs = [(i, i + by) for i in range(size) if 0 <= i + by < size]
    return lax.ppermute(array, axis, pairs)


def swapped(block, axis, apart):
    count = lax.axis_size(axis)
    route = []
    for low in range(count):
        high = low | 1 << apart
        if high != low and high < count:
            route += [(low, high), (high, low)]
    return lax.ppermute(block, axis, route)


def matmul(left, right, precision=lax.Precision.HIGHEST):
    return jnp.dot(left, right, precision=precision, preferred_element_type=jnp.float32)


def leaf_pass(outgoing):
    return passed_along(outgoing, "rows", 1)


def parent_pass(outgoing):
    return passed_along(outgoing, "rows", 1)


def front_forward(factor, right_side, section, sections, pass_tile):
    tile_rows = right_side.shape[0]

    def advance(tick, state):
        pending, solution, incoming = state
        source = tick - section
        useful = jnp.logical_and(source >= 0, source < section)
        safe_source = jnp.clip(source, 0, sections - 1)

        def apply_tile(values):
            factor_tile = lax.dynamic_slice_in_dim(factor, safe_source * tile_rows, tile_rows, 1)
            return values - matmul(factor_tile, incoming)

        pending = lax.cond(useful, apply_tile, lambda values: values, pending)
        own_turn = tick == 2 * section

        def solve_own(values):
            diagonal_tile = lax.dynamic_slice_in_dim(factor, section * tile_rows, tile_rows, 1)
            return matmul(diagonal_tile, values)

        solution = lax.cond(own_turn, solve_own, lambda values: solution, pending)
        outgoing = jnp.where(
            own_turn, solution, jnp.where(useful, incoming, jnp.zeros_like(incoming))
        )
        incoming = pass_tile(outgoing)
        return (pending, solution, incoming)

    initial = (right_side, jnp.zeros_like(right_side), jnp.zeros_like(right_side))
    return lax.fori_loop(0, 2 * sections - 1, advance, initial)[1]


def split_halves(values, sibling, column_half):
    lower_half = values[:, :column_half]
    upper_half = values[:, column_half:]
    kept_half = jnp.where(sibling == 0, lower_half, upper_half)
    sent_half = jnp.where(sibling == 0, upper_half, lower_half)
    return (kept_half, sent_half)


def pair_swap(block, axis):
    return lax.ppermute(block, axis, [(0, 1), (1, 0)])


def lower_coupling(factor, diagonal, section, precision):
    tile_rows = diagonal.shape[0]
    below = jnp.where(section > 0, factor[:, :tile_rows], jnp.zeros_like(diagonal))
    return matmul(diagonal, below, precision)


def two_section_leaf(factor, right_side, section, precision, early=()):
    tile_rows = right_side.shape[0]
    diagonal = lax.dynamic_slice_in_dim(factor, section * tile_rows, tile_rows, 1)
    first = matmul(diagonal, right_side, precision)
    arrived = pair_swap(first, "rows")
    arrived, early = lax.optimization_barrier((arrived, early))
    below = jnp.where(section > 0, factor[:, :tile_rows], jnp.zeros_like(diagonal))
    return matmul(diagonal, right_side - matmul(below, arrived, precision), precision), early


def inverse_order(update_blocks):
    targets = update_blocks[0]
    count = targets.shape[0]
    hits = targets[:, None] == jnp.arange(count)[None, :]
    return jnp.sum(jnp.where(hits, jnp.arange(count)[:, None], 0), axis=0)


def two_section_shards(leaf_factor, leaf_rhs, update_panel, update_blocks, parent_factor, parent_rhs):
    section = lax.axis_index("rows")
    precision = lax.Precision.HIGH
    blocks = update_panel.reshape(-1, ROW_BLOCK, update_panel.shape[1])
    order = inverse_order(update_blocks)

    placed_panel = jnp.take(blocks, order, axis=0, mode="clip").reshape(update_panel.shape)
    placed_panel = two_section_leaf(leaf_factor, leaf_rhs, section, precision, placed_panel)
    leaf_solution, placed_panel = placed_panel
    rows_half = placed_panel.shape[0] // 2
    panel_other = lax.dynamic_slice_in_dim(placed_panel, (1 - section) * rows_half, rows_half, 0)
    panel_own = lax.dynamic_slice_in_dim(placed_panel, section * rows_half, rows_half, 0)
    column_half = parent_rhs.shape[1]
    sibling = lax.axis_index("leaf") % 2
    solution_kept = lax.dynamic_slice_in_dim(leaf_solution, sibling * column_half, column_half, 1)
    solution_sent = lax.dynamic_slice_in_dim(leaf_solution, (1 - sibling) * column_half, column_half, 1)
    other_sent = matmul(panel_other, solution_sent, precision)
    arrived_sent = pair_swap(other_sent, "rows")
    other_kept = matmul(panel_other, solution_kept, precision)
    solution_sent, other_kept = lax.optimization_barrier((solution_sent, other_kept))
    arrived_kept = pair_swap(other_kept, "rows")
    own_sent = matmul(panel_own, solution_sent, precision)
    own_sent, arrived_sent = lax.optimization_barrier((own_sent, arrived_sent))
    sent = own_sent + arrived_sent
    sent, solution_kept = lax.optimization_barrier((sent, solution_kept))
    kept = matmul(panel_own, solution_kept, precision) + arrived_kept
    tile_rows = parent_rhs.shape[0]
    diagonal = lax.dynamic_slice_in_dim(parent_factor, section * tile_rows, tile_rows, 1)
    coupling = lower_coupling(parent_factor, diagonal, section, precision)
    arrived = swapped(sent, "leaf", 0)
    arrived, kept = lax.optimization_barrier((arrived, kept))
    pending = parent_rhs - (kept + arrived)
    half_rows = tile_rows // 2
    first_top = matmul(diagonal[:half_rows], pending, precision)
    arrived_top = pair_swap(first_top, "rows")
    first_bottom = matmul(diagonal[half_rows:], pending, precision)
    arrived_bottom = pair_swap(first_bottom, "rows")
    arrived_top, arrived_bottom, coupling = lax.optimization_barrier((arrived_top, arrived_bottom, coupling))
    correction = matmul(coupling[:, :half_rows], arrived_top, precision)
    correction = correction + matmul(coupling[:, half_rows:], arrived_bottom, precision)
    parent_solution = jnp.concatenate([first_top, first_bottom], axis=0) - correction
    return (leaf_solution, parent_solution)


def shards(leaf_factor, leaf_rhs, update_panel, update_blocks, parent_factor, parent_rhs):
    sections = lax.axis_size("rows")
    if sections == 2:
        return two_section_shards(leaf_factor, leaf_rhs, update_panel, update_blocks, parent_factor, parent_rhs)
    section = lax.axis_index("rows")
    leaf_solution = front_forward(leaf_factor, leaf_rhs, section, sections, leaf_pass)
    panel_product = matmul(update_panel, leaf_solution)
    columns = panel_product.shape[1]
    pieces = panel_product.reshape(-1, ROW_BLOCK, columns)
    placed = jnp.zeros_like(pieces).at[update_blocks[0]].set(pieces).reshape(panel_product.shape)
    column_half = parent_rhs.shape[1]
    sibling = lax.axis_index("leaf") % 2
    kept_half, sent_half = split_halves(placed, sibling, column_half)
    arrived = swapped(sent_half, "leaf", 0)
    update_sum = lax.psum_scatter(kept_half + arrived, "rows", scatter_dimension=0, tiled=True)
    pending = parent_rhs - update_sum
    parent_solution = front_forward(parent_factor, pending, section, sections, parent_pass)
    return (leaf_solution, parent_solution)


def solution(mesh):
    placed = (
        P(("leaf", "rows"), None),
        P(("leaf", "rows"), None),
        P("leaf", "rows"),
        P("leaf", None),
        P(("leaf", "rows"), None),
        P(("leaf", "rows"), None),
    )
    return jax.shard_map(
        shards,
        mesh=mesh,
        in_specs=placed,
        out_specs=(P(("leaf", "rows"), None), P(("leaf", "rows"), None)),
        check_vma=False,
    )
```

```python
import jax
import jax.numpy as jnp
from jax import lax
from jax.sharding import PartitionSpec as P

ROW_BLOCK = 128


def passed_along(array, axis, by):
    size = lax.axis_size(axis)
    pairs = [(i, i + by) for i in range(size) if 0 <= i + by < size]
    return lax.ppermute(array, axis, pairs)


def swapped(block, axis, apart):
    count = lax.axis_size(axis)
    route = []
    for low in range(count):
        high = low | 1 << apart
        if high != low and high < count:
            route += [(low, high), (high, low)]
    return lax.ppermute(block, axis, route)


def matmul(left, right, precision=lax.Precision.HIGHEST):
    return jnp.dot(left, right, precision=precision, preferred_element_type=jnp.float32)


def leaf_pass(outgoing):
    return passed_along(outgoing, "rows", 1)


def parent_pass(outgoing):
    return passed_along(outgoing, "rows", 1)


def front_forward(factor, right_side, section, sections, pass_tile):
    tile_rows = right_side.shape[0]

    def advance(tick, state):
        pending, solution, incoming = state
        source = tick - section
        useful = jnp.logical_and(source >= 0, source < section)
        safe_source = jnp.clip(source, 0, sections - 1)

        def apply_tile(values):
            factor_tile = lax.dynamic_slice_in_dim(factor, safe_source * tile_rows, tile_rows, 1)
            return values - matmul(factor_tile, incoming)

        pending = lax.cond(useful, apply_tile, lambda values: values, pending)
        own_turn = tick == 2 * section

        def solve_own(values):
            diagonal_tile = lax.dynamic_slice_in_dim(factor, section * tile_rows, tile_rows, 1)
            return matmul(diagonal_tile, values)

        solution = lax.cond(own_turn, solve_own, lambda values: solution, pending)
        outgoing = jnp.where(
            own_turn, solution, jnp.where(useful, incoming, jnp.zeros_like(incoming))
        )
        incoming = pass_tile(outgoing)
        return (pending, solution, incoming)

    initial = (right_side, jnp.zeros_like(right_side), jnp.zeros_like(right_side))
    return lax.fori_loop(0, 2 * sections - 1, advance, initial)[1]


def split_halves(values, sibling, column_half):
    lower_half = values[:, :column_half]
    upper_half = values[:, column_half:]
    kept_half = jnp.where(sibling == 0, lower_half, upper_half)
    sent_half = jnp.where(sibling == 0, upper_half, lower_half)
    return (kept_half, sent_half)


def pair_swap(block, axis):
    return lax.ppermute(block, axis, [(0, 1), (1, 0)])


def lower_coupling(factor, diagonal, section, precision):
    tile_rows = diagonal.shape[0]
    below = jnp.where(section > 0, factor[:, :tile_rows], jnp.zeros_like(diagonal))
    return matmul(diagonal, below, precision)


def two_section_leaf(factor, right_side, section, precision, early=()):
    tile_rows = right_side.shape[0]
    diagonal = lax.dynamic_slice_in_dim(factor, section * tile_rows, tile_rows, 1)
    first = matmul(diagonal, right_side, precision)
    arrived = pair_swap(first, "rows")
    arrived, early = lax.optimization_barrier((arrived, early))
    arrived = jnp.where(section > 0, arrived, jnp.zeros_like(arrived))
    return matmul(diagonal, right_side - matmul(factor[:, :tile_rows], arrived, precision), precision), early


def inverse_order(update_blocks):
    targets = update_blocks[0]
    count = targets.shape[0]
    hits = targets[:, None] == jnp.arange(count)[None, :]
    return jnp.sum(jnp.where(hits, jnp.arange(count)[:, None], 0), axis=0)


def two_section_shards(leaf_factor, leaf_rhs, update_panel, update_blocks, parent_factor, parent_rhs):
    section = lax.axis_index("rows")
    precision = lax.Precision.HIGH
    blocks = update_panel.reshape(-1, ROW_BLOCK, update_panel.shape[1])
    order = inverse_order(update_blocks)

    placed_panel = jnp.take(blocks, order, axis=0, mode="clip").reshape(update_panel.shape)
    placed_panel = two_section_leaf(leaf_factor, leaf_rhs, section, precision, placed_panel)
    leaf_solution, placed_panel = placed_panel
    rows_half = placed_panel.shape[0] // 2
    panel_other = lax.dynamic_slice_in_dim(placed_panel, (1 - section) * rows_half, rows_half, 0)
    panel_own = lax.dynamic_slice_in_dim(placed_panel, section * rows_half, rows_half, 0)
    column_half = parent_rhs.shape[1]
    sibling = lax.axis_index("leaf") % 2
    solution_kept = lax.dynamic_slice_in_dim(leaf_solution, sibling * column_half, column_half, 1)
    solution_sent = lax.dynamic_slice_in_dim(leaf_solution, (1 - sibling) * column_half, column_half, 1)
    other_sent = matmul(panel_other, solution_sent, precision)
    arrived_sent = pair_swap(other_sent, "rows")
    other_kept = matmul(panel_other, solution_kept, precision)
    solution_sent, other_kept = lax.optimization_barrier((solution_sent, other_kept))
    arrived_kept = pair_swap(other_kept, "rows")
    own_sent = matmul(panel_own, solution_sent, precision)
    own_sent, arrived_sent = lax.optimization_barrier((own_sent, arrived_sent))
    sent = own_sent + arrived_sent
    sent, solution_kept = lax.optimization_barrier((sent, solution_kept))
    kept = matmul(panel_own, solution_kept, precision) + arrived_kept
    tile_rows = parent_rhs.shape[0]
    diagonal = lax.dynamic_slice_in_dim(parent_factor, section * tile_rows, tile_rows, 1)
    coupling = lower_coupling(parent_factor, diagonal, section, precision)
    arrived = swapped(sent, "leaf", 0)
    arrived, kept = lax.optimization_barrier((arrived, kept))
    pending = parent_rhs - (kept + arrived)
    first = matmul(diagonal, pending, precision)
    arrived = pair_swap(first, "rows")
    arrived, coupling = lax.optimization_barrier((arrived, coupling))
    parent_solution = first - matmul(coupling, arrived, precision)
    return (leaf_solution, parent_solution)


def shards(leaf_factor, leaf_rhs, update_panel, update_blocks, parent_factor, parent_rhs):
    sections = lax.axis_size("rows")
    if sections == 2:
        return two_section_shards(leaf_factor, leaf_rhs, update_panel, update_blocks, parent_factor, parent_rhs)
    section = lax.axis_index("rows")
    leaf_solution = front_forward(leaf_factor, leaf_rhs, section, sections, leaf_pass)
    panel_product = matmul(update_panel, leaf_solution)
    columns = panel_product.shape[1]
    pieces = panel_product.reshape(-1, ROW_BLOCK, columns)
    placed = jnp.zeros_like(pieces).at[update_blocks[0]].set(pieces).reshape(panel_product.shape)
    column_half = parent_rhs.shape[1]
    sibling = lax.axis_index("leaf") % 2
    kept_half, sent_half = split_halves(placed, sibling, column_half)
    arrived = swapped(sent_half, "leaf", 0)
    update_sum = lax.psum_scatter(kept_half + arrived, "rows", scatter_dimension=0, tiled=True)
    pending = parent_rhs - update_sum
    parent_solution = front_forward(parent_factor, pending, section, sections, parent_pass)
    return (leaf_solution, parent_solution)


def solution(mesh):
    placed = (
        P(("leaf", "rows"), None),
        P(("leaf", "rows"), None),
        P("leaf", "rows"),
        P("leaf", None),
        P(("leaf", "rows"), None),
        P(("leaf", "rows"), None),
    )
    return jax.shard_map(
        shards,
        mesh=mesh,
        in_specs=placed,
        out_specs=(P(("leaf", "rows"), None), P(("leaf", "rows"), None)),
        check_vma=False,
    )
```

```python
import jax
import jax.numpy as jnp
from jax import lax
from jax.sharding import PartitionSpec as P

ROW_BLOCK = 128


def passed_along(array, axis, by):
    size = lax.axis_size(axis)
    pairs = [(i, i + by) for i in range(size) if 0 <= i + by < size]
    return lax.ppermute(array, axis, pairs)


def swapped(block, axis, apart):
    count = lax.axis_size(axis)
    route = []
    for low in range(count):
        high = low | 1 << apart
        if high != low and high < count:
            route += [(low, high), (high, low)]
    return lax.ppermute(block, axis, route)


def matmul(left, right, precision=lax.Precision.HIGHEST):
    return jnp.dot(left, right, precision=precision, preferred_element_type=jnp.float32)


def leaf_pass(outgoing):
    return passed_along(outgoing, "rows", 1)


def parent_pass(outgoing):
    return passed_along(outgoing, "rows", 1)


def front_forward(factor, right_side, section, sections, pass_tile):
    tile_rows = right_side.shape[0]

    def advance(tick, state):
        pending, solution, incoming = state
        source = tick - section
        useful = jnp.logical_and(source >= 0, source < section)
        safe_source = jnp.clip(source, 0, sections - 1)

        def apply_tile(values):
            factor_tile = lax.dynamic_slice_in_dim(factor, safe_source * tile_rows, tile_rows, 1)
            return values - matmul(factor_tile, incoming)

        pending = lax.cond(useful, apply_tile, lambda values: values, pending)
        own_turn = tick == 2 * section

        def solve_own(values):
            diagonal_tile = lax.dynamic_slice_in_dim(factor, section * tile_rows, tile_rows, 1)
            return matmul(diagonal_tile, values)

        solution = lax.cond(own_turn, solve_own, lambda values: solution, pending)
        outgoing = jnp.where(
            own_turn, solution, jnp.where(useful, incoming, jnp.zeros_like(incoming))
        )
        incoming = pass_tile(outgoing)
        return (pending, solution, incoming)

    initial = (right_side, jnp.zeros_like(right_side), jnp.zeros_like(right_side))
    return lax.fori_loop(0, 2 * sections - 1, advance, initial)[1]


def split_halves(values, sibling, column_half):
    lower_half = values[:, :column_half]
    upper_half = values[:, column_half:]
    kept_half = jnp.where(sibling == 0, lower_half, upper_half)
    sent_half = jnp.where(sibling == 0, upper_half, lower_half)
    return (kept_half, sent_half)


def pair_swap(block, axis):
    return lax.ppermute(block, axis, [(0, 1), (1, 0)])


def lower_coupling(factor, diagonal, section, precision):
    tile_rows = diagonal.shape[0]
    below = jnp.where(section > 0, factor[:, :tile_rows], jnp.zeros_like(diagonal))
    return matmul(diagonal, below, precision)


def two_section_leaf(factor, right_side, section, precision, early=()):
    tile_rows = right_side.shape[0]
    diagonal = lax.dynamic_slice_in_dim(factor, section * tile_rows, tile_rows, 1)
    first = matmul(diagonal, right_side, precision)
    arrived = pair_swap(first, "rows")
    arrived, early = lax.optimization_barrier((arrived, early))
    below = jnp.where(section > 0, factor[:, :tile_rows], jnp.zeros_like(diagonal))
    return matmul(diagonal, right_side - matmul(below, arrived, precision), precision), early


def inverse_order(update_blocks):
    targets = update_blocks[0]
    count = targets.shape[0]
    hits = targets[:, None] == jnp.arange(count)[None, :]
    return jnp.sum(jnp.where(hits, jnp.arange(count)[:, None], 0), axis=0)


def two_section_shards(leaf_factor, leaf_rhs, update_panel, update_blocks, parent_factor, parent_rhs):
    section = lax.axis_index("rows")
    precision = lax.Precision.HIGH
    blocks = update_panel.reshape(-1, ROW_BLOCK, update_panel.shape[1])
    order = inverse_order(update_blocks)

    placed_panel = jnp.take(blocks, order, axis=0, mode="clip").reshape(update_panel.shape)
    placed_panel = two_section_leaf(leaf_factor, leaf_rhs, section, precision, placed_panel)
    leaf_solution, placed_panel = placed_panel
    rows_half = placed_panel.shape[0] // 2
    panel_other = lax.dynamic_slice_in_dim(placed_panel, (1 - section) * rows_half, rows_half, 0)
    panel_own = lax.dynamic_slice_in_dim(placed_panel, section * rows_half, rows_half, 0)
    column_half = parent_rhs.shape[1]
    sibling = lax.axis_index("leaf") % 2
    solution_kept = lax.dynamic_slice_in_dim(leaf_solution, sibling * column_half, column_half, 1)
    solution_sent = lax.dynamic_slice_in_dim(leaf_solution, (1 - sibling) * column_half, column_half, 1)
    other_kept = matmul(panel_other, solution_kept, precision)
    arrived_kept = pair_swap(other_kept, "rows")
    solution_sent, other_kept = lax.optimization_barrier((solution_sent, other_kept))
    other_sent = matmul(panel_other, solution_sent, precision)
    arrived_sent = pair_swap(other_sent, "rows")
    own_sent = matmul(panel_own, solution_sent, precision)
    own_sent, arrived_sent = lax.optimization_barrier((own_sent, arrived_sent))
    sent = own_sent + arrived_sent
    sent, solution_kept = lax.optimization_barrier((sent, solution_kept))
    kept = matmul(panel_own, solution_kept, precision) + arrived_kept
    tile_rows = parent_rhs.shape[0]
    diagonal = lax.dynamic_slice_in_dim(parent_factor, section * tile_rows, tile_rows, 1)
    coupling = lower_coupling(parent_factor, diagonal, section, precision)
    arrived = swapped(sent, "leaf", 0)
    arrived, kept = lax.optimization_barrier((arrived, kept))
    pending = parent_rhs - (kept + arrived)
    first = matmul(diagonal, pending, precision)
    arrived = pair_swap(first, "rows")
    arrived, coupling = lax.optimization_barrier((arrived, coupling))
    parent_solution = first - matmul(coupling, arrived, precision)
    return (leaf_solution, parent_solution)


def shards(leaf_factor, leaf_rhs, update_panel, update_blocks, parent_factor, parent_rhs):
    sections = lax.axis_size("rows")
    if sections == 2:
        return two_section_shards(leaf_factor, leaf_rhs, update_panel, update_blocks, parent_factor, parent_rhs)
    section = lax.axis_index("rows")
    leaf_solution = front_forward(leaf_factor, leaf_rhs, section, sections, leaf_pass)
    panel_product = matmul(update_panel, leaf_solution)
    columns = panel_product.shape[1]
    pieces = panel_product.reshape(-1, ROW_BLOCK, columns)
    placed = jnp.zeros_like(pieces).at[update_blocks[0]].set(pieces).reshape(panel_product.shape)
    column_half = parent_rhs.shape[1]
    sibling = lax.axis_index("leaf") % 2
    kept_half, sent_half = split_halves(placed, sibling, column_half)
    arrived = swapped(sent_half, "leaf", 0)
    update_sum = lax.psum_scatter(kept_half + arrived, "rows", scatter_dimension=0, tiled=True)
    pending = parent_rhs - update_sum
    parent_solution = front_forward(parent_factor, pending, section, sections, parent_pass)
    return (leaf_solution, parent_solution)


def solution(mesh):
    placed = (
        P(("leaf", "rows"), None),
        P(("leaf", "rows"), None),
        P("leaf", "rows"),
        P("leaf", None),
        P(("leaf", "rows"), None),
        P(("leaf", "rows"), None),
    )
    return jax.shard_map(
        shards,
        mesh=mesh,
        in_specs=placed,
        out_specs=(P(("leaf", "rows"), None), P(("leaf", "rows"), None)),
        check_vma=False,
    )
```

```python
import jax
import jax.numpy as jnp
from jax import lax
from jax.sharding import PartitionSpec as P

ROW_BLOCK = 128


def passed_along(array, axis, by):
    size = lax.axis_size(axis)
    pairs = [(i, i + by) for i in range(size) if 0 <= i + by < size]
    return lax.ppermute(array, axis, pairs)


def swapped(block, axis, apart):
    count = lax.axis_size(axis)
    route = []
    for low in range(count):
        high = low | 1 << apart
        if high != low and high < count:
            route += [(low, high), (high, low)]
    return lax.ppermute(block, axis, route)


def matmul(left, right, precision=lax.Precision.HIGHEST):
    return jnp.dot(left, right, precision=precision, preferred_element_type=jnp.float32)


def leaf_pass(outgoing):
    return passed_along(outgoing, "rows", 1)


def parent_pass(outgoing):
    return passed_along(outgoing, "rows", 1)


def front_forward(factor, right_side, section, sections, pass_tile):
    tile_rows = right_side.shape[0]

    def advance(tick, state):
        pending, solution, incoming = state
        source = tick - section
        useful = jnp.logical_and(source >= 0, source < section)
        safe_source = jnp.clip(source, 0, sections - 1)

        def apply_tile(values):
            factor_tile = lax.dynamic_slice_in_dim(factor, safe_source * tile_rows, tile_rows, 1)
            return values - matmul(factor_tile, incoming)

        pending = lax.cond(useful, apply_tile, lambda values: values, pending)
        own_turn = tick == 2 * section

        def solve_own(values):
            diagonal_tile = lax.dynamic_slice_in_dim(factor, section * tile_rows, tile_rows, 1)
            return matmul(diagonal_tile, values)

        solution = lax.cond(own_turn, solve_own, lambda values: solution, pending)
        outgoing = jnp.where(
            own_turn, solution, jnp.where(useful, incoming, jnp.zeros_like(incoming))
        )
        incoming = pass_tile(outgoing)
        return (pending, solution, incoming)

    initial = (right_side, jnp.zeros_like(right_side), jnp.zeros_like(right_side))
    return lax.fori_loop(0, 2 * sections - 1, advance, initial)[1]


def split_halves(values, sibling, column_half):
    lower_half = values[:, :column_half]
    upper_half = values[:, column_half:]
    kept_half = jnp.where(sibling == 0, lower_half, upper_half)
    sent_half = jnp.where(sibling == 0, upper_half, lower_half)
    return (kept_half, sent_half)


def pair_swap(block, axis):
    return lax.ppermute(block, axis, [(0, 1), (1, 0)])


def lower_coupling(factor, diagonal, section, precision):
    tile_rows = diagonal.shape[0]
    below = jnp.where(section > 0, factor[:, :tile_rows], jnp.zeros_like(diagonal))
    return matmul(diagonal, below, precision)


def two_section_leaf(factor, right_side, section, precision, early=()):
    tile_rows = right_side.shape[0]
    diagonal = lax.dynamic_slice_in_dim(factor, section * tile_rows, tile_rows, 1)
    first = matmul(diagonal, right_side, precision)
    arrived = pair_swap(first, "rows")
    arrived, early = lax.optimization_barrier((arrived, early))
    below = jnp.where(section > 0, factor[:, :tile_rows], jnp.zeros_like(diagonal))
    return matmul(diagonal, right_side - matmul(below, arrived, precision), precision), early


def inverse_order(update_blocks):
    targets = update_blocks[0]
    count = targets.shape[0]
    hits = targets[:, None] == jnp.arange(count)[None, :]
    return jnp.sum(jnp.where(hits, jnp.arange(count)[:, None], 0), axis=0)


def two_section_shards(leaf_factor, leaf_rhs, update_panel, update_blocks, parent_factor, parent_rhs):
    section = lax.axis_index("rows")
    precision = lax.Precision.HIGH
    blocks = update_panel.reshape(-1, ROW_BLOCK, update_panel.shape[1])
    order = inverse_order(update_blocks)

    placed_panel = blocks.at[order].get(mode="promise_in_bounds").reshape(update_panel.shape)
    placed_panel = two_section_leaf(leaf_factor, leaf_rhs, section, precision, placed_panel)
    leaf_solution, placed_panel = placed_panel
    rows_half = placed_panel.shape[0] // 2
    panel_other = lax.dynamic_slice_in_dim(placed_panel, (1 - section) * rows_half, rows_half, 0)
    panel_own = lax.dynamic_slice_in_dim(placed_panel, section * rows_half, rows_half, 0)
    column_half = parent_rhs.shape[1]
    sibling = lax.axis_index("leaf") % 2
    solution_kept = lax.dynamic_slice_in_dim(leaf_solution, sibling * column_half, column_half, 1)
    solution_sent = lax.dynamic_slice_in_dim(leaf_solution, (1 - sibling) * column_half, column_half, 1)
    other_sent = matmul(panel_other, solution_sent, precision)
    arrived_sent = pair_swap(other_sent, "rows")
    other_kept = matmul(panel_other, solution_kept, precision)
    solution_sent, other_kept = lax.optimization_barrier((solution_sent, other_kept))
    arrived_kept = pair_swap(other_kept, "rows")
    own_sent = matmul(panel_own, solution_sent, precision)
    own_sent, arrived_sent = lax.optimization_barrier((own_sent, arrived_sent))
    sent = own_sent + arrived_sent
    sent, solution_kept = lax.optimization_barrier((sent, solution_kept))
    kept = matmul(panel_own, solution_kept, precision) + arrived_kept
    tile_rows = parent_rhs.shape[0]
    diagonal = lax.dynamic_slice_in_dim(parent_factor, section * tile_rows, tile_rows, 1)
    coupling = lower_coupling(parent_factor, diagonal, section, precision)
    arrived = swapped(sent, "leaf", 0)
    arrived, kept = lax.optimization_barrier((arrived, kept))
    pending = parent_rhs - (kept + arrived)
    first = matmul(diagonal, pending, precision)
    arrived = pair_swap(first, "rows")
    arrived, coupling = lax.optimization_barrier((arrived, coupling))
    parent_solution = first - matmul(coupling, arrived, precision)
    return (leaf_solution, parent_solution)


def shards(leaf_factor, leaf_rhs, update_panel, update_blocks, parent_factor, parent_rhs):
    sections = lax.axis_size("rows")
    if sections == 2:
        return two_section_shards(leaf_factor, leaf_rhs, update_panel, update_blocks, parent_factor, parent_rhs)
    section = lax.axis_index("rows")
    leaf_solution = front_forward(leaf_factor, leaf_rhs, section, sections, leaf_pass)
    panel_product = matmul(update_panel, leaf_solution)
    columns = panel_product.shape[1]
    pieces = panel_product.reshape(-1, ROW_BLOCK, columns)
    placed = jnp.zeros_like(pieces).at[update_blocks[0]].set(pieces).reshape(panel_product.shape)
    column_half = parent_rhs.shape[1]
    sibling = lax.axis_index("leaf") % 2
    kept_half, sent_half = split_halves(placed, sibling, column_half)
    arrived = swapped(sent_half, "leaf", 0)
    update_sum = lax.psum_scatter(kept_half + arrived, "rows", scatter_dimension=0, tiled=True)
    pending = parent_rhs - update_sum
    parent_solution = front_forward(parent_factor, pending, section, sections, parent_pass)
    return (leaf_solution, parent_solution)


def solution(mesh):
    placed = (
        P(("leaf", "rows"), None),
        P(("leaf", "rows"), None),
        P("leaf", "rows"),
        P("leaf", None),
        P(("leaf", "rows"), None),
        P(("leaf", "rows"), None),
    )
    return jax.shard_map(
        shards,
        mesh=mesh,
        in_specs=placed,
        out_specs=(P(("leaf", "rows"), None), P(("leaf", "rows"), None)),
        check_vma=False,
    )
```

```python
import jax
import jax.numpy as jnp
from jax import lax
from jax.sharding import PartitionSpec as P

ROW_BLOCK = 128


def passed_along(array, axis, by):
    size = lax.axis_size(axis)
    pairs = [(i, i + by) for i in range(size) if 0 <= i + by < size]
    return lax.ppermute(array, axis, pairs)


def swapped(block, axis, apart):
    count = lax.axis_size(axis)
    route = []
    for low in range(count):
        high = low | 1 << apart
        if high != low and high < count:
            route += [(low, high), (high, low)]
    return lax.ppermute(block, axis, route)


def matmul(left, right, precision=lax.Precision.HIGHEST):
    return jnp.dot(left, right, precision=precision, preferred_element_type=jnp.float32)


def leaf_pass(outgoing):
    return passed_along(outgoing, "rows", 1)


def parent_pass(outgoing):
    return passed_along(outgoing, "rows", 1)


def front_forward(factor, right_side, section, sections, pass_tile):
    tile_rows = right_side.shape[0]

    def advance(tick, state):
        pending, solution, incoming = state
        source = tick - section
        useful = jnp.logical_and(source >= 0, source < section)
        safe_source = jnp.clip(source, 0, sections - 1)

        def apply_tile(values):
            factor_tile = lax.dynamic_slice_in_dim(factor, safe_source * tile_rows, tile_rows, 1)
            return values - matmul(factor_tile, incoming)

        pending = lax.cond(useful, apply_tile, lambda values: values, pending)
        own_turn = tick == 2 * section

        def solve_own(values):
            diagonal_tile = lax.dynamic_slice_in_dim(factor, section * tile_rows, tile_rows, 1)
            return matmul(diagonal_tile, values)

        solution = lax.cond(own_turn, solve_own, lambda values: solution, pending)
        outgoing = jnp.where(
            own_turn, solution, jnp.where(useful, incoming, jnp.zeros_like(incoming))
        )
        incoming = pass_tile(outgoing)
        return (pending, solution, incoming)

    initial = (right_side, jnp.zeros_like(right_side), jnp.zeros_like(right_side))
    return lax.fori_loop(0, 2 * sections - 1, advance, initial)[1]


def split_halves(values, sibling, column_half):
    lower_half = values[:, :column_half]
    upper_half = values[:, column_half:]
    kept_half = jnp.where(sibling == 0, lower_half, upper_half)
    sent_half = jnp.where(sibling == 0, upper_half, lower_half)
    return (kept_half, sent_half)


def pair_swap(block, axis):
    return lax.ppermute(block, axis, [(0, 1), (1, 0)])


def lower_coupling(factor, diagonal, section, precision):
    tile_rows = diagonal.shape[0]
    below = jnp.where(section > 0, factor[:, :tile_rows], jnp.zeros_like(diagonal))
    return matmul(diagonal, below, precision)


def two_section_leaf(factor, right_side, section, precision, early=()):
    tile_rows = right_side.shape[0]
    diagonal = lax.dynamic_slice_in_dim(factor, section * tile_rows, tile_rows, 1)
    first = matmul(diagonal, right_side, precision)
    arrived = pair_swap(first, "rows")
    arrived, early = lax.optimization_barrier((arrived, early))
    arrived = jnp.where(section > 0, arrived, jnp.zeros_like(arrived))
    return matmul(diagonal, right_side - matmul(factor[:, :tile_rows], arrived, precision), precision), early


def inverse_order(update_blocks):
    targets = update_blocks[0]
    count = targets.shape[0]
    hits = targets[:, None] == jnp.arange(count)[None, :]
    return jnp.sum(jnp.where(hits, jnp.arange(count)[:, None], 0), axis=0)


def two_section_shards(leaf_factor, leaf_rhs, update_panel, update_blocks, parent_factor, parent_rhs):
    section = lax.axis_index("rows")
    precision = lax.Precision.HIGH
    blocks = update_panel.reshape(-1, ROW_BLOCK, update_panel.shape[1])
    order = inverse_order(update_blocks)

    placed_panel = blocks.at[order].get(mode="promise_in_bounds").reshape(update_panel.shape)
    placed_panel = two_section_leaf(leaf_factor, leaf_rhs, section, precision, placed_panel)
    leaf_solution, placed_panel = placed_panel
    rows_half = placed_panel.shape[0] // 2
    panel_other = lax.dynamic_slice_in_dim(placed_panel, (1 - section) * rows_half, rows_half, 0)
    panel_own = lax.dynamic_slice_in_dim(placed_panel, section * rows_half, rows_half, 0)
    column_half = parent_rhs.shape[1]
    sibling = lax.axis_index("leaf") % 2
    solution_kept = lax.dynamic_slice_in_dim(leaf_solution, sibling * column_half, column_half, 1)
    solution_sent = lax.dynamic_slice_in_dim(leaf_solution, (1 - sibling) * column_half, column_half, 1)
    other_sent = matmul(panel_other, solution_sent, precision)
    arrived_sent = pair_swap(other_sent, "rows")
    other_kept = matmul(panel_other, solution_kept, precision)
    solution_sent, other_kept = lax.optimization_barrier((solution_sent, other_kept))
    arrived_kept = pair_swap(other_kept, "rows")
    own_sent = matmul(panel_own, solution_sent, precision)
    own_sent, arrived_sent = lax.optimization_barrier((own_sent, arrived_sent))
    sent = own_sent + arrived_sent
    sent, solution_kept = lax.optimization_barrier((sent, solution_kept))
    kept = matmul(panel_own, solution_kept, precision) + arrived_kept
    tile_rows = parent_rhs.shape[0]
    diagonal = lax.dynamic_slice_in_dim(parent_factor, section * tile_rows, tile_rows, 1)
    coupling = lower_coupling(parent_factor, diagonal, section, precision)
    arrived = swapped(sent, "leaf", 0)
    arrived, kept = lax.optimization_barrier((arrived, kept))
    pending = parent_rhs - (kept + arrived)
    first = matmul(diagonal, pending, precision)
    arrived = pair_swap(first, "rows")
    arrived, coupling = lax.optimization_barrier((arrived, coupling))
    parent_solution = first - matmul(coupling, arrived, precision)
    return (leaf_solution, parent_solution)


def shards(leaf_factor, leaf_rhs, update_panel, update_blocks, parent_factor, parent_rhs):
    sections = lax.axis_size("rows")
    if sections == 2:
        return two_section_shards(leaf_factor, leaf_rhs, update_panel, update_blocks, parent_factor, parent_rhs)
    section = lax.axis_index("rows")
    leaf_solution = front_forward(leaf_factor, leaf_rhs, section, sections, leaf_pass)
    panel_product = matmul(update_panel, leaf_solution)
    columns = panel_product.shape[1]
    pieces = panel_product.reshape(-1, ROW_BLOCK, columns)
    placed = jnp.zeros_like(pieces).at[update_blocks[0]].set(pieces).reshape(panel_product.shape)
    column_half = parent_rhs.shape[1]
    sibling = lax.axis_index("leaf") % 2
    kept_half, sent_half = split_halves(placed, sibling, column_half)
    arrived = swapped(sent_half, "leaf", 0)
    update_sum = lax.psum_scatter(kept_half + arrived, "rows", scatter_dimension=0, tiled=True)
    pending = parent_rhs - update_sum
    parent_solution = front_forward(parent_factor, pending, section, sections, parent_pass)
    return (leaf_solution, parent_solution)


def solution(mesh):
    placed = (
        P(("leaf", "rows"), None),
        P(("leaf", "rows"), None),
        P("leaf", "rows"),
        P("leaf", None),
        P(("leaf", "rows"), None),
        P(("leaf", "rows"), None),
    )
    return jax.shard_map(
        shards,
        mesh=mesh,
        in_specs=placed,
        out_specs=(P(("leaf", "rows"), None), P(("leaf", "rows"), None)),
        check_vma=False,
    )
```

```python
import jax
import jax.numpy as jnp
from jax import lax
from jax.sharding import PartitionSpec as P

ROW_BLOCK = 128


def passed_along(array, axis, by):
    size = lax.axis_size(axis)
    pairs = [(i, i + by) for i in range(size) if 0 <= i + by < size]
    return lax.ppermute(array, axis, pairs)


def swapped(block, axis, apart):
    count = lax.axis_size(axis)
    route = []
    for low in range(count):
        high = low | 1 << apart
        if high != low and high < count:
            route += [(low, high), (high, low)]
    return lax.ppermute(block, axis, route)


def matmul(left, right, precision=lax.Precision.HIGHEST):
    return jnp.dot(left, right, precision=precision, preferred_element_type=jnp.float32)


def leaf_pass(outgoing):
    return passed_along(outgoing, "rows", 1)


def parent_pass(outgoing):
    return passed_along(outgoing, "rows", 1)


def front_forward(factor, right_side, section, sections, pass_tile):
    tile_rows = right_side.shape[0]

    def advance(tick, state):
        pending, solution, incoming = state
        source = tick - section
        useful = jnp.logical_and(source >= 0, source < section)
        safe_source = jnp.clip(source, 0, sections - 1)

        def apply_tile(values):
            factor_tile = lax.dynamic_slice_in_dim(factor, safe_source * tile_rows, tile_rows, 1)
            return values - matmul(factor_tile, incoming)

        pending = lax.cond(useful, apply_tile, lambda values: values, pending)
        own_turn = tick == 2 * section

        def solve_own(values):
            diagonal_tile = lax.dynamic_slice_in_dim(factor, section * tile_rows, tile_rows, 1)
            return matmul(diagonal_tile, values)

        solution = lax.cond(own_turn, solve_own, lambda values: solution, pending)
        outgoing = jnp.where(
            own_turn, solution, jnp.where(useful, incoming, jnp.zeros_like(incoming))
        )
        incoming = pass_tile(outgoing)
        return (pending, solution, incoming)

    initial = (right_side, jnp.zeros_like(right_side), jnp.zeros_like(right_side))
    return lax.fori_loop(0, 2 * sections - 1, advance, initial)[1]


def split_halves(values, sibling, column_half):
    lower_half = values[:, :column_half]
    upper_half = values[:, column_half:]
    kept_half = jnp.where(sibling == 0, lower_half, upper_half)
    sent_half = jnp.where(sibling == 0, upper_half, lower_half)
    return (kept_half, sent_half)


def pair_swap(block, axis):
    return lax.ppermute(block, axis, [(0, 1), (1, 0)])


def lower_coupling(factor, diagonal, section, precision):
    tile_rows = diagonal.shape[0]
    below = jnp.where(section > 0, factor[:, :tile_rows], jnp.zeros_like(diagonal))
    return matmul(diagonal, below, precision)


def two_section_leaf(factor, right_side, section, precision, early=()):
    tile_rows = right_side.shape[0]
    diagonal = lax.dynamic_slice_in_dim(factor, section * tile_rows, tile_rows, 1)
    first = matmul(diagonal, right_side, precision)
    arrived = pair_swap(first, "rows")
    arrived, early = lax.optimization_barrier((arrived, early))
    below = jnp.where(section > 0, factor[:, :tile_rows], jnp.zeros_like(diagonal))
    return matmul(diagonal, right_side - matmul(below, arrived, precision), precision), early


def inverse_order(update_blocks):
    targets = update_blocks[0]
    count = targets.shape[0]
    hits = targets[:, None] == jnp.arange(count)[None, :]
    return jnp.sum(jnp.where(hits, jnp.arange(count)[:, None], 0), axis=0)


def two_section_shards(leaf_factor, leaf_rhs, update_panel, update_blocks, parent_factor, parent_rhs):
    section = lax.axis_index("rows")
    precision = lax.Precision.HIGH
    blocks = update_panel.reshape(-1, ROW_BLOCK, update_panel.shape[1])
    order = inverse_order(update_blocks)

    placed_panel = jnp.take(blocks, order, axis=0, mode="clip").reshape(update_panel.shape)
    placed_panel = two_section_leaf(leaf_factor, leaf_rhs, section, precision, placed_panel)
    leaf_solution, placed_panel = placed_panel
    rows_half = placed_panel.shape[0] // 2
    panel_other = lax.dynamic_slice_in_dim(placed_panel, (1 - section) * rows_half, rows_half, 0)
    panel_own = lax.dynamic_slice_in_dim(placed_panel, section * rows_half, rows_half, 0)
    column_half = parent_rhs.shape[1]
    sibling = lax.axis_index("leaf") % 2
    solution_kept = lax.dynamic_slice_in_dim(leaf_solution, sibling * column_half, column_half, 1)
    solution_sent = lax.dynamic_slice_in_dim(leaf_solution, (1 - sibling) * column_half, column_half, 1)
    other_sent = matmul(panel_other, solution_sent, precision)
    arrived_sent = pair_swap(other_sent, "rows")
    other_kept = matmul(panel_other, solution_kept, precision)
    solution_sent, other_kept = lax.optimization_barrier((solution_sent, other_kept))
    arrived_kept = pair_swap(other_kept, "rows")
    own_sent = matmul(panel_own, solution_sent, precision)
    own_sent, arrived_sent = lax.optimization_barrier((own_sent, arrived_sent))
    sent = own_sent + arrived_sent
    sent, solution_kept = lax.optimization_barrier((sent, solution_kept))
    kept = matmul(panel_own, solution_kept, precision) + arrived_kept
    tile_rows = parent_rhs.shape[0]
    diagonal = lax.dynamic_slice_in_dim(parent_factor, section * tile_rows, tile_rows, 1)
    coupling = matmul(diagonal, parent_factor[:, :tile_rows], precision)
    arrived = swapped(sent, "leaf", 0)
    arrived, kept = lax.optimization_barrier((arrived, kept))
    pending = parent_rhs - (kept + arrived)
    first = matmul(diagonal, pending, precision)
    arrived = pair_swap(first, "rows")
    arrived, coupling = lax.optimization_barrier((arrived, coupling))
    arrived = jnp.where(section > 0, arrived, jnp.zeros_like(arrived))
    parent_solution = first - matmul(coupling, arrived, precision)
    return (leaf_solution, parent_solution)


def shards(leaf_factor, leaf_rhs, update_panel, update_blocks, parent_factor, parent_rhs):
    sections = lax.axis_size("rows")
    if sections == 2:
        return two_section_shards(leaf_factor, leaf_rhs, update_panel, update_blocks, parent_factor, parent_rhs)
    section = lax.axis_index("rows")
    leaf_solution = front_forward(leaf_factor, leaf_rhs, section, sections, leaf_pass)
    panel_product = matmul(update_panel, leaf_solution)
    columns = panel_product.shape[1]
    pieces = panel_product.reshape(-1, ROW_BLOCK, columns)
    placed = jnp.zeros_like(pieces).at[update_blocks[0]].set(pieces).reshape(panel_product.shape)
    column_half = parent_rhs.shape[1]
    sibling = lax.axis_index("leaf") % 2
    kept_half, sent_half = split_halves(placed, sibling, column_half)
    arrived = swapped(sent_half, "leaf", 0)
    update_sum = lax.psum_scatter(kept_half + arrived, "rows", scatter_dimension=0, tiled=True)
    pending = parent_rhs - update_sum
    parent_solution = front_forward(parent_factor, pending, section, sections, parent_pass)
    return (leaf_solution, parent_solution)


def solution(mesh):
    placed = (
        P(("leaf", "rows"), None),
        P(("leaf", "rows"), None),
        P("leaf", "rows"),
        P("leaf", None),
        P(("leaf", "rows"), None),
        P(("leaf", "rows"), None),
    )
    return jax.shard_map(
        shards,
        mesh=mesh,
        in_specs=placed,
        out_specs=(P(("leaf", "rows"), None), P(("leaf", "rows"), None)),
        check_vma=False,
    )
```
